32 devices in a mesh: member: 2 (over y), lon: 4 (over z), lev: 4 (over x, core).
Axes of the slice: x: 2, y: 2, z: 4, core: 2. Of those that a mesh axis runs over, the one named last changes fastest.
Arguments:
- latent: bfloat16 [512, 8, 512], P('lev', 'member', 'lon'), parts along dimension 1, may hold values from -9 to 9
- att_gain: float32 [512], replicated, may hold values from 0.1 to 1.9
- qkv_weight: bfloat16 [3, 512, 512], P(None, 'lev'), may hold values from -0.25 to 0.25
- out_weight: bfloat16 [512, 512], P('lev'), may hold values from -0.25 to 0.25
- stencil_weight: float32 [2, 9, 512], P(None, None, 'lev'), may hold values from -2.5 to 2.5
- block_gain: float32 [2, 512], replicated, may hold values from 0.1 to 1.9
- up_weight: bfloat16 [2, 2048, 512], P(None, 'lev'), may hold values from -0.25 to 0.25
- down_weight: bfloat16 [2, 2048, 512], P(None, 'lev'), may hold values from -0.125 to 0.125
Outputs:
- decoded: bfloat16 [512, 8, 512], P('lev', 'member', 'lon'), parts along dimension 1
The draws below stay inside these ranges and needn't reach their ends.
There are 2 independent parts, one for each index of `member`. The reference program is written for one: setup_inputs(seed, part) draws one part's arguments, and reference() takes and returns one part's arrays. A program takes and returns all parts, laid end to end along the dimension named above; an argument that names none is the same for every part. Nothing has to cross between parts.
All inputs are finite; a program needn't handle non-finite values.
Results may differ from the reference program's by a relative error of at most 0.017.
Values may be sent and summed in bfloat16 or wider, within the bound.
No kernel may reach another device: no remote copies, remote signals or barrier semaphores. Data moves between devices by JAX's collectives and lax.ppermute only.
A program may use at most 64 MiB of HBM per device.

```python
import math
import jax
import jax.numpy as jnp
from jax import lax

C = 512
H = 8
F = 2048
BLOCKS = 2
LAT = 4
LON = 512
N_LEV = 4


def draw_latent(key, part):
    base_key = jax.random.fold_in(key, 0)
    values = jnp.clip(jax.random.normal(base_key, (C, LAT, LON), jnp.float32), -4.0, 4.0)
    return values.astype(jnp.bfloat16)


def block_levels(rng, shape, cuts, smallest, top_value):
    loudness, own = 1.0, jax.random.fold_in(rng, 6)
    for position, shards_of in cuts:
        steps = jnp.exp(jax.random.uniform(jax.random.fold_in(own, position), (shards_of,), jnp.float32, smallest / len(cuts), top_value / len(cuts)))
        loudness = loudness * jnp.repeat(steps, shape[position] // shards_of).reshape([-1 if axis == position else 1 for axis in range(len(shape))])
    return loudness


def scatter_about(own_key, shape, width, bound, shards=(), kind=jnp.bfloat16):
    values = width * jax.random.normal(own_key, shape, jnp.float32)
    if shards:
        values = values * block_levels(own_key, shape, shards, -0.22, 0.18)
    return jnp.clip(values, -bound, bound).astype(kind)


def setup_inputs(seed: int = 0, part: int = 0) -> dict:
    splits = jax.random.split(jax.random.key(seed), 9)
    part_splits = jax.random.split(jax.random.fold_in(splits[8], part), 9)
    latent = draw_latent(jax.random.fold_in(jax.random.fold_in(splits[8], part), 71), part)
    att_gain = jnp.clip(1.0 + 0.18 * jax.random.normal(splits[1], (C,), jnp.float32), 0.1, 1.9)
    qkv_weight = scatter_about(splits[2], (3, C, C), C ** -0.5, 0.25, ((1, 4),))
    out_weight = scatter_about(splits[3], (C, C), C ** -0.5, 0.25, ((0, 4),))
    stencil_weight = scatter_about(splits[4], (BLOCKS, 9, C), 0.35, 2.5, ((2, 4),), jnp.float32)
    block_gain = jnp.clip(1.0 + 0.18 * jax.random.normal(splits[5], (BLOCKS, C), jnp.float32), 0.1, 1.9)
    up_weight = scatter_about(splits[6], (BLOCKS, F, C), C ** -0.5, 0.25, ((1, 4),))
    down_weight = scatter_about(splits[7], (BLOCKS, F, C), F ** -0.5, 0.125, ((1, 4),))
    return {"latent": latent, "att_gain": att_gain, "qkv_weight": qkv_weight, "out_weight": out_weight, "stencil_weight": stencil_weight, "block_gain": block_gain, "up_weight": up_weight, "down_weight": down_weight}


attention_scale = 24.0
band_start = 30.0
grid_step = 0.25
epsilon = 1e-06

def rounded(values):
    return lax.optimization_barrier(values.astype(jnp.bfloat16))

def secant_rows(count):
    rows = jnp.arange(count).astype(jnp.float32)
    return 1.0 / jnp.cos((band_start + grid_step * rows) * (math.pi / 180.0))

def norm_channels(values, gain):
    scale = lax.rsqrt(lax.optimization_barrier(jnp.mean(values * values, axis=0, keepdims=True)) + epsilon)
    return values * scale * gain[:, None, None]

def unit_heads(values):
    return values * lax.rsqrt(lax.optimization_barrier(jnp.sum(values * values, axis=1, keepdims=True)) + epsilon)

def group_sum(weight, activation):
    grouped_w = weight.reshape(N_LEV, -1, weight.shape[1])
    grouped_a = activation.reshape(N_LEV, -1, activation.shape[1])

    def add_group(running, operands):
        partial_sum = jnp.dot(operands[0].T, operands[1], preferred_element_type=jnp.float32)
        return (running + rounded(partial_sum).astype(jnp.float32), None)
    start_sum = jnp.zeros((weight.shape[1], activation.shape[1]), jnp.float32)
    running, _ = lax.scan(add_group, start_sum, (grouped_w, grouped_a))
    return running

def stencil(values, tap_weights):
    lat_rows = values.shape[1]
    secants = secant_rows(lat_rows)[None, :, None]
    padded = jnp.pad(values, ((0, 0), (1, 1), (0, 0)))
    stencil_sum = jnp.zeros(values.shape, jnp.float32)
    for row_step in (-1, 0, 1):
        row_shift = padded[:, 1 + row_step:1 + row_step + lat_rows, :]
        for col_step in (-1, 0, 1):
            shifted = jnp.roll(row_shift, -col_step, axis=2)
            tap_row = tap_weights[3 * (row_step + 1) + col_step + 1][:, None, None]
            if col_step != 0:
                stencil_sum = stencil_sum + tap_row * secants * shifted
            else:
                stencil_sum = stencil_sum + tap_row * shifted
    return stencil_sum

def attend_head(operands):
    queries, key_rows, value_rows = operands
    scores = jnp.einsum('dri,drj->rij', queries.astype(jnp.float32), key_rows.astype(jnp.float32)) * attention_scale
    weights = jnp.exp(scores)
    denominator = lax.optimization_barrier(jnp.sum(weights, axis=2))
    numerator = jnp.einsum('rij,drj->dri', rounded(weights).astype(jnp.float32), value_rows.astype(jnp.float32))
    return (numerator / denominator[None]).astype(jnp.bfloat16)

def reference(latent, att_gain, qkv_weight, out_weight, stencil_weight, block_gain, up_weight, down_weight):
    channels, lat_rows, lon_cols = latent.shape
    head_size = C // H
    normed = norm_channels(latent.astype(jnp.float32), att_gain).astype(jnp.bfloat16).reshape(channels, -1)
    projected = [jnp.dot(qkv_weight[slot], normed, preferred_element_type=jnp.float32).reshape(H, head_size, lat_rows, lon_cols) for slot in range(3)]
    queries = unit_heads(projected[0]).astype(jnp.bfloat16)
    key_rows = unit_heads(projected[1]).astype(jnp.bfloat16)
    value_rows = projected[2].astype(jnp.bfloat16)
    attended = lax.map(attend_head, (queries, key_rows, value_rows)).reshape(channels, -1)
    update = group_sum(out_weight, attended)
    latent_state = rounded(latent.astype(jnp.float32) + update.reshape(latent.shape))
    for block_index in range(BLOCKS):
        smoothed = rounded(stencil(latent_state.astype(jnp.float32), stencil_weight[block_index]))
        block_normed = norm_channels(smoothed.astype(jnp.float32), block_gain[block_index]).astype(jnp.bfloat16).reshape(channels, -1)
        hidden = jax.nn.gelu(jnp.dot(up_weight[block_index], block_normed, preferred_element_type=jnp.float32)).astype(jnp.bfloat16)
        update = group_sum(down_weight[block_index], hidden)
        latent_state = rounded(latent_state.astype(jnp.float32) + update.reshape(latent.shape))
    return latent_state
```

```python
import math

import jax
import jax.numpy as jnp
from jax import lax
from jax.sharding import PartitionSpec as P

C = 512
H = 8
BLOCKS = 2


attention_scale = 24.0
band_start = 30.0
grid_step = 0.25
epsilon = 1e-06


def with_halo(array, sides, width):
    for axis, dim in sides:
        devices, length = (lax.axis_size(axis), array.shape[dim])
        up = [(i, (i + 1) % devices) for i in range(devices)]
        down = [(j, i) for i, j in up]
        last = lax.slice_in_dim(array, length - width, length, axis=dim)
        leading = lax.slice_in_dim(array, 0, width, axis=dim)
        before = lax.ppermute(last, axis, up)
        after = lax.ppermute(leading, axis, down)
        array = jnp.concatenate([before, array, after], axis=dim)
    return array


def secant_rows(count):
    rows = jnp.arange(count).astype(jnp.float32)
    return 1.0 / jnp.cos((band_start + grid_step * rows) * (math.pi / 180.0))


def norm_channels(values, gain):
    scale = lax.rsqrt(jnp.mean(values * values, axis=0, keepdims=True) + epsilon)
    return values * scale * gain[:, None, None]


def unit_heads(values):
    return values * lax.rsqrt(jnp.sum(values * values, axis=1, keepdims=True) + epsilon)


def gather_channels(values):
    return lax.all_gather(values, "lev", axis=0, tiled=True)


def scatter_sum(partial, axis):
    devices = lax.axis_size(axis)
    me = lax.axis_index(axis)
    blocks = partial.reshape(devices, -1, *partial.shape[1:])
    total = jnp.take(blocks, me, axis=0).astype(jnp.float32)
    for shift in range(1, devices):
        pairs = [(i, (i + shift) % devices) for i in range(devices)]
        chunk = jnp.take(blocks, (me + shift) % devices, axis=0)
        total = total + lax.ppermute(chunk, axis, pairs).astype(jnp.float32)
    return total


def spread_sum(weight, activation):
    partial = lax.dot_general(
        weight, activation, (((0,), (0,)), ((), ())), preferred_element_type=jnp.float32
    ).astype(jnp.bfloat16)
    return scatter_sum(partial, "lev")


def gather_strips(values, axis):
    devices = lax.axis_size(axis)
    pieces = [values]
    for shift in range(1, devices):
        pairs = [(i, (i + shift) % devices) for i in range(devices)]
        pieces.append(lax.ppermute(values, axis, pairs))
    return jnp.concatenate(pieces, axis=-1)


def make_fold(queries, pieces):
    key_part, value_part = pieces
    scores = (
        jnp.einsum("hdri,hdrj->hrij", queries, key_part, preferred_element_type=jnp.float32)
        * attention_scale
    )
    weights = jnp.exp(scores)
    numerator = jnp.einsum(
        "hrij,hdrj->hdri",
        weights.astype(jnp.bfloat16),
        value_part,
        preferred_element_type=jnp.float32,
    )
    return (numerator, jnp.sum(weights, axis=3))


def block_apply(extended, block_index, stencil_weight, block_gain, up_weight, down_weight):
    lat_rows = extended.shape[1]
    out_cols = extended.shape[2] - 2
    secants = secant_rows(lat_rows)[None, :, None]
    padded = jnp.pad(extended.astype(jnp.float32), ((0, 0), (1, 1), (0, 0)))
    tap_weights = stencil_weight[block_index]
    stencil_sum = jnp.zeros((extended.shape[0], lat_rows, out_cols), jnp.float32)
    for row_step in (-1, 0, 1):
        for col_step in (-1, 0, 1):
            shifted = padded[
                :, 1 + row_step : 1 + row_step + lat_rows, 1 + col_step : 1 + col_step + out_cols
            ]
            tap_row = tap_weights[3 * (row_step + 1) + col_step + 1][:, None, None]
            if col_step != 0:
                stencil_sum = stencil_sum + tap_row * secants * shifted
            else:
                stencil_sum = stencil_sum + tap_row * shifted
    smoothed = stencil_sum.astype(jnp.bfloat16)
    full_channels = gather_channels(smoothed)
    block_normed = norm_channels(full_channels.astype(jnp.float32), block_gain[block_index]).astype(
        jnp.bfloat16
    )
    block_normed = block_normed.reshape(full_channels.shape[0], -1)
    hidden = jax.nn.gelu(
        jnp.dot(up_weight[block_index], block_normed, preferred_element_type=jnp.float32)
    ).astype(jnp.bfloat16)
    update = spread_sum(down_weight[block_index], hidden)
    center = extended[:, :, 1:-1]
    return (center.astype(jnp.float32) + update.reshape(center.shape)).astype(jnp.bfloat16)


def per_device(
    latent, att_gain, qkv_weight, out_weight, stencil_weight, block_gain, up_weight, down_weight
):
    ch_local, lat_rows, columns = latent.shape
    head_size = C // H
    heads_local = qkv_weight.shape[1] // head_size
    gathered = gather_channels(latent)
    normed = norm_channels(gathered.astype(jnp.float32), att_gain).astype(jnp.bfloat16)
    projected = jnp.einsum("koc,crw->korw", qkv_weight, normed, preferred_element_type=jnp.float32)
    projected = projected.reshape(3, heads_local, head_size, lat_rows, columns)
    queries = unit_heads(projected[0]).astype(jnp.bfloat16)
    key_rows = unit_heads(projected[1]).astype(jnp.bfloat16)
    value_rows = projected[2].astype(jnp.bfloat16)
    key_value = gather_strips(jnp.stack([key_rows, value_rows]), "lon")
    numerator, denominator = make_fold(queries, (key_value[0], key_value[1]))
    attended = (numerator / denominator[:, None]).astype(jnp.bfloat16)
    update = spread_sum(out_weight, attended.reshape(ch_local, -1))
    latent_state = (latent.astype(jnp.float32) + update.reshape(latent.shape)).astype(jnp.bfloat16)
    current = latent_state
    for block_index in range(BLOCKS):
        extended = with_halo(current, (("lon", 2),), 1)
        current = block_apply(
            extended, block_index, stencil_weight, block_gain, up_weight, down_weight
        )
    return current


def solution(mesh):
    placed = (
        P("lev", "member", "lon"),
        P(),
        P(None, "lev", None),
        P("lev", None),
        P(None, None, "lev"),
        P(),
        P(None, "lev", None),
        P(None, "lev", None),
    )
    return jax.shard_map(
        per_device, mesh=mesh, in_specs=placed, out_specs=P("lev", "member", "lon"), check_vma=False
    )
```

```python
import math

import jax
import jax.numpy as jnp
from jax import lax
from jax.sharding import PartitionSpec as P

C = 512
H = 8
BLOCKS = 2


attention_scale = 24.0
band_start = 30.0
grid_step = 0.25
epsilon = 1e-06


def secant_rows(count):
    rows = jnp.arange(count).astype(jnp.float32)
    return 1.0 / jnp.cos((band_start + grid_step * rows) * (math.pi / 180.0))


def norm_channels(values, gain):
    scale = lax.rsqrt(jnp.mean(values * values, axis=0, keepdims=True) + epsilon)
    return values * scale * gain[:, None, None]


def unit_heads(values):
    return values * lax.rsqrt(jnp.sum(values * values, axis=1, keepdims=True) + epsilon)


def gather_channels(values):
    return lax.all_gather(values, "lev", axis=0, tiled=True)


def scatter_sum(partial, axis, halo=False):
    devices = lax.axis_size(axis)
    me = lax.axis_index(axis)
    strips = lax.axis_size("lon")
    blocks = partial.reshape(devices, -1, *partial.shape[1:])
    total = jnp.take(blocks, me, axis=0).astype(jnp.float32)
    before = jnp.zeros(total.shape[:-1] + (1,), jnp.float32)
    after = jnp.zeros(total.shape[:-1] + (1,), jnp.float32)
    for shift in range(devices):
        chunk = jnp.take(blocks, (me + shift) % devices, axis=0)
        if shift:
            pairs = [(i, (i + shift) % devices) for i in range(devices)]
            total = total + lax.ppermute(chunk, axis, pairs).astype(jnp.float32)
        if halo:
            for step, edge, sums in ((1, chunk[..., -1:], "before"), (-1, chunk[..., :1], "after")):
                pairs = [
                    (s * devices + i, ((s + step) % strips) * devices + (i + shift) % devices)
                    for s in range(strips)
                    for i in range(devices)
                ]
                got = lax.ppermute(edge, ("lon", axis), pairs).astype(jnp.float32)
                if sums == "before":
                    before = before + got
                else:
                    after = after + got
    return total, before, after


def spread_sum(weight, activation, shape, halo=False):
    partial = lax.dot_general(
        weight, activation, (((0,), (0,)), ((), ())), preferred_element_type=jnp.float32
    ).astype(jnp.bfloat16)
    return scatter_sum(partial.reshape(weight.shape[1], *shape), "lev", halo)


def add_update(state, sums):
    return tuple((s.astype(jnp.float32) + u).astype(jnp.bfloat16) for s, u in zip(state, sums))


def gather_strips(values, axis):
    devices = lax.axis_size(axis)
    pieces = [values]
    for shift in range(1, devices):
        pairs = [(i, (i + shift) % devices) for i in range(devices)]
        pieces.append(lax.ppermute(values, axis, pairs))
    return jnp.concatenate(pieces, axis=-1)


def make_fold(queries, pieces):
    key_part, value_part = pieces
    scores = (
        jnp.einsum("hdri,hdrj->hrij", queries, key_part, preferred_element_type=jnp.float32)
        * attention_scale
    )
    weights = jnp.exp(scores)
    numerator = jnp.einsum(
        "hrij,hdrj->hdri",
        weights.astype(jnp.bfloat16),
        value_part,
        preferred_element_type=jnp.float32,
    )
    return (numerator, jnp.sum(weights, axis=3))


def block_apply(state, block_index, stencil_weight, block_gain, up_weight, down_weight, halo):
    extended = jnp.concatenate([state[1], state[0], state[2]], axis=2)
    lat_rows = extended.shape[1]
    out_cols = extended.shape[2] - 2
    secants = secant_rows(lat_rows)[None, :, None]
    padded = jnp.pad(extended.astype(jnp.float32), ((0, 0), (1, 1), (0, 0)))
    tap_weights = stencil_weight[block_index]
    stencil_sum = jnp.zeros((extended.shape[0], lat_rows, out_cols), jnp.float32)
    for row_step in (-1, 0, 1):
        for col_step in (-1, 0, 1):
            shifted = padded[
                :, 1 + row_step : 1 + row_step + lat_rows, 1 + col_step : 1 + col_step + out_cols
            ]
            tap_row = tap_weights[3 * (row_step + 1) + col_step + 1][:, None, None]
            if col_step != 0:
                stencil_sum = stencil_sum + tap_row * secants * shifted
            else:
                stencil_sum = stencil_sum + tap_row * shifted
    smoothed = stencil_sum.astype(jnp.bfloat16)
    full_channels = gather_channels(smoothed)
    block_normed = norm_channels(full_channels.astype(jnp.float32), block_gain[block_index]).astype(
        jnp.bfloat16
    )
    block_normed = block_normed.reshape(full_channels.shape[0], -1)
    hidden = jax.nn.gelu(
        jnp.dot(up_weight[block_index], block_normed, preferred_element_type=jnp.float32)
    ).astype(jnp.bfloat16)
    sums = spread_sum(down_weight[block_index], hidden, state[0].shape[1:], halo)
    return add_update(state, sums)


def per_device(
    latent, att_gain, qkv_weight, out_weight, stencil_weight, block_gain, up_weight, down_weight
):
    ch_local, lat_rows, columns = latent.shape
    head_size = C // H
    heads_local = qkv_weight.shape[1] // head_size
    gathered = gather_channels(latent)
    normed = norm_channels(gathered.astype(jnp.float32), att_gain).astype(jnp.bfloat16)
    projected = jnp.einsum("koc,crw->korw", qkv_weight, normed, preferred_element_type=jnp.float32)
    projected = projected.reshape(3, heads_local, head_size, lat_rows, columns)
    queries = unit_heads(projected[0]).astype(jnp.bfloat16)
    key_rows = unit_heads(projected[1]).astype(jnp.bfloat16)
    value_rows = projected[2].astype(jnp.bfloat16)
    key_value = gather_strips(jnp.stack([key_rows, value_rows]), "lon")
    numerator, denominator = make_fold(queries, (key_value[0], key_value[1]))
    attended = (numerator / denominator[:, None]).astype(jnp.bfloat16)
    strips = lax.axis_size("lon")
    latent_before = lax.ppermute(latent[..., -1:], "lon", [(i, (i + 1) % strips) for i in range(strips)])
    latent_after = lax.ppermute(latent[..., :1], "lon", [(i, (i - 1) % strips) for i in range(strips)])
    sums = spread_sum(out_weight, attended.reshape(ch_local, -1), latent.shape[1:], True)
    current = add_update((latent, latent_before, latent_after), sums)
    for block_index in range(BLOCKS):
        current = block_apply(
            current, block_index, stencil_weight, block_gain, up_weight, down_weight,
            block_index < BLOCKS - 1,
        )
    return current[0]


def solution(mesh):
    placed = (
        P("lev", "member", "lon"),
        P(),
        P(None, "lev", None),
        P("lev", None),
        P(None, None, "lev"),
        P(),
        P(None, "lev", None),
        P(None, "lev", None),
    )
    return jax.shard_map(
        per_device, mesh=mesh, in_specs=placed, out_specs=P("lev", "member", "lon"), check_vma=False
    )
```

```python
import math

import jax
import jax.numpy as jnp
from jax import lax
from jax.sharding import PartitionSpec as P

C = 512
H = 8
BLOCKS = 2


attention_scale = 24.0
band_start = 30.0
grid_step = 0.25
epsilon = 1e-06


def secant_rows(count):
    rows = jnp.arange(count).astype(jnp.float32)
    return 1.0 / jnp.cos((band_start + grid_step * rows) * (math.pi / 180.0))


def norm_channels(values, gain):
    scale = lax.rsqrt(jnp.mean(values * values, axis=0, keepdims=True) + epsilon)
    return values * scale * gain[:, None, None]


def unit_heads(values):
    return values * lax.rsqrt(jnp.sum(values * values, axis=1, keepdims=True) + epsilon)


def gather_channels(values):
    return lax.all_gather(values, "lev", axis=0, tiled=True)


def scatter_sum(partial, axis):
    devices = lax.axis_size(axis)
    me = lax.axis_index(axis)
    blocks = partial.reshape(devices, -1, *partial.shape[1:])
    total = jnp.take(blocks, me, axis=0).astype(jnp.float32)
    for shift in range(1, devices):
        pairs = [(i, (i + shift) % devices) for i in range(devices)]
        chunk = jnp.take(blocks, (me + shift) % devices, axis=0)
        total = total + lax.ppermute(chunk, axis, pairs).astype(jnp.float32)
    return total


def spread_sum(weight, activation):
    partial = lax.dot_general(
        weight, activation, (((0,), (0,)), ((), ())), preferred_element_type=jnp.float32
    ).astype(jnp.bfloat16)
    return scatter_sum(partial, "lev")


def gather_strips(values, axis):
    devices = lax.axis_size(axis)
    pieces = [values]
    for shift in range(1, devices):
        pairs = [(i, (i + shift) % devices) for i in range(devices)]
        pieces.append(lax.ppermute(values, axis, pairs))
    return jnp.concatenate(pieces, axis=-1)


def make_fold(queries, pieces):
    key_part, value_part = pieces
    scores = (
        jnp.einsum("hdri,hdrj->hrij", queries, key_part, preferred_element_type=jnp.float32)
        * attention_scale
    )
    weights = jnp.exp(scores)
    numerator = jnp.einsum(
        "hrij,hdrj->hdri",
        weights.astype(jnp.bfloat16),
        value_part,
        preferred_element_type=jnp.float32,
    )
    return (numerator, jnp.sum(weights, axis=3))


def block_apply(state, block_index, stencil_weight, block_gain, up_weight, down_weight):
    lat_rows = state.shape[1]
    out_cols = state.shape[2] - 2
    secants = secant_rows(lat_rows)[None, :, None]
    padded = jnp.pad(state.astype(jnp.float32), ((0, 0), (1, 1), (0, 0)))
    tap_weights = stencil_weight[block_index]
    stencil_sum = jnp.zeros((state.shape[0], lat_rows, out_cols), jnp.float32)
    for row_step in (-1, 0, 1):
        for col_step in (-1, 0, 1):
            shifted = padded[
                :, 1 + row_step : 1 + row_step + lat_rows, 1 + col_step : 1 + col_step + out_cols
            ]
            tap_row = tap_weights[3 * (row_step + 1) + col_step + 1][:, None, None]
            if col_step != 0:
                stencil_sum = stencil_sum + tap_row * secants * shifted
            else:
                stencil_sum = stencil_sum + tap_row * shifted
    smoothed = stencil_sum.astype(jnp.bfloat16)
    full_channels = gather_channels(smoothed)
    block_normed = norm_channels(full_channels.astype(jnp.float32), block_gain[block_index]).astype(
        jnp.bfloat16
    )
    block_normed = block_normed.reshape(full_channels.shape[0], -1)
    hidden = jax.nn.gelu(
        jnp.dot(up_weight[block_index], block_normed, preferred_element_type=jnp.float32)
    ).astype(jnp.bfloat16)
    update = spread_sum(down_weight[block_index], hidden)
    center = state[:, :, 1:-1]
    return (center.astype(jnp.float32) + update.reshape(center.shape)).astype(jnp.bfloat16)


def edges(values, width):
    return jnp.concatenate([values[..., :width], values[..., -width:]], axis=-1)


def per_device(
    latent, att_gain, qkv_weight, out_weight, stencil_weight, block_gain, up_weight, down_weight
):
    ch_local, lat_rows, columns = latent.shape
    head_size = C // H
    heads_local = qkv_weight.shape[1] // head_size
    reach = BLOCKS
    gathered = gather_channels(latent)
    normed = norm_channels(gathered.astype(jnp.float32), att_gain).astype(jnp.bfloat16)
    projected = jnp.einsum("koc,crw->korw", qkv_weight, normed, preferred_element_type=jnp.float32)
    projected = projected.reshape(3, heads_local, head_size, lat_rows, columns)
    queries = unit_heads(projected[0]).astype(jnp.bfloat16)
    key_rows = unit_heads(projected[1]).astype(jnp.bfloat16)
    value_rows = projected[2].astype(jnp.bfloat16)

    key_value = jnp.stack([key_rows, value_rows]).reshape(-1, lat_rows, columns)
    rim = jnp.stack([edges(queries.reshape(ch_local, lat_rows, columns), reach), edges(latent, reach)])
    rim_rows = rim.size // (lat_rows * columns)
    payload = jnp.concatenate([key_value, rim.reshape(rim_rows, lat_rows, columns)], axis=0)
    strips = lax.axis_size("lon")
    pieces = [key_value]
    from_left = from_right = None
    for shift in range(1, strips):
        pairs = [(i, (i + shift) % strips) for i in range(strips)]
        sent = payload if shift in (1, strips - 1) else key_value
        got = lax.ppermute(sent, "lon", pairs)
        pieces.append(got[: key_value.shape[0]])
        if shift == 1:
            from_left = got[key_value.shape[0] :].reshape(rim.shape)[..., reach:]
        if shift == strips - 1:
            from_right = got[key_value.shape[0] :].reshape(rim.shape)[..., :reach]
    all_keys = jnp.concatenate(pieces, axis=-1).reshape(2, heads_local, head_size, lat_rows, -1)
    wide_queries = jnp.concatenate(
        [from_left[0], queries.reshape(ch_local, lat_rows, columns), from_right[0]], axis=-1
    ).reshape(heads_local, head_size, lat_rows, -1)
    wide_latent = jnp.concatenate([from_left[1], latent, from_right[1]], axis=-1)

    numerator, denominator = make_fold(wide_queries, (all_keys[0], all_keys[1]))
    attended = (numerator / denominator[:, None]).astype(jnp.bfloat16)
    update = spread_sum(out_weight, attended.reshape(ch_local, -1))
    current = (wide_latent.astype(jnp.float32) + update.reshape(wide_latent.shape)).astype(
        jnp.bfloat16
    )
    for block_index in range(BLOCKS):
        current = block_apply(
            current, block_index, stencil_weight, block_gain, up_weight, down_weight
        )
    return current


def solution(mesh):
    placed = (
        P("lev", "member", "lon"),
        P(),
        P(None, "lev", None),
        P("lev", None),
        P(None, None, "lev"),
        P(),
        P(None, "lev", None),
        P(None, "lev", None),
    )
    return jax.shard_map(
        per_device, mesh=mesh, in_specs=placed, out_specs=P("lev", "member", "lon"), check_vma=False
    )
```

```python
import math

import jax
import jax.numpy as jnp
from jax import lax
from jax.sharding import PartitionSpec as P

C = 512
H = 8
BLOCKS = 2


attention_scale = 24.0
band_start = 30.0
grid_step = 0.25
epsilon = 1e-06


def secant_rows(count):
    rows = jnp.arange(count).astype(jnp.float32)
    return 1.0 / jnp.cos((band_start + grid_step * rows) * (math.pi / 180.0))


def norm_channels(values, gain):
    scale = lax.rsqrt(jnp.mean(values * values, axis=0, keepdims=True) + epsilon)
    return values * scale * gain[:, None, None]


def unit_heads(values):
    return values * lax.rsqrt(jnp.sum(values * values, axis=1, keepdims=True) + epsilon)


def gather_channels(values):
    return lax.all_gather(values, "lev", axis=0, tiled=True)


def spread_sum(weight, activation):
    devices = lax.axis_size("lev")
    me = lax.axis_index("lev")
    width = weight.shape[1] // devices

    def chunk(shift):
        block = lax.dynamic_slice_in_dim(weight, ((me + shift) % devices) * width, width, axis=1)
        return lax.dot_general(
            block, activation, (((0,), (0,)), ((), ())), preferred_element_type=jnp.float32
        ).astype(jnp.bfloat16)

    total = chunk(0).astype(jnp.float32)
    for shift in range(1, devices):
        pairs = [(i, (i + shift) % devices) for i in range(devices)]
        total = total + lax.ppermute(chunk(shift), "lev", pairs).astype(jnp.float32)
    return total


def make_fold(queries, pieces):
    numerator = denominator = 0.0
    for key_part, value_part in pieces:
        scores = (
            jnp.einsum("hdri,hdrj->hrij", queries, key_part, preferred_element_type=jnp.float32)
            * attention_scale
        )
        weights = jnp.exp(scores)
        numerator = numerator + jnp.einsum(
            "hrij,hdrj->hdri",
            weights.astype(jnp.bfloat16),
            value_part,
            preferred_element_type=jnp.float32,
        )
        denominator = denominator + jnp.sum(weights, axis=3)
    return (numerator, denominator)


def block_apply(state, block_index, stencil_weight, block_gain, up_weight, down_weight):
    lat_rows = state.shape[1]
    out_cols = state.shape[2] - 2
    secants = secant_rows(lat_rows)[None, :, None]
    padded = jnp.pad(state.astype(jnp.float32), ((0, 0), (1, 1), (0, 0)))
    tap_weights = stencil_weight[block_index]
    stencil_sum = jnp.zeros((state.shape[0], lat_rows, out_cols), jnp.float32)
    for row_step in (-1, 0, 1):
        for col_step in (-1, 0, 1):
            shifted = padded[
                :, 1 + row_step : 1 + row_step + lat_rows, 1 + col_step : 1 + col_step + out_cols
            ]
            tap_row = tap_weights[3 * (row_step + 1) + col_step + 1][:, None, None]
            if col_step != 0:
                stencil_sum = stencil_sum + tap_row * secants * shifted
            else:
                stencil_sum = stencil_sum + tap_row * shifted
    smoothed = stencil_sum.astype(jnp.bfloat16)
    full_channels = gather_channels(smoothed)
    block_normed = norm_channels(full_channels.astype(jnp.float32), block_gain[block_index]).astype(
        jnp.bfloat16
    )
    block_normed = block_normed.reshape(full_channels.shape[0], -1)
    hidden = jax.nn.gelu(
        jnp.dot(up_weight[block_index], block_normed, preferred_element_type=jnp.float32)
    ).astype(jnp.bfloat16)
    update = spread_sum(down_weight[block_index], hidden)
    center = state[:, :, 1:-1]
    return (center.astype(jnp.float32) + update.reshape(center.shape)).astype(jnp.bfloat16)


def edges(values, width):
    return jnp.concatenate([values[..., :width], values[..., -width:]], axis=-1)


def per_device(
    latent, att_gain, qkv_weight, out_weight, stencil_weight, block_gain, up_weight, down_weight
):
    ch_local, lat_rows, columns = latent.shape
    head_size = C // H
    heads_local = qkv_weight.shape[1] // head_size
    reach = BLOCKS
    gathered = gather_channels(latent)
    normed = norm_channels(gathered.astype(jnp.float32), att_gain).astype(jnp.bfloat16)
    projected = jnp.einsum("koc,crw->korw", qkv_weight, normed, preferred_element_type=jnp.float32)
    projected = projected.reshape(3, heads_local, head_size, lat_rows, columns)
    queries = unit_heads(projected[0]).astype(jnp.bfloat16)
    key_rows = unit_heads(projected[1]).astype(jnp.bfloat16)
    value_rows = projected[2].astype(jnp.bfloat16)

    key_value = jnp.stack([key_rows, value_rows]).reshape(-1, lat_rows, columns)
    rim = jnp.stack([edges(queries.reshape(ch_local, lat_rows, columns), reach), edges(latent, reach)])
    rim_rows = rim.size // (lat_rows * columns)
    payload = jnp.concatenate([key_value, rim.reshape(rim_rows, lat_rows, columns)], axis=0)
    strips = lax.axis_size("lon")
    kv_shape = (2, heads_local, head_size, lat_rows, columns)
    pieces = [(key_rows, value_rows)]
    from_left = from_right = None
    for shift in range(1, strips):
        pairs = [(i, (i + shift) % strips) for i in range(strips)]
        got = lax.ppermute(payload, "lon", pairs)
        kv = got[: key_value.shape[0]].reshape(kv_shape)
        pieces.append((kv[0], kv[1]))
        if shift == 1:
            from_left = got[key_value.shape[0] :].reshape(rim.shape)[..., reach:]
        if shift == strips - 1:
            from_right = got[key_value.shape[0] :].reshape(rim.shape)[..., :reach]
    wide_queries = jnp.concatenate(
        [from_left[0], queries.reshape(ch_local, lat_rows, columns), from_right[0]], axis=-1
    ).reshape(heads_local, head_size, lat_rows, -1)
    wide_latent = jnp.concatenate([from_left[1], latent, from_right[1]], axis=-1)

    numerator, denominator = make_fold(wide_queries, pieces)
    attended = (numerator / denominator[:, None]).astype(jnp.bfloat16)
    update = spread_sum(out_weight, attended.reshape(ch_local, -1))
    current = (wide_latent.astype(jnp.float32) + update.reshape(wide_latent.shape)).astype(
        jnp.bfloat16
    )
    for block_index in range(BLOCKS):
        current = block_apply(
            current, block_index, stencil_weight, block_gain, up_weight, down_weight
        )
    return current


def solution(mesh):
    placed = (
        P("lev", "member", "lon"),
        P(),
        P(None, "lev", None),
        P("lev", None),
        P(None, None, "lev"),
        P(),
        P(None, "lev", None),
        P(None, "lev", None),
    )
    return jax.shard_map(
        per_device, mesh=mesh, in_specs=placed, out_specs=P("lev", "member", "lon"), check_vma=False
    )
```

```python
import math

import jax
import jax.numpy as jnp
from jax import lax
from jax.sharding import PartitionSpec as P

C = 512
H = 8
BLOCKS = 2


attention_scale = 24.0
band_start = 30.0
grid_step = 0.25
epsilon = 1e-06


def secant_rows(count):
    rows = jnp.arange(count).astype(jnp.float32)
    return 1.0 / jnp.cos((band_start + grid_step * rows) * (math.pi / 180.0))


def norm_channels(values, gain):
    scale = lax.rsqrt(jnp.mean(values * values, axis=0, keepdims=True) + epsilon)
    return values * scale * gain[:, None, None]


def unit_heads(values):
    return values * lax.rsqrt(jnp.sum(values * values, axis=1, keepdims=True) + epsilon)


def gather_channels(values):
    return lax.all_gather(values, "lev", axis=0, tiled=True)


def spread_sum(weight, activation):
    devices = lax.axis_size("lev")
    me = lax.axis_index("lev")
    width = weight.shape[1] // devices

    def chunk(shift):
        block = lax.dynamic_slice_in_dim(weight, ((me + shift) % devices) * width, width, axis=1)
        return lax.dot_general(
            block, activation, (((0,), (0,)), ((), ())), preferred_element_type=jnp.float32
        ).astype(jnp.bfloat16)

    total = chunk(0).astype(jnp.float32)
    for shift in range(1, devices):
        pairs = [(i, (i + shift) % devices) for i in range(devices)]
        total = total + lax.ppermute(chunk(shift), "lev", pairs).astype(jnp.float32)
    return total


def gather_strips(values, axis):
    devices = lax.axis_size(axis)
    pieces = [values]
    for shift in range(1, devices):
        pairs = [(i, (i + shift) % devices) for i in range(devices)]
        pieces.append(lax.ppermute(values, axis, pairs))
    return jnp.concatenate(pieces, axis=-1)


def make_fold(queries, pieces):
    key_part, value_part = pieces
    scores = (
        jnp.einsum("hdri,hdrj->hrij", queries, key_part, preferred_element_type=jnp.float32)
        * attention_scale
    )
    weights = jnp.exp(scores)
    numerator = jnp.einsum(
        "hrij,hdrj->hdri",
        weights.astype(jnp.bfloat16),
        value_part,
        preferred_element_type=jnp.float32,
    )
    return (numerator, jnp.sum(weights, axis=3))


def block_apply(state, block_index, stencil_weight, block_gain, up_weight, down_weight):
    lat_rows = state.shape[1]
    out_cols = state.shape[2] - 2
    secants = secant_rows(lat_rows)[None, :, None]
    padded = jnp.pad(state.astype(jnp.float32), ((0, 0), (1, 1), (0, 0)))
    tap_weights = stencil_weight[block_index]
    stencil_sum = jnp.zeros((state.shape[0], lat_rows, out_cols), jnp.float32)
    for row_step in (-1, 0, 1):
        for col_step in (-1, 0, 1):
            shifted = padded[
                :, 1 + row_step : 1 + row_step + lat_rows, 1 + col_step : 1 + col_step + out_cols
            ]
            tap_row = tap_weights[3 * (row_step + 1) + col_step + 1][:, None, None]
            if col_step != 0:
                stencil_sum = stencil_sum + tap_row * secants * shifted
            else:
                stencil_sum = stencil_sum + tap_row * shifted
    smoothed = stencil_sum.astype(jnp.bfloat16)
    full_channels = gather_channels(smoothed)
    block_normed = norm_channels(full_channels.astype(jnp.float32), block_gain[block_index]).astype(
        jnp.bfloat16
    )
    block_normed = block_normed.reshape(full_channels.shape[0], -1)
    hidden = jax.nn.gelu(
        jnp.dot(up_weight[block_index], block_normed, preferred_element_type=jnp.float32)
    ).astype(jnp.bfloat16)
    update = spread_sum(down_weight[block_index], hidden)
    center = state[:, :, 1:-1]
    return (center.astype(jnp.float32) + update.reshape(center.shape)).astype(jnp.bfloat16)


def edges(values, width):
    return jnp.concatenate([values[..., :width], values[..., -width:]], axis=-1)


def per_device(
    latent, att_gain, qkv_weight, out_weight, stencil_weight, block_gain, up_weight, down_weight
):
    ch_local, lat_rows, columns = latent.shape
    head_size = C // H
    heads_local = qkv_weight.shape[1] // head_size
    reach = BLOCKS
    gathered = gather_channels(latent)
    normed = norm_channels(gathered.astype(jnp.float32), att_gain).astype(jnp.bfloat16)
    projected = jnp.einsum("koc,crw->korw", qkv_weight, normed, preferred_element_type=jnp.float32)
    projected = projected.reshape(3, heads_local, head_size, lat_rows, columns)
    queries = unit_heads(projected[0]).astype(jnp.bfloat16)
    key_rows = unit_heads(projected[1]).astype(jnp.bfloat16)
    value_rows = projected[2].astype(jnp.bfloat16)

    key_value = jnp.stack([key_rows, value_rows]).reshape(-1, lat_rows, columns)
    rim = jnp.stack([edges(queries.reshape(ch_local, lat_rows, columns), reach), edges(latent, reach)])
    rim_rows = rim.size // (lat_rows * columns)
    payload = jnp.concatenate([key_value, rim.reshape(rim_rows, lat_rows, columns)], axis=0)
    strips = lax.axis_size("lon")
    pieces = [key_value]
    from_left = from_right = None
    for shift in range(1, strips):
        pairs = [(i, (i + shift) % strips) for i in range(strips)]
        sent = payload if shift in (1, strips - 1) else key_value
        got = lax.ppermute(sent, "lon", pairs)
        pieces.append(got[: key_value.shape[0]])
        if shift == 1:
            from_left = got[key_value.shape[0] :].reshape(rim.shape)[..., reach:]
        if shift == strips - 1:
            from_right = got[key_value.shape[0] :].reshape(rim.shape)[..., :reach]
    all_keys = jnp.concatenate(pieces, axis=-1).reshape(2, heads_local, head_size, lat_rows, -1)
    wide_queries = jnp.concatenate(
        [from_left[0], queries.reshape(ch_local, lat_rows, columns), from_right[0]], axis=-1
    ).reshape(heads_local, head_size, lat_rows, -1)
    wide_latent = jnp.concatenate([from_left[1], latent, from_right[1]], axis=-1)

    numerator, denominator = make_fold(wide_queries, (all_keys[0], all_keys[1]))
    attended = (numerator / denominator[:, None]).astype(jnp.bfloat16)
    update = spread_sum(out_weight, attended.reshape(ch_local, -1))
    current = (wide_latent.astype(jnp.float32) + update.reshape(wide_latent.shape)).astype(
        jnp.bfloat16
    )
    for block_index in range(BLOCKS):
        current = block_apply(
            current, block_index, stencil_weight, block_gain, up_weight, down_weight
        )
    return current


def solution(mesh):
    placed = (
        P("lev", "member", "lon"),
        P(),
        P(None, "lev", None),
        P("lev", None),
        P(None, None, "lev"),
        P(),
        P(None, "lev", None),
        P(None, "lev", None),
    )
    return jax.shard_map(
        per_device, mesh=mesh, in_specs=placed, out_specs=P("lev", "member", "lon"), check_vma=False
    )
```

```python
import math

import jax
import jax.numpy as jnp
from jax import lax
from jax.sharding import PartitionSpec as P

C = 512
H = 8
BLOCKS = 2


attention_scale = 24.0
band_start = 30.0
grid_step = 0.25
epsilon = 1e-06


def secant_rows(count):
    rows = jnp.arange(count).astype(jnp.float32)
    return 1.0 / jnp.cos((band_start + grid_step * rows) * (math.pi / 180.0))


def norm_channels(values, gain):
    scale = lax.rsqrt(jnp.mean(values * values, axis=0, keepdims=True) + epsilon)
    return values * scale * gain[:, None, None]


def unit_heads(values):
    return values * lax.rsqrt(jnp.sum(values * values, axis=1, keepdims=True) + epsilon)


def gather_channels(values):
    return lax.all_gather(values, "lev", axis=0, tiled=True)


def scatter_sum(partial, axis):
    devices = lax.axis_size(axis)
    me = lax.axis_index(axis)
    blocks = partial.reshape(devices, -1, *partial.shape[1:])
    total = jnp.take(blocks, me, axis=0).astype(jnp.float32)
    for shift in range(1, devices):
        pairs = [(i, (i + shift) % devices) for i in range(devices)]
        chunk = jnp.take(blocks, (me + shift) % devices, axis=0)
        total = total + lax.ppermute(chunk, axis, pairs).astype(jnp.float32)
    return total


def spread_sum(weight, activation):
    partial = lax.dot_general(
        weight, activation, (((0,), (0,)), ((), ())), preferred_element_type=jnp.float32
    ).astype(jnp.bfloat16)
    return scatter_sum(partial, "lev")


def gather_strips(values, axis):
    devices = lax.axis_size(axis)
    pieces = [values]
    for shift in range(1, devices):
        pairs = [(i, (i + shift) % devices) for i in range(devices)]
        pieces.append(lax.ppermute(values, axis, pairs))
    return jnp.concatenate(pieces, axis=-1)


def make_fold(queries, pieces):
    key_part, value_part = pieces
    scores = (
        jnp.einsum("hdri,hdrj->hrij", queries, key_part, preferred_element_type=jnp.float32)
        * attention_scale
    )
    weights = jnp.exp(scores)
    numerator = jnp.einsum(
        "hrij,hdrj->hdri",
        weights.astype(jnp.bfloat16),
        value_part,
        preferred_element_type=jnp.float32,
    )
    return (numerator, jnp.sum(weights, axis=3))


def block_apply(state, block_index, stencil_weight, block_gain, up_weight, down_weight):
    lat_rows = state.shape[1]
    out_cols = state.shape[2] - 2
    secants = secant_rows(lat_rows)[None, :, None]
    padded = jnp.pad(state.astype(jnp.float32), ((0, 0), (1, 1), (0, 0)))
    tap_weights = stencil_weight[block_index]
    stencil_sum = jnp.zeros((state.shape[0], lat_rows, out_cols), jnp.float32)
    for row_step in (-1, 0, 1):
        for col_step in (-1, 0, 1):
            shifted = padded[
                :, 1 + row_step : 1 + row_step + lat_rows, 1 + col_step : 1 + col_step + out_cols
            ]
            tap_row = tap_weights[3 * (row_step + 1) + col_step + 1][:, None, None]
            if col_step != 0:
                stencil_sum = stencil_sum + tap_row * secants * shifted
            else:
                stencil_sum = stencil_sum + tap_row * shifted
    smoothed = stencil_sum.astype(jnp.bfloat16)
    full_channels = gather_channels(smoothed)
    block_normed = norm_channels(full_channels.astype(jnp.float32), block_gain[block_index]).astype(
        jnp.bfloat16
    )
    block_normed = block_normed.reshape(full_channels.shape[0], -1)
    hidden = jax.nn.gelu(
        jnp.dot(up_weight[block_index], block_normed, preferred_element_type=jnp.float32)
    ).astype(jnp.bfloat16)
    update = spread_sum(down_weight[block_index], hidden)
    center = state[:, :, 1:-1]
    return (center.astype(jnp.float32) + update.reshape(center.shape)).astype(jnp.bfloat16)


def edges(values, width):
    return jnp.concatenate([values[..., :width], values[..., -width:]], axis=-1)


def per_device(
    latent, att_gain, qkv_weight, out_weight, stencil_weight, block_gain, up_weight, down_weight
):
    ch_local, lat_rows, columns = latent.shape
    head_size = C // H
    heads_local = qkv_weight.shape[1] // head_size
    reach = BLOCKS
    gathered = gather_channels(latent)
    normed = norm_channels(gathered.astype(jnp.float32), att_gain).astype(jnp.bfloat16)
    projected = jnp.einsum("koc,crw->korw", qkv_weight, normed, preferred_element_type=jnp.float32)
    projected = projected.reshape(3, heads_local, head_size, lat_rows, columns)
    queries = unit_heads(projected[0]).astype(jnp.bfloat16)
    key_rows = unit_heads(projected[1]).astype(jnp.bfloat16)
    value_rows = projected[2].astype(jnp.bfloat16)

    strips = lax.axis_size("lon")
    split = lat_rows // 2
    arrived = None
    states = []
    for low, high in ((0, split), (split, lat_rows)):
        rows = high - low
        key_value = jnp.stack([key_rows, value_rows])[:, :, :, low:high].reshape(-1, rows, columns)
        own_queries = queries[:, :, low:high].reshape(ch_local, rows, columns)
        own_latent = latent[:, low:high]
        rim = jnp.stack([edges(own_queries, reach), edges(own_latent, reach)])
        rim_rows = rim.size // (rows * columns)
        payload = jnp.concatenate([key_value, rim.reshape(rim_rows, rows, columns)], axis=0)
        if arrived is not None:
            key_value, payload = lax.optimization_barrier((key_value, payload, arrived))[:2]
        pieces = [key_value]
        from_left = from_right = None
        for shift in range(1, strips):
            pairs = [(i, (i + shift) % strips) for i in range(strips)]
            sent = payload if shift in (1, strips - 1) else key_value
            got = lax.ppermute(sent, "lon", pairs)
            pieces.append(got[: key_value.shape[0]])
            if shift == 1:
                from_left = got[key_value.shape[0] :].reshape(rim.shape)[..., reach:]
            if shift == strips - 1:
                from_right = got[key_value.shape[0] :].reshape(rim.shape)[..., :reach]
        arrived = pieces[1:]
        all_keys = jnp.concatenate(pieces, axis=-1).reshape(2, heads_local, head_size, rows, -1)
        wide_queries = jnp.concatenate([from_left[0], own_queries, from_right[0]], axis=-1).reshape(
            heads_local, head_size, rows, -1
        )
        wide_latent = jnp.concatenate([from_left[1], own_latent, from_right[1]], axis=-1)
        numerator, denominator = make_fold(wide_queries, (all_keys[0], all_keys[1]))
        attended = (numerator / denominator[:, None]).astype(jnp.bfloat16)
        update = spread_sum(out_weight, attended.reshape(ch_local, -1))
        states.append(
            (wide_latent.astype(jnp.float32) + update.reshape(wide_latent.shape)).astype(jnp.bfloat16)
        )
    current = jnp.concatenate(states, axis=1)
    for block_index in range(BLOCKS):
        current = block_apply(
            current, block_index, stencil_weight, block_gain, up_weight, down_weight
        )
    return current


def solution(mesh):
    placed = (
        P("lev", "member", "lon"),
        P(),
        P(None, "lev", None),
        P("lev", None),
        P(None, None, "lev"),
        P(),
        P(None, "lev", None),
        P(None, "lev", None),
    )
    return jax.shard_map(
        per_device, mesh=mesh, in_specs=placed, out_specs=P("lev", "member", "lon"), check_vma=False
    )
```

```python
import math

import jax
import jax.numpy as jnp
from jax import lax
from jax.sharding import PartitionSpec as P

C = 512
H = 8
BLOCKS = 2


attention_scale = 24.0
band_start = 30.0
grid_step = 0.25
epsilon = 1e-06


def secant_rows(count):
    rows = jnp.arange(count).astype(jnp.float32)
    return 1.0 / jnp.cos((band_start + grid_step * rows) * (math.pi / 180.0))


def norm_channels(values, gain):
    scale = lax.rsqrt(jnp.mean(values * values, axis=0, keepdims=True) + epsilon)
    return values * scale * gain[:, None, None]


def unit_heads(values):
    return values * lax.rsqrt(jnp.sum(values * values, axis=1, keepdims=True) + epsilon)


def gather_channels(values):
    return lax.all_gather(values, "lev", axis=0, tiled=True)


def scatter_sum(partial, axis):
    devices = lax.axis_size(axis)
    me = lax.axis_index(axis)
    blocks = partial.reshape(devices, -1, *partial.shape[1:])
    total = jnp.take(blocks, me, axis=0).astype(jnp.float32)
    for shift in range(1, devices):
        pairs = [(i, (i + shift) % devices) for i in range(devices)]
        chunk = jnp.take(blocks, (me + shift) % devices, axis=0)
        total = total + lax.ppermute(chunk, axis, pairs).astype(jnp.float32)
    return total


def spread_sum(weight, activation):
    partial = lax.dot_general(
        weight, activation, (((0,), (0,)), ((), ())), preferred_element_type=jnp.float32
    ).astype(jnp.bfloat16)
    return scatter_sum(partial, "lev")


def gather_strips(values, axis):
    devices = lax.axis_size(axis)
    pieces = [values]
    for shift in range(1, devices):
        pairs = [(i, (i + shift) % devices) for i in range(devices)]
        pieces.append(lax.ppermute(values, axis, pairs))
    return jnp.concatenate(pieces, axis=-1)


def make_fold(queries, pieces):
    key_part, value_part = pieces
    scores = (
        jnp.einsum("hdri,hdrj->hrij", queries, key_part, preferred_element_type=jnp.float32)
        * attention_scale
    )
    weights = jnp.exp(scores)
    numerator = jnp.einsum(
        "hrij,hdrj->hdri",
        weights.astype(jnp.bfloat16),
        value_part,
        preferred_element_type=jnp.float32,
    )
    return (numerator, jnp.sum(weights, axis=3))


def block_apply(state, block_index, stencil_weight, block_gain, up_weight, down_weight):
    lat_rows = state.shape[1]
    out_cols = state.shape[2] - 2
    secants = secant_rows(lat_rows)[None, :, None]
    padded = jnp.pad(state.astype(jnp.float32), ((0, 0), (1, 1), (0, 0)))
    tap_weights = stencil_weight[block_index]
    stencil_sum = jnp.zeros((state.shape[0], lat_rows, out_cols), jnp.float32)
    for row_step in (-1, 0, 1):
        for col_step in (-1, 0, 1):
            shifted = padded[
                :, 1 + row_step : 1 + row_step + lat_rows, 1 + col_step : 1 + col_step + out_cols
            ]
            tap_row = tap_weights[3 * (row_step + 1) + col_step + 1][:, None, None]
            if col_step != 0:
                stencil_sum = stencil_sum + tap_row * secants * shifted
            else:
                stencil_sum = stencil_sum + tap_row * shifted
    smoothed = stencil_sum.astype(jnp.bfloat16)
    full_channels = gather_channels(smoothed)
    block_normed = norm_channels(full_channels.astype(jnp.float32), block_gain[block_index]).astype(
        jnp.bfloat16
    )
    block_normed = block_normed.reshape(full_channels.shape[0], -1)
    hidden = jax.nn.gelu(
        jnp.dot(up_weight[block_index], block_normed, preferred_element_type=jnp.float32)
    ).astype(jnp.bfloat16)
    update = spread_sum(down_weight[block_index], hidden)
    center = state[:, :, 1:-1]
    return (center.astype(jnp.float32) + update.reshape(center.shape)).astype(jnp.bfloat16)


def edges(values, width):
    return jnp.concatenate([values[..., :width], values[..., -width:]], axis=-1)


def per_device(
    latent, att_gain, qkv_weight, out_weight, stencil_weight, block_gain, up_weight, down_weight
):
    ch_local, lat_rows, columns = latent.shape
    head_size = C // H
    heads_local = qkv_weight.shape[1] // head_size
    reach = BLOCKS
    gathered = gather_channels(latent)
    normed = norm_channels(gathered.astype(jnp.float32), att_gain).astype(jnp.bfloat16)
    projected = jnp.einsum("koc,crw->korw", qkv_weight, normed, preferred_element_type=jnp.float32)
    projected = projected.reshape(3, heads_local, head_size, lat_rows, columns)
    queries = unit_heads(projected[0]).astype(jnp.bfloat16)
    key_rows = unit_heads(projected[1]).astype(jnp.bfloat16)
    value_rows = projected[2].astype(jnp.bfloat16)

    key_value = jnp.stack([key_rows, value_rows]).reshape(-1, lat_rows, columns)
    strips = lax.axis_size("lon")
    pieces = [key_value]
    for shift in range(1, strips):
        pairs = [(i, (i + shift) % strips) for i in range(strips)]
        pieces.append(lax.ppermute(key_value, "lon", pairs))
    all_keys = jnp.concatenate(pieces, axis=-1).reshape(2, heads_local, head_size, lat_rows, -1)
    flat_queries = queries.reshape(ch_local, lat_rows, columns)
    rim_right = jnp.stack([flat_queries[..., -reach:], latent[..., -reach:]])
    rim_left = jnp.stack([flat_queries[..., :reach], latent[..., :reach]])
    from_left = lax.ppermute(rim_right, "lon", [(i, (i + 1) % strips) for i in range(strips)])
    from_right = lax.ppermute(rim_left, "lon", [(i, (i - 1) % strips) for i in range(strips)])
    wide_queries = jnp.concatenate([from_left[0], flat_queries, from_right[0]], axis=-1).reshape(
        heads_local, head_size, lat_rows, -1
    )
    wide_latent = jnp.concatenate([from_left[1], latent, from_right[1]], axis=-1)

    numerator, denominator = make_fold(wide_queries, (all_keys[0], all_keys[1]))
    attended = (numerator / denominator[:, None]).astype(jnp.bfloat16)
    update = spread_sum(out_weight, attended.reshape(ch_local, -1))
    current = (wide_latent.astype(jnp.float32) + update.reshape(wide_latent.shape)).astype(
        jnp.bfloat16
    )
    for block_index in range(BLOCKS):
        current = block_apply(
            current, block_index, stencil_weight, block_gain, up_weight, down_weight
        )
    return current


def solution(mesh):
    placed = (
        P("lev", "member", "lon"),
        P(),
        P(None, "lev", None),
        P("lev", None),
        P(None, None, "lev"),
        P(),
        P(None, "lev", None),
        P(None, "lev", None),
    )
    return jax.shard_map(
        per_device, mesh=mesh, in_specs=placed, out_specs=P("lev", "member", "lon"), check_vma=False
    )
```

```python
import math

import jax
import jax.numpy as jnp
from jax import lax
from jax.sharding import PartitionSpec as P

C = 512
H = 8
BLOCKS = 2


attention_scale = 24.0
band_start = 30.0
grid_step = 0.25
epsilon = 1e-06


def secant_rows(count):
    rows = jnp.arange(count).astype(jnp.float32)
    return 1.0 / jnp.cos((band_start + grid_step * rows) * (math.pi / 180.0))


def norm_channels(values, gain):
    scale = lax.rsqrt(jnp.mean(values * values, axis=0, keepdims=True) + epsilon)
    return values * scale * gain[:, None, None]


def unit_heads(values):
    return values * lax.rsqrt(jnp.sum(values * values, axis=1, keepdims=True) + epsilon)


def gather_channels(values):
    return lax.all_gather(values, "lev", axis=0, tiled=True)


def scatter_sum(partial, axis):
    devices = lax.axis_size(axis)
    me = lax.axis_index(axis)
    blocks = partial.reshape(devices, -1, *partial.shape[1:])
    total = jnp.take(blocks, me, axis=0).astype(jnp.float32)
    for shift in range(1, devices):
        pairs = [(i, (i + shift) % devices) for i in range(devices)]
        chunk = jnp.take(blocks, (me + shift) % devices, axis=0)
        total = total + lax.ppermute(chunk, axis, pairs).astype(jnp.float32)
    return total


def spread_sum(weight, activation):
    partial = lax.dot_general(
        weight, activation, (((0,), (0,)), ((), ())), preferred_element_type=jnp.float32
    ).astype(jnp.bfloat16)
    return scatter_sum(partial, "lev")


def gather_strips(values, axis):
    devices = lax.axis_size(axis)
    pieces = [values]
    for shift in range(1, devices):
        pairs = [(i, (i + shift) % devices) for i in range(devices)]
        pieces.append(lax.ppermute(values, axis, pairs))
    return jnp.concatenate(pieces, axis=-1)


def make_fold(queries, pieces):
    key_part, value_part = pieces
    scores = (
        jnp.einsum("hdri,phdrj->hripj", queries, key_part, preferred_element_type=jnp.float32)
        * attention_scale
    )
    weights = jnp.exp(scores)
    numerator = jnp.einsum(
        "hripj,phdrj->hdri",
        weights.astype(jnp.bfloat16),
        value_part,
        preferred_element_type=jnp.float32,
    )
    return (numerator, jnp.sum(weights, axis=(3, 4)))


def block_apply(state, block_index, stencil_weight, block_gain, up_weight, down_weight):
    lat_rows = state.shape[1]
    out_cols = state.shape[2] - 2
    secants = secant_rows(lat_rows)[None, :, None]
    padded = jnp.pad(state.astype(jnp.float32), ((0, 0), (1, 1), (0, 0)))
    tap_weights = stencil_weight[block_index]
    stencil_sum = jnp.zeros((state.shape[0], lat_rows, out_cols), jnp.float32)
    for row_step in (-1, 0, 1):
        for col_step in (-1, 0, 1):
            shifted = padded[
                :, 1 + row_step : 1 + row_step + lat_rows, 1 + col_step : 1 + col_step + out_cols
            ]
            tap_row = tap_weights[3 * (row_step + 1) + col_step + 1][:, None, None]
            if col_step != 0:
                stencil_sum = stencil_sum + tap_row * secants * shifted
            else:
                stencil_sum = stencil_sum + tap_row * shifted
    smoothed = stencil_sum.astype(jnp.bfloat16)
    full_channels = gather_channels(smoothed)
    block_normed = norm_channels(full_channels.astype(jnp.float32), block_gain[block_index]).astype(
        jnp.bfloat16
    )
    block_normed = block_normed.reshape(full_channels.shape[0], -1)
    hidden = jax.nn.gelu(
        jnp.dot(up_weight[block_index], block_normed, preferred_element_type=jnp.float32)
    ).astype(jnp.bfloat16)
    update = spread_sum(down_weight[block_index], hidden)
    center = state[:, :, 1:-1]
    return (center.astype(jnp.float32) + update.reshape(center.shape)).astype(jnp.bfloat16)


def edges(values, width):
    return jnp.concatenate([values[..., :width], values[..., -width:]], axis=-1)


def per_device(
    latent, att_gain, qkv_weight, out_weight, stencil_weight, block_gain, up_weight, down_weight
):
    ch_local, lat_rows, columns = latent.shape
    head_size = C // H
    heads_local = qkv_weight.shape[1] // head_size
    reach = BLOCKS
    gathered = gather_channels(latent)
    normed = norm_channels(gathered.astype(jnp.float32), att_gain).astype(jnp.bfloat16)
    projected = jnp.einsum("koc,crw->korw", qkv_weight, normed, preferred_element_type=jnp.float32)
    projected = projected.reshape(3, heads_local, head_size, lat_rows, columns)
    queries = unit_heads(projected[0]).astype(jnp.bfloat16)
    key_rows = unit_heads(projected[1]).astype(jnp.bfloat16)
    value_rows = projected[2].astype(jnp.bfloat16)

    key_value = jnp.stack([key_rows, value_rows]).reshape(-1, lat_rows, columns)
    rim = jnp.stack([edges(queries.reshape(ch_local, lat_rows, columns), reach), edges(latent, reach)])
    rim_rows = rim.size // (lat_rows * columns)
    payload = jnp.concatenate([key_value, rim.reshape(rim_rows, lat_rows, columns)], axis=0)
    strips = lax.axis_size("lon")
    pieces = [key_value]
    from_left = from_right = None
    for shift in range(1, strips):
        pairs = [(i, (i + shift) % strips) for i in range(strips)]
        sent = payload if shift in (1, strips - 1) else key_value
        got = lax.ppermute(sent, "lon", pairs)
        pieces.append(got[: key_value.shape[0]])
        if shift == 1:
            from_left = got[key_value.shape[0] :].reshape(rim.shape)[..., reach:]
        if shift == strips - 1:
            from_right = got[key_value.shape[0] :].reshape(rim.shape)[..., :reach]
    all_keys = jnp.stack(pieces).reshape(strips, 2, heads_local, head_size, lat_rows, columns)
    wide_queries = jnp.concatenate(
        [from_left[0], queries.reshape(ch_local, lat_rows, columns), from_right[0]], axis=-1
    ).reshape(heads_local, head_size, lat_rows, -1)
    wide_latent = jnp.concatenate([from_left[1], latent, from_right[1]], axis=-1)

    numerator, denominator = make_fold(wide_queries, (all_keys[:, 0], all_keys[:, 1]))
    attended = (numerator / denominator[:, None]).astype(jnp.bfloat16)
    update = spread_sum(out_weight, attended.reshape(ch_local, -1))
    current = (wide_latent.astype(jnp.float32) + update.reshape(wide_latent.shape)).astype(
        jnp.bfloat16
    )
    for block_index in range(BLOCKS):
        current = block_apply(
            current, block_index, stencil_weight, block_gain, up_weight, down_weight
        )
    return current


def solution(mesh):
    placed = (
        P("lev", "member", "lon"),
        P(),
        P(None, "lev", None),
        P("lev", None),
        P(None, None, "lev"),
        P(),
        P(None, "lev", None),
        P(None, "lev", None),
    )
    return jax.shard_map(
        per_device, mesh=mesh, in_specs=placed, out_specs=P("lev", "member", "lon"), check_vma=False
    )
```

```python
import math

import jax
import jax.numpy as jnp
from jax import lax
from jax.sharding import PartitionSpec as P

C = 512
H = 8
BLOCKS = 2


attention_scale = 24.0
band_start = 30.0
grid_step = 0.25
epsilon = 1e-06


def secant_rows(count):
    rows = jnp.arange(count).astype(jnp.float32)
    return 1.0 / jnp.cos((band_start + grid_step * rows) * (math.pi / 180.0))


def norm_channels(values, gain):
    scale = lax.rsqrt(jnp.mean(values * values, axis=0, keepdims=True) + epsilon)
    return values * scale * gain[:, None, None]


def unit_heads(values):
    return values * lax.rsqrt(jnp.sum(values * values, axis=1, keepdims=True) + epsilon)


def gather_channels(values):
    return lax.all_gather(values, "lev", axis=0, tiled=True)


def scatter_sum(partial, axis):
    devices = lax.axis_size(axis)
    me = lax.axis_index(axis)
    blocks = partial.reshape(devices, -1, *partial.shape[1:])
    total = jnp.take(blocks, me, axis=0).astype(jnp.float32)
    for shift in range(1, devices):
        pairs = [(i, (i + shift) % devices) for i in range(devices)]
        chunk = jnp.take(blocks, (me + shift) % devices, axis=0)
        total = total + lax.ppermute(chunk, axis, pairs).astype(jnp.float32)
    return total


def spread_sum(weight, activation):
    partial = lax.dot_general(
        weight, activation, (((0,), (0,)), ((), ())), preferred_element_type=jnp.float32
    ).astype(jnp.bfloat16)
    return scatter_sum(partial, "lev")


def gather_strips(values, axis):
    devices = lax.axis_size(axis)
    pieces = [values]
    for shift in range(1, devices):
        pairs = [(i, (i + shift) % devices) for i in range(devices)]
        pieces.append(lax.ppermute(values, axis, pairs))
    return jnp.concatenate(pieces, axis=-1)


def make_fold(queries, pieces):
    key_part, value_part = pieces
    scores = (
        jnp.einsum("hdri,phdrj->hripj", queries, key_part, preferred_element_type=jnp.float32)
        * attention_scale
    )
    weights = jnp.exp(scores)
    numerator = jnp.einsum(
        "hripj,phdrj->hdri",
        weights.astype(jnp.bfloat16),
        value_part,
        preferred_element_type=jnp.float32,
    )
    return (numerator, jnp.sum(weights, axis=(3, 4)))


def block_apply(state, block_index, stencil_weight, block_gain, up_weight, down_weight):
    lat_rows = state.shape[1]
    out_cols = state.shape[2] - 2
    secants = secant_rows(lat_rows)[None, :, None]
    padded = jnp.pad(state.astype(jnp.float32), ((0, 0), (1, 1), (0, 0)))
    tap_weights = stencil_weight[block_index]
    stencil_sum = jnp.zeros((state.shape[0], lat_rows, out_cols), jnp.float32)
    for row_step in (-1, 0, 1):
        for col_step in (-1, 0, 1):
            shifted = padded[
                :, 1 + row_step : 1 + row_step + lat_rows, 1 + col_step : 1 + col_step + out_cols
            ]
            tap_row = tap_weights[3 * (row_step + 1) + col_step + 1][:, None, None]
            if col_step != 0:
                stencil_sum = stencil_sum + tap_row * secants * shifted
            else:
                stencil_sum = stencil_sum + tap_row * shifted
    smoothed = stencil_sum.astype(jnp.bfloat16)
    full_channels = gather_channels(smoothed)
    block_normed = norm_channels(full_channels.astype(jnp.float32), block_gain[block_index]).astype(
        jnp.bfloat16
    )
    block_normed = block_normed.reshape(full_channels.shape[0], -1)
    hidden = jax.nn.gelu(
        jnp.dot(up_weight[block_index], block_normed, preferred_element_type=jnp.float32)
    ).astype(jnp.bfloat16)
    update = spread_sum(down_weight[block_index], hidden)
    center = state[:, :, 1:-1]
    return (center.astype(jnp.float32) + update.reshape(center.shape)).astype(jnp.bfloat16)


def edges(values, width):
    return jnp.concatenate([values[..., :width], values[..., -width:]], axis=-1)


def per_device(
    latent, att_gain, qkv_weight, out_weight, stencil_weight, block_gain, up_weight, down_weight
):
    ch_local, lat_rows, columns = latent.shape
    head_size = C // H
    heads_local = qkv_weight.shape[1] // head_size
    reach = BLOCKS
    gathered = gather_channels(latent)
    normed = norm_channels(gathered.astype(jnp.float32), att_gain).astype(jnp.bfloat16)
    projected = jnp.einsum("koc,crw->korw", qkv_weight, normed, preferred_element_type=jnp.float32)
    projected = projected.reshape(3, heads_local, head_size, lat_rows, columns)
    queries = unit_heads(projected[0]).astype(jnp.bfloat16)
    key_rows = unit_heads(projected[1]).astype(jnp.bfloat16)
    value_rows = projected[2].astype(jnp.bfloat16)

    key_value = jnp.stack([key_rows, value_rows]).reshape(-1, lat_rows, columns)
    flat_queries = queries.reshape(ch_local, lat_rows, columns)
    rim = jnp.stack([edges(flat_queries, reach), edges(latent, reach)]).transpose(0, 3, 2, 1)
    rim_rows = rim.size // (lat_rows * columns)
    payload = jnp.concatenate([key_value, rim.reshape(rim_rows, lat_rows, columns)], axis=0)
    strips = lax.axis_size("lon")
    pieces = [key_value]
    from_left = from_right = None
    for shift in range(1, strips):
        pairs = [(i, (i + shift) % strips) for i in range(strips)]
        sent = payload if shift in (1, strips - 1) else key_value
        got = lax.ppermute(sent, "lon", pairs)
        pieces.append(got[: key_value.shape[0]])
        if shift == 1:
            from_left = got[key_value.shape[0] :].reshape(rim.shape)[:, reach:].transpose(0, 3, 2, 1)
        if shift == strips - 1:
            from_right = got[key_value.shape[0] :].reshape(rim.shape)[:, :reach].transpose(0, 3, 2, 1)
    all_keys = jnp.stack(pieces).reshape(strips, 2, heads_local, head_size, lat_rows, columns)
    wide_queries = jnp.concatenate([from_left[0], flat_queries, from_right[0]], axis=-1).reshape(
        heads_local, head_size, lat_rows, -1
    )
    wide_latent = jnp.concatenate([from_left[1], latent, from_right[1]], axis=-1)

    numerator, denominator = make_fold(wide_queries, (all_keys[:, 0], all_keys[:, 1]))
    attended = (numerator / denominator[:, None]).astype(jnp.bfloat16)
    update = spread_sum(out_weight, attended.reshape(ch_local, -1))
    current = (wide_latent.astype(jnp.float32) + update.reshape(wide_latent.shape)).astype(
        jnp.bfloat16
    )
    for block_index in range(BLOCKS):
        current = block_apply(
            current, block_index, stencil_weight, block_gain, up_weight, down_weight
        )
    return current


def solution(mesh):
    placed = (
        P("lev", "member", "lon"),
        P(),
        P(None, "lev", None),
        P("lev", None),
        P(None, None, "lev"),
        P(),
        P(None, "lev", None),
        P(None, "lev", None),
    )
    return jax.shard_map(
        per_device, mesh=mesh, in_specs=placed, out_specs=P("lev", "member", "lon"), check_vma=False
    )
```

```python
import math

import jax
import jax.numpy as jnp
from jax import lax
from jax.sharding import PartitionSpec as P

C = 512
H = 8
BLOCKS = 2


attention_scale = 24.0
band_start = 30.0
grid_step = 0.25
epsilon = 1e-06


def secant_rows(count):
    rows = jnp.arange(count).astype(jnp.float32)
    return 1.0 / jnp.cos((band_start + grid_step * rows) * (math.pi / 180.0))


def norm_channels(values, gain):
    scale = lax.rsqrt(jnp.mean(values * values, axis=0, keepdims=True) + epsilon)
    return values * scale * gain[:, None, None]


def unit_heads(values):
    return values * lax.rsqrt(jnp.sum(values * values, axis=1, keepdims=True) + epsilon)


def gather_channels(values):
    return lax.all_gather(values, "lev", axis=0, tiled=True)


def scatter_sum(partial, axis):
    devices = lax.axis_size(axis)
    me = lax.axis_index(axis)
    chips, core = devices // 2, me % 2
    chip = me // 2
    blocks = partial.reshape(chips, 2, -1, *partial.shape[1:])
    mine = jnp.take(blocks, core, axis=1).astype(jnp.float32)
    theirs = jnp.take(blocks, 1 - core, axis=1)
    pair = mine + lax.ppermute(theirs, axis, [(i, i ^ 1) for i in range(devices)]).astype(jnp.float32)
    total = jnp.take(pair, chip, axis=0)
    for shift in range(1, chips):
        pairs = [(i, ((i // 2 + shift) % chips) * 2 + i % 2) for i in range(devices)]
        sent = jnp.take(pair, (chip + shift) % chips, axis=0).astype(jnp.bfloat16)
        total = total + lax.ppermute(sent, axis, pairs).astype(jnp.float32)
    return total


def spread_sum(weight, activation):
    partial = lax.dot_general(
        weight, activation, (((0,), (0,)), ((), ())), preferred_element_type=jnp.float32
    ).astype(jnp.bfloat16)
    return scatter_sum(partial, "lev")


def gather_strips(values, axis):
    devices = lax.axis_size(axis)
    pieces = [values]
    for shift in range(1, devices):
        pairs = [(i, (i + shift) % devices) for i in range(devices)]
        pieces.append(lax.ppermute(values, axis, pairs))
    return jnp.concatenate(pieces, axis=-1)


def make_fold(queries, pieces):
    key_part, value_part = pieces
    scores = (
        jnp.einsum("hdri,phdrj->hripj", queries, key_part, preferred_element_type=jnp.float32)
        * attention_scale
    )
    weights = jnp.exp(scores)
    numerator = jnp.einsum(
        "hripj,phdrj->hdri",
        weights.astype(jnp.bfloat16),
        value_part,
        preferred_element_type=jnp.float32,
    )
    return (numerator, jnp.sum(weights, axis=(3, 4)))


def block_apply(state, block_index, stencil_weight, block_gain, up_weight, down_weight):
    lat_rows = state.shape[1]
    out_cols = state.shape[2] - 2
    secants = secant_rows(lat_rows)[None, :, None]
    padded = jnp.pad(state.astype(jnp.float32), ((0, 0), (1, 1), (0, 0)))
    tap_weights = stencil_weight[block_index]
    stencil_sum = jnp.zeros((state.shape[0], lat_rows, out_cols), jnp.float32)
    for row_step in (-1, 0, 1):
        for col_step in (-1, 0, 1):
            shifted = padded[
                :, 1 + row_step : 1 + row_step + lat_rows, 1 + col_step : 1 + col_step + out_cols
            ]
            tap_row = tap_weights[3 * (row_step + 1) + col_step + 1][:, None, None]
            if col_step != 0:
                stencil_sum = stencil_sum + tap_row * secants * shifted
            else:
                stencil_sum = stencil_sum + tap_row * shifted
    smoothed = stencil_sum.astype(jnp.bfloat16)
    full_channels = gather_channels(smoothed)
    block_normed = norm_channels(full_channels.astype(jnp.float32), block_gain[block_index]).astype(
        jnp.bfloat16
    )
    block_normed = block_normed.reshape(full_channels.shape[0], -1)
    hidden = jax.nn.gelu(
        jnp.dot(up_weight[block_index], block_normed, preferred_element_type=jnp.float32)
    ).astype(jnp.bfloat16)
    update = spread_sum(down_weight[block_index], hidden)
    center = state[:, :, 1:-1]
    return (center.astype(jnp.float32) + update.reshape(center.shape)).astype(jnp.bfloat16)


def edges(values, width):
    return jnp.concatenate([values[..., :width], values[..., -width:]], axis=-1)


def per_device(
    latent, att_gain, qkv_weight, out_weight, stencil_weight, block_gain, up_weight, down_weight
):
    ch_local, lat_rows, columns = latent.shape
    head_size = C // H
    heads_local = qkv_weight.shape[1] // head_size
    reach = BLOCKS
    gathered = gather_channels(latent)
    normed = norm_channels(gathered.astype(jnp.float32), att_gain).astype(jnp.bfloat16)
    projected = jnp.einsum("koc,crw->korw", qkv_weight, normed, preferred_element_type=jnp.float32)
    projected = projected.reshape(3, heads_local, head_size, lat_rows, columns)
    queries = unit_heads(projected[0]).astype(jnp.bfloat16)
    key_rows = unit_heads(projected[1]).astype(jnp.bfloat16)
    value_rows = projected[2].astype(jnp.bfloat16)

    key_value = jnp.stack([key_rows, value_rows]).reshape(-1, lat_rows, columns)
    rim = jnp.stack([edges(queries.reshape(ch_local, lat_rows, columns), reach), edges(latent, reach)])
    rim_rows = rim.size // (lat_rows * columns)
    payload = jnp.concatenate([key_value, rim.reshape(rim_rows, lat_rows, columns)], axis=0)
    strips = lax.axis_size("lon")
    pieces = [key_value]
    from_left = from_right = None
    for shift in range(1, strips):
        pairs = [(i, (i + shift) % strips) for i in range(strips)]
        sent = payload if shift in (1, strips - 1) else key_value
        got = lax.ppermute(sent, "lon", pairs)
        pieces.append(got[: key_value.shape[0]])
        if shift == 1:
            from_left = got[key_value.shape[0] :].reshape(rim.shape)[..., reach:]
        if shift == strips - 1:
            from_right = got[key_value.shape[0] :].reshape(rim.shape)[..., :reach]
    all_keys = jnp.stack(pieces).reshape(strips, 2, heads_local, head_size, lat_rows, columns)
    wide_queries = jnp.concatenate(
        [from_left[0], queries.reshape(ch_local, lat_rows, columns), from_right[0]], axis=-1
    ).reshape(heads_local, head_size, lat_rows, -1)
    wide_latent = jnp.concatenate([from_left[1], latent, from_right[1]], axis=-1)

    numerator, denominator = make_fold(wide_queries, (all_keys[:, 0], all_keys[:, 1]))
    attended = (numerator / denominator[:, None]).astype(jnp.bfloat16)
    update = spread_sum(out_weight, attended.reshape(ch_local, -1))
    current = (wide_latent.astype(jnp.float32) + update.reshape(wide_latent.shape)).astype(
        jnp.bfloat16
    )
    for block_index in range(BLOCKS):
        current = block_apply(
            current, block_index, stencil_weight, block_gain, up_weight, down_weight
        )
    return current


def solution(mesh):
    placed = (
        P("lev", "member", "lon"),
        P(),
        P(None, "lev", None),
        P("lev", None),
        P(None, None, "lev"),
        P(),
        P(None, "lev", None),
        P(None, "lev", None),
    )
    return jax.shard_map(
        per_device, mesh=mesh, in_specs=placed, out_specs=P("lev", "member", "lon"), check_vma=False
    )
```

```python
import math

import jax
import jax.numpy as jnp
from jax import lax
from jax.sharding import PartitionSpec as P

C = 512
H = 8
BLOCKS = 2


attention_scale = 24.0
band_start = 30.0
grid_step = 0.25
epsilon = 1e-06


def secant_rows(count):
    rows = jnp.arange(count).astype(jnp.float32)
    return 1.0 / jnp.cos((band_start + grid_step * rows) * (math.pi / 180.0))


def norm_channels(values, gain):
    scale = lax.rsqrt(jnp.mean(values * values, axis=0, keepdims=True) + epsilon)
    return values * scale * gain[:, None, None]


def unit_heads(values):
    return values * lax.rsqrt(jnp.sum(values * values, axis=1, keepdims=True) + epsilon)


def gather_channels(values):
    devices = lax.axis_size("lev")
    me = lax.axis_index("lev")
    chips, core = devices // 2, me % 2
    chip = me // 2
    stacked = [values]
    for shift in range(1, chips):
        pairs = [(i, ((i // 2 - shift) % chips) * 2 + i % 2) for i in range(devices)]
        stacked.append(lax.ppermute(values, "lev", pairs))
    mine = jnp.roll(jnp.stack(stacked), chip, axis=0)
    theirs = lax.ppermute(mine, "lev", [(i, i ^ 1) for i in range(devices)])
    both = jnp.where(core == 0, jnp.stack([mine, theirs], axis=1), jnp.stack([theirs, mine], axis=1))
    return both.reshape(devices * values.shape[0], *values.shape[1:])


def scatter_sum(partial, axis):
    devices = lax.axis_size(axis)
    me = lax.axis_index(axis)
    chips, core = devices // 2, me % 2
    chip = me // 2
    blocks = partial.reshape(chips, 2, -1, *partial.shape[1:])
    mine = jnp.take(blocks, core, axis=1).astype(jnp.float32)
    theirs = jnp.take(blocks, 1 - core, axis=1)
    pair = mine + lax.ppermute(theirs, axis, [(i, i ^ 1) for i in range(devices)]).astype(jnp.float32)
    total = jnp.take(pair, chip, axis=0)
    for shift in range(1, chips):
        pairs = [(i, ((i // 2 + shift) % chips) * 2 + i % 2) for i in range(devices)]
        sent = jnp.take(pair, (chip + shift) % chips, axis=0).astype(jnp.bfloat16)
        total = total + lax.ppermute(sent, axis, pairs).astype(jnp.float32)
    return total


def spread_sum(weight, activation):
    partial = lax.dot_general(
        weight, activation, (((0,), (0,)), ((), ())), preferred_element_type=jnp.float32
    ).astype(jnp.bfloat16)
    return scatter_sum(partial, "lev")


def gather_strips(values, axis):
    devices = lax.axis_size(axis)
    pieces = [values]
    for shift in range(1, devices):
        pairs = [(i, (i + shift) % devices) for i in range(devices)]
        pieces.append(lax.ppermute(values, axis, pairs))
    return jnp.concatenate(pieces, axis=-1)


def make_fold(queries, pieces):
    key_part, value_part = pieces
    scores = (
        jnp.einsum("hdri,phdrj->hripj", queries, key_part, preferred_element_type=jnp.float32)
        * attention_scale
    )
    weights = jnp.exp(scores)
    numerator = jnp.einsum(
        "hripj,phdrj->hdri",
        weights.astype(jnp.bfloat16),
        value_part,
        preferred_element_type=jnp.float32,
    )
    return (numerator, jnp.sum(weights, axis=(3, 4)))


def block_apply(state, block_index, stencil_weight, block_gain, up_weight, down_weight):
    lat_rows = state.shape[1]
    out_cols = state.shape[2] - 2
    secants = secant_rows(lat_rows)[None, :, None]
    padded = jnp.pad(state.astype(jnp.float32), ((0, 0), (1, 1), (0, 0)))
    tap_weights = stencil_weight[block_index]
    stencil_sum = jnp.zeros((state.shape[0], lat_rows, out_cols), jnp.float32)
    for row_step in (-1, 0, 1):
        for col_step in (-1, 0, 1):
            shifted = padded[
                :, 1 + row_step : 1 + row_step + lat_rows, 1 + col_step : 1 + col_step + out_cols
            ]
            tap_row = tap_weights[3 * (row_step + 1) + col_step + 1][:, None, None]
            if col_step != 0:
                stencil_sum = stencil_sum + tap_row * secants * shifted
            else:
                stencil_sum = stencil_sum + tap_row * shifted
    smoothed = stencil_sum.astype(jnp.bfloat16)
    full_channels = gather_channels(smoothed)
    block_normed = norm_channels(full_channels.astype(jnp.float32), block_gain[block_index]).astype(
        jnp.bfloat16
    )
    block_normed = block_normed.reshape(full_channels.shape[0], -1)
    hidden = jax.nn.gelu(
        jnp.dot(up_weight[block_index], block_normed, preferred_element_type=jnp.float32)
    ).astype(jnp.bfloat16)
    update = spread_sum(down_weight[block_index], hidden)
    center = state[:, :, 1:-1]
    return (center.astype(jnp.float32) + update.reshape(center.shape)).astype(jnp.bfloat16)


def edges(values, width):
    return jnp.concatenate([values[..., :width], values[..., -width:]], axis=-1)


def per_device(
    latent, att_gain, qkv_weight, out_weight, stencil_weight, block_gain, up_weight, down_weight
):
    ch_local, lat_rows, columns = latent.shape
    head_size = C // H
    heads_local = qkv_weight.shape[1] // head_size
    reach = BLOCKS
    gathered = gather_channels(latent)
    normed = norm_channels(gathered.astype(jnp.float32), att_gain).astype(jnp.bfloat16)
    projected = jnp.einsum("koc,crw->korw", qkv_weight, normed, preferred_element_type=jnp.float32)
    projected = projected.reshape(3, heads_local, head_size, lat_rows, columns)
    queries = unit_heads(projected[0]).astype(jnp.bfloat16)
    key_rows = unit_heads(projected[1]).astype(jnp.bfloat16)
    value_rows = projected[2].astype(jnp.bfloat16)

    key_value = jnp.stack([key_rows, value_rows]).reshape(-1, lat_rows, columns)
    rim = jnp.stack([edges(queries.reshape(ch_local, lat_rows, columns), reach), edges(latent, reach)])
    rim_rows = rim.size // (lat_rows * columns)
    payload = jnp.concatenate([key_value, rim.reshape(rim_rows, lat_rows, columns)], axis=0)
    strips = lax.axis_size("lon")
    pieces = [key_value]
    from_left = from_right = None
    for shift in range(1, strips):
        pairs = [(i, (i + shift) % strips) for i in range(strips)]
        sent = payload if shift in (1, strips - 1) else key_value
        got = lax.ppermute(sent, "lon", pairs)
        pieces.append(got[: key_value.shape[0]])
        if shift == 1:
            from_left = got[key_value.shape[0] :].reshape(rim.shape)[..., reach:]
        if shift == strips - 1:
            from_right = got[key_value.shape[0] :].reshape(rim.shape)[..., :reach]
    all_keys = jnp.stack(pieces).reshape(strips, 2, heads_local, head_size, lat_rows, columns)
    wide_queries = jnp.concatenate(
        [from_left[0], queries.reshape(ch_local, lat_rows, columns), from_right[0]], axis=-1
    ).reshape(heads_local, head_size, lat_rows, -1)
    wide_latent = jnp.concatenate([from_left[1], latent, from_right[1]], axis=-1)

    numerator, denominator = make_fold(wide_queries, (all_keys[:, 0], all_keys[:, 1]))
    attended = (numerator / denominator[:, None]).astype(jnp.bfloat16)
    update = spread_sum(out_weight, attended.reshape(ch_local, -1))
    current = (wide_latent.astype(jnp.float32) + update.reshape(wide_latent.shape)).astype(
        jnp.bfloat16
    )
    for block_index in range(BLOCKS):
        current = block_apply(
            current, block_index, stencil_weight, block_gain, up_weight, down_weight
        )
    return current


def solution(mesh):
    placed = (
        P("lev", "member", "lon"),
        P(),
        P(None, "lev", None),
        P("lev", None),
        P(None, None, "lev"),
        P(),
        P(None, "lev", None),
        P(None, "lev", None),
    )
    return jax.shard_map(
        per_device, mesh=mesh, in_specs=placed, out_specs=P("lev", "member", "lon"), check_vma=False
    )
```

```python
import math

import jax
import jax.numpy as jnp
from jax import lax
from jax.sharding import PartitionSpec as P

C = 512
H = 8
BLOCKS = 2


attention_scale = 24.0
band_start = 30.0
grid_step = 0.25
epsilon = 1e-06


def secant_rows(count):
    rows = jnp.arange(count).astype(jnp.float32)
    return 1.0 / jnp.cos((band_start + grid_step * rows) * (math.pi / 180.0))


def norm_channels(values, gain):
    scale = lax.rsqrt(jnp.mean(values * values, axis=0, keepdims=True) + epsilon)
    return values * scale * gain[:, None, None]


def unit_heads(values):
    return values * lax.rsqrt(jnp.sum(values * values, axis=1, keepdims=True) + epsilon)


def gather_channels(values):
    return lax.all_gather(values, "lev", axis=0, tiled=True)


def scatter_sum(partial, axis):
    devices = lax.axis_size(axis)
    me = lax.axis_index(axis)
    chips, core = devices // 2, me % 2
    chip = me // 2
    blocks = partial.reshape(chips, 2, -1, *partial.shape[1:])
    mine = jnp.take(blocks, core, axis=1).astype(jnp.float32)
    theirs = jnp.take(blocks, 1 - core, axis=1)
    pair = mine + lax.ppermute(theirs, axis, [(i, i ^ 1) for i in range(devices)]).astype(jnp.float32)
    total = jnp.take(pair, chip, axis=0)
    for shift in range(1, chips):
        pairs = [(i, ((i // 2 + shift) % chips) * 2 + i % 2) for i in range(devices)]
        sent = jnp.take(pair, (chip + shift) % chips, axis=0).astype(jnp.bfloat16)
        total = total + lax.ppermute(sent, axis, pairs).astype(jnp.float32)
    return total


def core_half(values, axis=0):
    devices = lax.axis_size("lev")
    grouped = values.reshape(*values.shape[:axis], devices // 2, 2, -1, *values.shape[axis + 1 :])
    taken = jnp.take(grouped, lax.axis_index("lev") % 2, axis=axis + 1)
    return taken.reshape(*values.shape[:axis], -1, *values.shape[axis + 1 :])


def reduce_half(partial):
    devices = lax.axis_size("lev")
    me = lax.axis_index("lev")
    chips, core = devices // 2, me % 2
    blocks = partial.reshape(chips, 2, -1, *partial.shape[1:])
    mine = jnp.take(blocks, core, axis=1).astype(jnp.float32)
    theirs = jnp.take(blocks, 1 - core, axis=1)
    pair = mine + lax.ppermute(theirs, "lev", [(i, i ^ 1) for i in range(devices)]).astype(jnp.float32)
    pair = pair.astype(jnp.bfloat16)
    total = pair.astype(jnp.float32)
    for shift in range(1, chips):
        pairs = [(i, ((i // 2 + shift) % chips) * 2 + i % 2) for i in range(devices)]
        total = total + lax.ppermute(pair, "lev", pairs).astype(jnp.float32)
    return total.reshape(-1, *partial.shape[1:])


def gather_half(values):
    devices = lax.axis_size("lev")
    core = lax.axis_index("lev") % 2
    mine = values.reshape(devices // 2, -1, *values.shape[1:])
    theirs = lax.ppermute(mine, "lev", [(i, i ^ 1) for i in range(devices)])
    both = jnp.where(core == 0, jnp.stack([mine, theirs], axis=1), jnp.stack([theirs, mine], axis=1))
    return both.reshape(-1, *values.shape[1:])


def half_weights(weights):
    devices = lax.axis_size("lev")
    chips = devices // 2
    chip = lax.axis_index("lev") // 2
    stacked = [weights]
    for shift in range(1, chips):
        pairs = [(i, ((i // 2 - shift) % chips) * 2 + i % 2) for i in range(devices)]
        stacked.append(lax.ppermute(weights, "lev", pairs))
    ordered = jnp.roll(jnp.stack(stacked), chip, axis=0)
    return jnp.moveaxis(ordered, 0, -2).reshape(*weights.shape[:-1], -1)


def group_partial(weight, activation):
    return lax.dot_general(
        weight, activation, (((0,), (0,)), ((), ())), preferred_element_type=jnp.float32
    ).astype(jnp.bfloat16)


def gather_strips(values, axis):
    devices = lax.axis_size(axis)
    pieces = [values]
    for shift in range(1, devices):
        pairs = [(i, (i + shift) % devices) for i in range(devices)]
        pieces.append(lax.ppermute(values, axis, pairs))
    return jnp.concatenate(pieces, axis=-1)


def make_fold(queries, pieces):
    key_part, value_part = pieces
    scores = (
        jnp.einsum("hdri,phdrj->hripj", queries, key_part, preferred_element_type=jnp.float32)
        * attention_scale
    )
    weights = jnp.exp(scores)
    numerator = jnp.einsum(
        "hripj,phdrj->hdri",
        weights.astype(jnp.bfloat16),
        value_part,
        preferred_element_type=jnp.float32,
    )
    return (numerator, jnp.sum(weights, axis=(3, 4)))


def block_apply(state, block_index, tap_weights, block_gain, up_weight, down_weight, last):
    lat_rows = state.shape[1]
    out_cols = state.shape[2] - 2
    secants = secant_rows(lat_rows)[None, :, None]
    padded = jnp.pad(state.astype(jnp.float32), ((0, 0), (1, 1), (0, 0)))
    stencil_sum = jnp.zeros((state.shape[0], lat_rows, out_cols), jnp.float32)
    for row_step in (-1, 0, 1):
        for col_step in (-1, 0, 1):
            shifted = padded[
                :, 1 + row_step : 1 + row_step + lat_rows, 1 + col_step : 1 + col_step + out_cols
            ]
            tap_row = tap_weights[3 * (row_step + 1) + col_step + 1][:, None, None]
            if col_step != 0:
                stencil_sum = stencil_sum + tap_row * secants * shifted
            else:
                stencil_sum = stencil_sum + tap_row * shifted
    smoothed = stencil_sum.astype(jnp.bfloat16)
    full_channels = gather_half(smoothed)
    block_normed = norm_channels(full_channels.astype(jnp.float32), block_gain[block_index]).astype(
        jnp.bfloat16
    )
    block_normed = block_normed.reshape(full_channels.shape[0], -1)
    hidden = jax.nn.gelu(
        jnp.dot(up_weight[block_index], block_normed, preferred_element_type=jnp.float32)
    ).astype(jnp.bfloat16)
    partial = group_partial(down_weight[block_index], hidden)
    center = state[:, :, 1:-1]
    if last:
        chips = lax.axis_size("lev") // 2
        chip = lax.axis_index("lev") // 2
        center = jnp.take(center.reshape(chips, -1, *center.shape[1:]), chip, axis=0)
        update = scatter_sum(partial, "lev")
    else:
        update = reduce_half(partial)
    return (center.astype(jnp.float32) + update.reshape(center.shape)).astype(jnp.bfloat16)


def edges(values, width):
    return jnp.concatenate([values[..., :width], values[..., -width:]], axis=-1)


def per_device(
    latent, att_gain, qkv_weight, out_weight, stencil_weight, block_gain, up_weight, down_weight
):
    ch_local, lat_rows, columns = latent.shape
    head_size = C // H
    heads_local = qkv_weight.shape[1] // head_size
    reach = BLOCKS
    gathered = gather_channels(latent)
    taps = half_weights(stencil_weight)
    own_latent = core_half(gathered)
    normed = norm_channels(gathered.astype(jnp.float32), att_gain).astype(jnp.bfloat16)
    projected = jnp.einsum("koc,crw->korw", qkv_weight, normed, preferred_element_type=jnp.float32)
    projected = projected.reshape(3, heads_local, head_size, lat_rows, columns)
    queries = unit_heads(projected[0]).astype(jnp.bfloat16)
    key_rows = unit_heads(projected[1]).astype(jnp.bfloat16)
    value_rows = projected[2].astype(jnp.bfloat16)

    key_value = jnp.stack([key_rows, value_rows]).reshape(-1, lat_rows, columns)
    rim = jnp.concatenate([edges(queries.reshape(ch_local, lat_rows, columns), reach), edges(own_latent, reach)])
    rim_rows = rim.size // (lat_rows * columns)
    payload = jnp.concatenate([key_value, rim.reshape(rim_rows, lat_rows, columns)], axis=0)
    strips = lax.axis_size("lon")
    pieces = [key_value]
    from_left = from_right = None
    for shift in range(1, strips):
        pairs = [(i, (i + shift) % strips) for i in range(strips)]
        sent = payload if shift in (1, strips - 1) else key_value
        got = lax.ppermute(sent, "lon", pairs)
        pieces.append(got[: key_value.shape[0]])
        if shift == 1:
            from_left = got[key_value.shape[0] :].reshape(rim.shape)[..., reach:]
        if shift == strips - 1:
            from_right = got[key_value.shape[0] :].reshape(rim.shape)[..., :reach]
    all_keys = jnp.stack(pieces).reshape(strips, 2, heads_local, head_size, lat_rows, columns)
    wide_queries = jnp.concatenate(
        [from_left[:ch_local], queries.reshape(ch_local, lat_rows, columns), from_right[:ch_local]], axis=-1
    ).reshape(heads_local, head_size, lat_rows, -1)
    wide_latent = jnp.concatenate([from_left[ch_local:], own_latent, from_right[ch_local:]], axis=-1)

    numerator, denominator = make_fold(wide_queries, (all_keys[:, 0], all_keys[:, 1]))
    attended = (numerator / denominator[:, None]).astype(jnp.bfloat16)
    update = reduce_half(group_partial(out_weight, attended.reshape(ch_local, -1)))
    current = (wide_latent.astype(jnp.float32) + update.reshape(wide_latent.shape)).astype(
        jnp.bfloat16
    )
    for block_index in range(BLOCKS):
        current = block_apply(
            current, block_index, taps[block_index], block_gain, up_weight, down_weight,
            block_index == BLOCKS - 1,
        )
    return current


def solution(mesh):
    placed = (
        P("lev", "member", "lon"),
        P(),
        P(None, "lev", None),
        P("lev", None),
        P(None, None, "lev"),
        P(),
        P(None, "lev", None),
        P(None, "lev", None),
    )
    return jax.shard_map(
        per_device, mesh=mesh, in_specs=placed, out_specs=P("lev", "member", "lon"), check_vma=False
    )
```

```python
import math

import jax
import jax.numpy as jnp
from jax import lax
from jax.sharding import PartitionSpec as P

C = 512
H = 8
BLOCKS = 2


attention_scale = 24.0
band_start = 30.0
grid_step = 0.25
epsilon = 1e-06


def secant_rows(count):
    rows = jnp.arange(count).astype(jnp.float32)
    return 1.0 / jnp.cos((band_start + grid_step * rows) * (math.pi / 180.0))


def norm_channels(values, gain):
    scale = lax.rsqrt(jnp.mean(values * values, axis=0, keepdims=True) + epsilon)
    return values * scale * gain[:, None, None]


def unit_heads(values):
    return values * lax.rsqrt(jnp.sum(values * values, axis=1, keepdims=True) + epsilon)


def gather_channels(values):
    return lax.all_gather(values, "lev", axis=0, tiled=True)


def scatter_sum(weight, activation, axis):
    devices = lax.axis_size(axis)
    me = lax.axis_index(axis)
    chips, core = devices // 2, me % 2
    chip = me // 2
    grouped = weight.reshape(weight.shape[0], chips, 2, -1)

    def part(which):
        columns = jnp.take(grouped, which, axis=2).reshape(weight.shape[0], -1)
        product = jnp.dot(columns.T, activation, preferred_element_type=jnp.float32)
        return product.astype(jnp.bfloat16).reshape(chips, -1, activation.shape[1])

    mine = part(core).astype(jnp.float32)
    theirs = part(1 - core)
    pair = mine + lax.ppermute(theirs, axis, [(i, i ^ 1) for i in range(devices)]).astype(jnp.float32)
    total = jnp.take(pair, chip, axis=0)
    for shift in range(1, chips):
        pairs = [(i, ((i // 2 + shift) % chips) * 2 + i % 2) for i in range(devices)]
        sent = jnp.take(pair, (chip + shift) % chips, axis=0).astype(jnp.bfloat16)
        total = total + lax.ppermute(sent, axis, pairs).astype(jnp.float32)
    return total


def spread_sum(weight, activation):
    return scatter_sum(weight, activation, "lev")


def gather_strips(values, axis):
    devices = lax.axis_size(axis)
    pieces = [values]
    for shift in range(1, devices):
        pairs = [(i, (i + shift) % devices) for i in range(devices)]
        pieces.append(lax.ppermute(values, axis, pairs))
    return jnp.concatenate(pieces, axis=-1)


def make_fold(queries, pieces):
    key_part, value_part = pieces
    scores = (
        jnp.einsum("hdri,phdrj->hripj", queries, key_part, preferred_element_type=jnp.float32)
        * attention_scale
    )
    weights = jnp.exp(scores)
    numerator = jnp.einsum(
        "hripj,phdrj->hdri",
        weights.astype(jnp.bfloat16),
        value_part,
        preferred_element_type=jnp.float32,
    )
    return (numerator, jnp.sum(weights, axis=(3, 4)))


def block_apply(state, block_index, stencil_weight, block_gain, up_weight, down_weight):
    lat_rows = state.shape[1]
    out_cols = state.shape[2] - 2
    secants = secant_rows(lat_rows)[None, :, None]
    padded = jnp.pad(state.astype(jnp.float32), ((0, 0), (1, 1), (0, 0)))
    tap_weights = stencil_weight[block_index]
    stencil_sum = jnp.zeros((state.shape[0], lat_rows, out_cols), jnp.float32)
    for row_step in (-1, 0, 1):
        for col_step in (-1, 0, 1):
            shifted = padded[
                :, 1 + row_step : 1 + row_step + lat_rows, 1 + col_step : 1 + col_step + out_cols
            ]
            tap_row = tap_weights[3 * (row_step + 1) + col_step + 1][:, None, None]
            if col_step != 0:
                stencil_sum = stencil_sum + tap_row * secants * shifted
            else:
                stencil_sum = stencil_sum + tap_row * shifted
    smoothed = stencil_sum.astype(jnp.bfloat16)
    full_channels = gather_channels(smoothed)
    block_normed = norm_channels(full_channels.astype(jnp.float32), block_gain[block_index]).astype(
        jnp.bfloat16
    )
    block_normed = block_normed.reshape(full_channels.shape[0], -1)
    hidden = jax.nn.gelu(
        jnp.dot(up_weight[block_index], block_normed, preferred_element_type=jnp.float32)
    ).astype(jnp.bfloat16)
    update = spread_sum(down_weight[block_index], hidden)
    center = state[:, :, 1:-1]
    return (center.astype(jnp.float32) + update.reshape(center.shape)).astype(jnp.bfloat16)


def edges(values, width):
    return jnp.concatenate([values[..., :width], values[..., -width:]], axis=-1)


def per_device(
    latent, att_gain, qkv_weight, out_weight, stencil_weight, block_gain, up_weight, down_weight
):
    ch_local, lat_rows, columns = latent.shape
    head_size = C // H
    heads_local = qkv_weight.shape[1] // head_size
    reach = BLOCKS
    wide_source, latent = lax.optimization_barrier((latent.astype(jnp.float32), latent))
    gathered = gather_channels(latent)
    normed = norm_channels(gathered.astype(jnp.float32), att_gain).astype(jnp.bfloat16)
    projected = jnp.einsum("koc,crw->korw", qkv_weight, normed, preferred_element_type=jnp.float32)
    projected = projected.reshape(3, heads_local, head_size, lat_rows, columns)
    queries = unit_heads(projected[0]).astype(jnp.bfloat16)
    key_rows = unit_heads(projected[1]).astype(jnp.bfloat16)
    value_rows = projected[2].astype(jnp.bfloat16)

    key_value = jnp.stack([key_rows, value_rows]).reshape(-1, lat_rows, columns)
    rim = jnp.stack(
        [edges(queries.reshape(ch_local, lat_rows, columns), reach), edges(wide_source, reach).astype(jnp.bfloat16)]
    )
    rim_rows = rim.size // (lat_rows * columns)
    payload = jnp.concatenate([key_value, rim.reshape(rim_rows, lat_rows, columns)], axis=0)
    strips = lax.axis_size("lon")
    pieces = [key_value]
    from_left = from_right = None
    for shift in range(1, strips):
        pairs = [(i, (i + shift) % strips) for i in range(strips)]
        sent = payload if shift in (1, strips - 1) else key_value
        got = lax.ppermute(sent, "lon", pairs)
        pieces.append(got[: key_value.shape[0]])
        if shift == 1:
            from_left = got[key_value.shape[0] :].reshape(rim.shape)[..., reach:]
        if shift == strips - 1:
            from_right = got[key_value.shape[0] :].reshape(rim.shape)[..., :reach]
    all_keys = jnp.stack(pieces).reshape(strips, 2, heads_local, head_size, lat_rows, columns)
    wide_queries = jnp.concatenate(
        [from_left[0], queries.reshape(ch_local, lat_rows, columns), from_right[0]], axis=-1
    ).reshape(heads_local, head_size, lat_rows, -1)
    wide_latent = jnp.concatenate(
        [from_left[1].astype(jnp.float32), wide_source, from_right[1].astype(jnp.float32)], axis=-1
    )

    numerator, denominator = make_fold(wide_queries, (all_keys[:, 0], all_keys[:, 1]))
    attended = (numerator / denominator[:, None]).astype(jnp.bfloat16)
    update = spread_sum(out_weight, attended.reshape(ch_local, -1))
    current = (wide_latent.astype(jnp.float32) + update.reshape(wide_latent.shape)).astype(
        jnp.bfloat16
    )
    for block_index in range(BLOCKS):
        current = block_apply(
            current, block_index, stencil_weight, block_gain, up_weight, down_weight
        )
    return current


def solution(mesh):
    placed = (
        P("lev", "member", "lon"),
        P(),
        P(None, "lev", None),
        P("lev", None),
        P(None, None, "lev"),
        P(),
        P(None, "lev", None),
        P(None, "lev", None),
    )
    return jax.shard_map(
        per_device, mesh=mesh, in_specs=placed, out_specs=P("lev", "member", "lon"), check_vma=False
    )
```

```python
import math

import jax
import jax.numpy as jnp
from jax import lax
from jax.sharding import PartitionSpec as P

C = 512
H = 8
BLOCKS = 2


attention_scale = 24.0
band_start = 30.0
grid_step = 0.25
epsilon = 1e-06


def secant_rows(count):
    rows = jnp.arange(count).astype(jnp.float32)
    return 1.0 / jnp.cos((band_start + grid_step * rows) * (math.pi / 180.0))


def norm_channels(values, gain):
    scale = lax.rsqrt(jnp.mean(values * values, axis=0, keepdims=True) + epsilon)
    return values * scale * gain[:, None, None]


def unit_heads(values):
    return values * lax.rsqrt(jnp.sum(values * values, axis=1, keepdims=True) + epsilon)


def gather_channels(values):
    return lax.all_gather(values, "lev", axis=0, tiled=True)


def scatter_sum(partial, axis):
    devices = lax.axis_size(axis)
    me = lax.axis_index(axis)
    chips, core = devices // 2, me % 2
    chip = me // 2
    blocks = partial.reshape(chips, 2, -1, *partial.shape[1:])
    mine = jnp.take(blocks, core, axis=1).astype(jnp.float32)
    theirs = jnp.take(blocks, 1 - core, axis=1)
    pair = mine + lax.ppermute(theirs, axis, [(i, i ^ 1) for i in range(devices)]).astype(jnp.float32)
    total = jnp.take(pair, chip, axis=0)
    for shift in range(1, chips):
        pairs = [(i, ((i // 2 + shift) % chips) * 2 + i % 2) for i in range(devices)]
        sent = jnp.take(pair, (chip + shift) % chips, axis=0).astype(jnp.bfloat16)
        total = total + lax.ppermute(sent, axis, pairs).astype(jnp.float32)
    return total


def core_half(values, axis=0):
    devices = lax.axis_size("lev")
    grouped = values.reshape(*values.shape[:axis], devices // 2, 2, -1, *values.shape[axis + 1 :])
    taken = jnp.take(grouped, lax.axis_index("lev") % 2, axis=axis + 1)
    return taken.reshape(*values.shape[:axis], -1, *values.shape[axis + 1 :])


def reduce_half(partial):
    devices = lax.axis_size("lev")
    me = lax.axis_index("lev")
    chips, core = devices // 2, me % 2
    blocks = partial.reshape(chips, 2, -1, *partial.shape[1:])
    mine = jnp.take(blocks, core, axis=1).astype(jnp.float32)
    theirs = jnp.take(blocks, 1 - core, axis=1)
    pair = mine + lax.ppermute(theirs, "lev", [(i, i ^ 1) for i in range(devices)]).astype(jnp.float32)
    pair = pair.astype(jnp.bfloat16)
    total = pair.astype(jnp.float32)
    for shift in range(1, chips):
        pairs = [(i, ((i // 2 + shift) % chips) * 2 + i % 2) for i in range(devices)]
        total = total + lax.ppermute(pair, "lev", pairs).astype(jnp.float32)
    return total.reshape(-1, *partial.shape[1:])


def gather_half(values):
    devices = lax.axis_size("lev")
    theirs = lax.ppermute(values, "lev", [(i, i ^ 1) for i in range(devices)])
    return jnp.concatenate([values, theirs], axis=0)


def mine_first(values, axis):
    devices = lax.axis_size("lev")
    grouped = values.reshape(*values.shape[:axis], devices // 2, 2, -1, *values.shape[axis + 1 :])
    swapped = jnp.flip(grouped, axis=axis + 1)
    chosen = jnp.where(lax.axis_index("lev") % 2 == 0, grouped, swapped)
    return jnp.moveaxis(chosen, axis + 1, axis).reshape(values.shape)


def half_weights(weights):
    devices = lax.axis_size("lev")
    chips = devices // 2
    chip = lax.axis_index("lev") // 2
    stacked = [weights]
    for shift in range(1, chips):
        pairs = [(i, ((i // 2 - shift) % chips) * 2 + i % 2) for i in range(devices)]
        stacked.append(lax.ppermute(weights, "lev", pairs))
    ordered = jnp.roll(jnp.stack(stacked), chip, axis=0)
    return jnp.moveaxis(ordered, 0, -2).reshape(*weights.shape[:-1], -1)


def group_partial(weight, activation):
    return lax.dot_general(
        weight, activation, (((0,), (0,)), ((), ())), preferred_element_type=jnp.float32
    ).astype(jnp.bfloat16)


def gather_strips(values, axis):
    devices = lax.axis_size(axis)
    pieces = [values]
    for shift in range(1, devices):
        pairs = [(i, (i + shift) % devices) for i in range(devices)]
        pieces.append(lax.ppermute(values, axis, pairs))
    return jnp.concatenate(pieces, axis=-1)


def make_fold(queries, pieces):
    key_part, value_part = pieces
    scores = (
        jnp.einsum("hdri,phdrj->hripj", queries, key_part, preferred_element_type=jnp.float32)
        * attention_scale
    )
    weights = jnp.exp(scores)
    numerator = jnp.einsum(
        "hripj,phdrj->hdri",
        weights.astype(jnp.bfloat16),
        value_part,
        preferred_element_type=jnp.float32,
    )
    return (numerator, jnp.sum(weights, axis=(3, 4)))


def block_apply(state, block_index, tap_weights, block_gain, up_weight, down_weight, last):
    lat_rows = state.shape[1]
    out_cols = state.shape[2] - 2
    secants = secant_rows(lat_rows)[None, :, None]
    padded = jnp.pad(state.astype(jnp.float32), ((0, 0), (1, 1), (0, 0)))
    stencil_sum = jnp.zeros((state.shape[0], lat_rows, out_cols), jnp.float32)
    for row_step in (-1, 0, 1):
        for col_step in (-1, 0, 1):
            shifted = padded[
                :, 1 + row_step : 1 + row_step + lat_rows, 1 + col_step : 1 + col_step + out_cols
            ]
            tap_row = tap_weights[3 * (row_step + 1) + col_step + 1][:, None, None]
            if col_step != 0:
                stencil_sum = stencil_sum + tap_row * secants * shifted
            else:
                stencil_sum = stencil_sum + tap_row * shifted
    smoothed = stencil_sum.astype(jnp.bfloat16)
    full_channels = gather_half(smoothed)
    gain = mine_first(block_gain[block_index], 0)
    block_normed = norm_channels(full_channels.astype(jnp.float32), gain).astype(jnp.bfloat16)
    block_normed = block_normed.reshape(full_channels.shape[0], -1)
    hidden = jax.nn.gelu(
        jnp.dot(mine_first(up_weight[block_index], 1), block_normed, preferred_element_type=jnp.float32)
    ).astype(jnp.bfloat16)
    partial = group_partial(down_weight[block_index], hidden)
    center = state[:, :, 1:-1]
    if last:
        chips = lax.axis_size("lev") // 2
        chip = lax.axis_index("lev") // 2
        center = jnp.take(center.reshape(chips, -1, *center.shape[1:]), chip, axis=0)
        update = scatter_sum(partial, "lev")
    else:
        update = reduce_half(partial)
    return (center.astype(jnp.float32) + update.reshape(center.shape)).astype(jnp.bfloat16)


def edges(values, width):
    return jnp.concatenate([values[..., :width], values[..., -width:]], axis=-1)


def per_device(
    latent, att_gain, qkv_weight, out_weight, stencil_weight, block_gain, up_weight, down_weight
):
    ch_local, lat_rows, columns = latent.shape
    head_size = C // H
    heads_local = qkv_weight.shape[1] // head_size
    reach = BLOCKS
    gathered = gather_channels(latent)
    taps = half_weights(stencil_weight)
    own_latent = core_half(gathered)
    normed = norm_channels(gathered.astype(jnp.float32), att_gain).astype(jnp.bfloat16)
    projected = jnp.einsum("koc,crw->korw", qkv_weight, normed, preferred_element_type=jnp.float32)
    projected = projected.reshape(3, heads_local, head_size, lat_rows, columns)
    queries = unit_heads(projected[0]).astype(jnp.bfloat16)
    key_rows = unit_heads(projected[1]).astype(jnp.bfloat16)
    value_rows = projected[2].astype(jnp.bfloat16)

    key_value = jnp.stack([key_rows, value_rows]).reshape(-1, lat_rows, columns)
    rim = jnp.concatenate([edges(queries.reshape(ch_local, lat_rows, columns), reach), edges(own_latent, reach)])
    rim_rows = rim.size // (lat_rows * columns)
    payload = jnp.concatenate([key_value, rim.reshape(rim_rows, lat_rows, columns)], axis=0)
    strips = lax.axis_size("lon")
    pieces = [key_value]
    from_left = from_right = None
    for shift in range(1, strips):
        pairs = [(i, (i + shift) % strips) for i in range(strips)]
        sent = payload if shift in (1, strips - 1) else key_value
        got = lax.ppermute(sent, "lon", pairs)
        pieces.append(got[: key_value.shape[0]])
        if shift == 1:
            from_left = got[key_value.shape[0] :].reshape(rim.shape)[..., reach:]
        if shift == strips - 1:
            from_right = got[key_value.shape[0] :].reshape(rim.shape)[..., :reach]
    all_keys = jnp.stack(pieces).reshape(strips, 2, heads_local, head_size, lat_rows, columns)
    wide_queries = jnp.concatenate(
        [from_left[:ch_local], queries.reshape(ch_local, lat_rows, columns), from_right[:ch_local]], axis=-1
    ).reshape(heads_local, head_size, lat_rows, -1)
    wide_latent = jnp.concatenate([from_left[ch_local:], own_latent, from_right[ch_local:]], axis=-1)

    numerator, denominator = make_fold(wide_queries, (all_keys[:, 0], all_keys[:, 1]))
    attended = (numerator / denominator[:, None]).astype(jnp.bfloat16)
    update = reduce_half(group_partial(out_weight, attended.reshape(ch_local, -1)))
    current = (wide_latent.astype(jnp.float32) + update.reshape(wide_latent.shape)).astype(
        jnp.bfloat16
    )
    for block_index in range(BLOCKS):
        current = block_apply(
            current, block_index, taps[block_index], block_gain, up_weight, down_weight,
            block_index == BLOCKS - 1,
        )
    return current


def solution(mesh):
    placed = (
        P("lev", "member", "lon"),
        P(),
        P(None, "lev", None),
        P("lev", None),
        P(None, None, "lev"),
        P(),
        P(None, "lev", None),
        P(None, "lev", None),
    )
    return jax.shard_map(
        per_device, mesh=mesh, in_specs=placed, out_specs=P("lev", "member", "lon"), check_vma=False
    )
```

```python
import math

import jax
import jax.numpy as jnp
from jax import lax
from jax.sharding import PartitionSpec as P

C = 512
H = 8
BLOCKS = 2


attention_scale = 24.0
band_start = 30.0
grid_step = 0.25
epsilon = 1e-06


def secant_rows(count):
    rows = jnp.arange(count).astype(jnp.float32)
    return 1.0 / jnp.cos((band_start + grid_step * rows) * (math.pi / 180.0))


def norm_channels(values, gain):
    scale = lax.rsqrt(jnp.mean(values * values, axis=0, keepdims=True) + epsilon)
    return values * scale * gain[:, None, None]


def unit_heads(values):
    return values * lax.rsqrt(jnp.sum(values * values, axis=1, keepdims=True) + epsilon)


def gather_channels(values):
    return lax.all_gather(values, "lev", axis=0, tiled=True)


def scatter_sum(partial, axis):
    devices = lax.axis_size(axis)
    me = lax.axis_index(axis)
    chips, core = devices // 2, me % 2
    chip = me // 2
    blocks = partial.reshape(chips, 2, -1, *partial.shape[1:])
    mine = jnp.take(blocks, core, axis=1).astype(jnp.float32)
    theirs = jnp.take(blocks, 1 - core, axis=1)
    pair = mine + lax.ppermute(theirs, axis, [(i, i ^ 1) for i in range(devices)]).astype(jnp.float32)
    total = jnp.take(pair, chip, axis=0)
    for shift in range(1, chips):
        pairs = [(i, ((i // 2 + shift) % chips) * 2 + i % 2) for i in range(devices)]
        sent = jnp.take(pair, (chip + shift) % chips, axis=0).astype(jnp.bfloat16)
        total = total + lax.ppermute(sent, axis, pairs).astype(jnp.float32)
    return total


def core_half(values, axis=0):
    devices = lax.axis_size("lev")
    grouped = values.reshape(*values.shape[:axis], devices // 2, 2, -1, *values.shape[axis + 1 :])
    taken = jnp.take(grouped, lax.axis_index("lev") % 2, axis=axis + 1)
    return taken.reshape(*values.shape[:axis], -1, *values.shape[axis + 1 :])


def reduce_half(partial):
    devices = lax.axis_size("lev")
    me = lax.axis_index("lev")
    chips, core = devices // 2, me % 2
    blocks = partial.reshape(chips, 2, -1, *partial.shape[1:])
    mine = jnp.take(blocks, core, axis=1).astype(jnp.float32)
    theirs = jnp.take(blocks, 1 - core, axis=1)
    pair = mine + lax.ppermute(theirs, "lev", [(i, i ^ 1) for i in range(devices)]).astype(jnp.float32)
    pair = pair.astype(jnp.bfloat16)
    total = pair.astype(jnp.float32)
    for shift in range(1, chips):
        pairs = [(i, ((i // 2 + shift) % chips) * 2 + i % 2) for i in range(devices)]
        total = total + lax.ppermute(pair, "lev", pairs).astype(jnp.float32)
    return total.reshape(-1, *partial.shape[1:])


def gather_half(values):
    devices = lax.axis_size("lev")
    theirs = lax.ppermute(values, "lev", [(i, i ^ 1) for i in range(devices)])
    return jnp.concatenate([values, theirs], axis=0)


def mine_first(values, axis):
    devices = lax.axis_size("lev")
    grouped = values.reshape(*values.shape[:axis], devices // 2, 2, -1, *values.shape[axis + 1 :])
    swapped = jnp.flip(grouped, axis=axis + 1)
    chosen = jnp.where(lax.axis_index("lev") % 2 == 0, grouped, swapped)
    return jnp.moveaxis(chosen, axis + 1, axis).reshape(values.shape)


def half_weights(weights):
    devices = lax.axis_size("lev")
    chips = devices // 2
    chip = lax.axis_index("lev") // 2
    stacked = [weights]
    for shift in range(1, chips):
        pairs = [(i, ((i // 2 - shift) % chips) * 2 + i % 2) for i in range(devices)]
        stacked.append(lax.ppermute(weights, "lev", pairs))
    ordered = jnp.roll(jnp.stack(stacked), chip, axis=0)
    return jnp.moveaxis(ordered, 0, -2).reshape(*weights.shape[:-1], -1)


def group_partial(weight, activation):
    return lax.dot_general(
        weight, activation, (((0,), (0,)), ((), ())), preferred_element_type=jnp.float32
    ).astype(jnp.bfloat16)


def gather_strips(values, axis):
    devices = lax.axis_size(axis)
    pieces = [values]
    for shift in range(1, devices):
        pairs = [(i, (i + shift) % devices) for i in range(devices)]
        pieces.append(lax.ppermute(values, axis, pairs))
    return jnp.concatenate(pieces, axis=-1)


def make_fold(queries, pieces):
    key_part, value_part = pieces
    scores = (
        jnp.einsum("hdri,phdrj->hripj", queries, key_part, preferred_element_type=jnp.float32)
        * attention_scale
    )
    weights = jnp.exp(scores)
    numerator = jnp.einsum(
        "hripj,phdrj->hdri",
        weights.astype(jnp.bfloat16),
        value_part,
        preferred_element_type=jnp.float32,
    )
    return (numerator, jnp.sum(weights, axis=(3, 4)))


def block_apply(state, block_index, tap_weights, block_gain, up_weight, down_weight, last):
    lat_rows = state.shape[1]
    out_cols = state.shape[2] - 2
    secants = secant_rows(lat_rows)[None, :, None]
    padded = jnp.pad(state.astype(jnp.float32), ((0, 0), (1, 1), (0, 0)))
    stencil_sum = jnp.zeros((state.shape[0], lat_rows, out_cols), jnp.float32)
    for row_step in (-1, 0, 1):
        for col_step in (-1, 0, 1):
            shifted = padded[
                :, 1 + row_step : 1 + row_step + lat_rows, 1 + col_step : 1 + col_step + out_cols
            ]
            tap_row = tap_weights[3 * (row_step + 1) + col_step + 1][:, None, None]
            if col_step != 0:
                stencil_sum = stencil_sum + tap_row * secants * shifted
            else:
                stencil_sum = stencil_sum + tap_row * shifted
    smoothed = stencil_sum.astype(jnp.bfloat16)
    full_channels = gather_half(smoothed)
    gain = mine_first(block_gain[block_index], 0)
    block_normed = norm_channels(full_channels.astype(jnp.float32), gain).astype(jnp.bfloat16)
    block_normed = block_normed.reshape(full_channels.shape[0], -1)
    hidden = jax.nn.gelu(
        jnp.dot(mine_first(up_weight[block_index], 1), block_normed, preferred_element_type=jnp.float32)
    ).astype(jnp.bfloat16)
    partial = group_partial(down_weight[block_index], hidden)
    center = state[:, :, 1:-1]
    if last:
        chips = lax.axis_size("lev") // 2
        chip = lax.axis_index("lev") // 2
        center = jnp.take(center.reshape(chips, -1, *center.shape[1:]), chip, axis=0)
        update = scatter_sum(partial, "lev")
    else:
        update = reduce_half(partial)
    return (center.astype(jnp.float32) + update.reshape(center.shape)).astype(jnp.bfloat16)


def edges(values, width):
    return jnp.concatenate([values[..., :width], values[..., -width:]], axis=-1)


def per_device(
    latent, att_gain, qkv_weight, out_weight, stencil_weight, block_gain, up_weight, down_weight
):
    ch_local, lat_rows, columns = latent.shape
    head_size = C // H
    heads_local = qkv_weight.shape[1] // head_size
    reach = BLOCKS
    gathered = gather_channels(latent)
    own_latent = core_half(gathered)
    normed = norm_channels(gathered.astype(jnp.float32), att_gain).astype(jnp.bfloat16)
    projected = jnp.einsum("koc,crw->korw", qkv_weight, normed, preferred_element_type=jnp.float32)
    projected = projected.reshape(3, heads_local, head_size, lat_rows, columns)
    queries = unit_heads(projected[0]).astype(jnp.bfloat16)
    key_rows = unit_heads(projected[1]).astype(jnp.bfloat16)
    value_rows = projected[2].astype(jnp.bfloat16)

    key_value = jnp.stack([key_rows, value_rows]).reshape(-1, lat_rows, columns)
    rim = jnp.concatenate([edges(queries.reshape(ch_local, lat_rows, columns), reach), edges(own_latent, reach)])
    rim_rows = rim.size // (lat_rows * columns)
    payload = jnp.concatenate([key_value, rim.reshape(rim_rows, lat_rows, columns)], axis=0)
    strips = lax.axis_size("lon")
    pieces = [key_value]
    from_left = from_right = None
    for shift in range(1, strips):
        pairs = [(i, (i + shift) % strips) for i in range(strips)]
        sent = payload if shift in (1, strips - 1) else key_value
        got = lax.ppermute(sent, "lon", pairs)
        pieces.append(got[: key_value.shape[0]])
        if shift == 1:
            from_left = got[key_value.shape[0] :].reshape(rim.shape)[..., reach:]
        if shift == strips - 1:
            from_right = got[key_value.shape[0] :].reshape(rim.shape)[..., :reach]
    taps = half_weights(lax.optimization_barrier((stencil_weight, pieces[-1]))[0])
    all_keys = jnp.stack(pieces).reshape(strips, 2, heads_local, head_size, lat_rows, columns)
    wide_queries = jnp.concatenate(
        [from_left[:ch_local], queries.reshape(ch_local, lat_rows, columns), from_right[:ch_local]], axis=-1
    ).reshape(heads_local, head_size, lat_rows, -1)
    wide_latent = jnp.concatenate([from_left[ch_local:], own_latent, from_right[ch_local:]], axis=-1)

    numerator, denominator = make_fold(wide_queries, (all_keys[:, 0], all_keys[:, 1]))
    attended = (numerator / denominator[:, None]).astype(jnp.bfloat16)
    update = reduce_half(group_partial(out_weight, attended.reshape(ch_local, -1)))
    current = (wide_latent.astype(jnp.float32) + update.reshape(wide_latent.shape)).astype(
        jnp.bfloat16
    )
    for block_index in range(BLOCKS):
        current = block_apply(
            current, block_index, taps[block_index], block_gain, up_weight, down_weight,
            block_index == BLOCKS - 1,
        )
    return current


def solution(mesh):
    placed = (
        P("lev", "member", "lon"),
        P(),
        P(None, "lev", None),
        P("lev", None),
        P(None, None, "lev"),
        P(),
        P(None, "lev", None),
        P(None, "lev", None),
    )
    return jax.shard_map(
        per_device, mesh=mesh, in_specs=placed, out_specs=P("lev", "member", "lon"), check_vma=False
    )
```

```python
import math

import jax
import jax.numpy as jnp
from jax import lax
from jax.sharding import PartitionSpec as P

C = 512
H = 8
BLOCKS = 2


attention_scale = 24.0
band_start = 30.0
grid_step = 0.25
epsilon = 1e-06


def secant_rows(count):
    rows = jnp.arange(count).astype(jnp.float32)
    return 1.0 / jnp.cos((band_start + grid_step * rows) * (math.pi / 180.0))


def norm_channels(values, gain):
    scale = lax.rsqrt(jnp.mean(values * values, axis=0, keepdims=True) + epsilon)
    return values * scale * gain[:, None, None]


def unit_heads(values):
    return values * lax.rsqrt(jnp.sum(values * values, axis=1, keepdims=True) + epsilon)


def gather_channels(values):
    return lax.all_gather(values, "lev", axis=0, tiled=True)


def scatter_sum(partial, axis):
    devices = lax.axis_size(axis)
    me = lax.axis_index(axis)
    chips, core = devices // 2, me % 2
    chip = me // 2
    blocks = partial.reshape(chips, 2, -1, *partial.shape[1:])
    mine = jnp.take(blocks, core, axis=1).astype(jnp.float32)
    theirs = jnp.take(blocks, 1 - core, axis=1)
    pair = mine + lax.ppermute(theirs, axis, [(i, i ^ 1) for i in range(devices)]).astype(jnp.float32)
    total = jnp.take(pair, chip, axis=0)
    for shift in range(1, chips):
        pairs = [(i, ((i // 2 + shift) % chips) * 2 + i % 2) for i in range(devices)]
        sent = jnp.take(pair, (chip + shift) % chips, axis=0).astype(jnp.bfloat16)
        total = total + lax.ppermute(sent, axis, pairs).astype(jnp.float32)
    return total


def core_half(values, axis=0):
    devices = lax.axis_size("lev")
    grouped = values.reshape(*values.shape[:axis], devices // 2, 2, -1, *values.shape[axis + 1 :])
    taken = jnp.take(grouped, lax.axis_index("lev") % 2, axis=axis + 1)
    return taken.reshape(*values.shape[:axis], -1, *values.shape[axis + 1 :])


def reduce_half(partial, extra=None):
    devices = lax.axis_size("lev")
    me = lax.axis_index("lev")
    chips, core = devices // 2, me % 2
    chip = me // 2
    blocks = partial.reshape(chips, 2, -1, *partial.shape[1:])
    mine = jnp.take(blocks, core, axis=1).astype(jnp.float32)
    theirs = jnp.take(blocks, 1 - core, axis=1)
    pair = mine + lax.ppermute(theirs, "lev", [(i, i ^ 1) for i in range(devices)]).astype(jnp.float32)
    pair = pair.astype(jnp.bfloat16).reshape(-1, *partial.shape[1:])
    total = pair.astype(jnp.float32)
    rows = pair.shape[0]
    sent = pair
    if extra is not None:
        width = partial.shape[1]
        flat = extra.reshape(-1)
        spare = (-flat.shape[0]) % width
        sent = jnp.concatenate([pair, jnp.pad(flat, (0, spare)).reshape(-1, width)], axis=0)
    extras = [extra]
    for shift in range(1, chips):
        pairs = [(i, ((i // 2 - shift) % chips) * 2 + i % 2) for i in range(devices)]
        got = lax.ppermute(sent, "lev", pairs)
        total = total + got[:rows].astype(jnp.float32)
        if extra is not None:
            extras.append(got[rows:].reshape(-1)[: extra.size].reshape(extra.shape))
    if extra is None:
        return total
    return total, jnp.roll(jnp.stack(extras), chip, axis=0)


def gather_half(values):
    devices = lax.axis_size("lev")
    theirs = lax.ppermute(values, "lev", [(i, i ^ 1) for i in range(devices)])
    return jnp.concatenate([values, theirs], axis=0)


def mine_first(values, axis):
    devices = lax.axis_size("lev")
    grouped = values.reshape(*values.shape[:axis], devices // 2, 2, -1, *values.shape[axis + 1 :])
    swapped = jnp.flip(grouped, axis=axis + 1)
    chosen = jnp.where(lax.axis_index("lev") % 2 == 0, grouped, swapped)
    return jnp.moveaxis(chosen, axis + 1, axis).reshape(values.shape)


def half_weights(weights):
    devices = lax.axis_size("lev")
    chips = devices // 2
    chip = lax.axis_index("lev") // 2
    stacked = [weights]
    for shift in range(1, chips):
        pairs = [(i, ((i // 2 - shift) % chips) * 2 + i % 2) for i in range(devices)]
        stacked.append(lax.ppermute(weights, "lev", pairs))
    ordered = jnp.roll(jnp.stack(stacked), chip, axis=0)
    return jnp.moveaxis(ordered, 0, -2).reshape(*weights.shape[:-1], -1)


def group_partial(weight, activation):
    return lax.dot_general(
        weight, activation, (((0,), (0,)), ((), ())), preferred_element_type=jnp.float32
    ).astype(jnp.bfloat16)


def gather_strips(values, axis):
    devices = lax.axis_size(axis)
    pieces = [values]
    for shift in range(1, devices):
        pairs = [(i, (i + shift) % devices) for i in range(devices)]
        pieces.append(lax.ppermute(values, axis, pairs))
    return jnp.concatenate(pieces, axis=-1)


def make_fold(queries, pieces):
    key_part, value_part = pieces
    scores = (
        jnp.einsum("hdri,phdrj->hripj", queries, key_part, preferred_element_type=jnp.float32)
        * attention_scale
    )
    weights = jnp.exp(scores)
    numerator = jnp.einsum(
        "hripj,phdrj->hdri",
        weights.astype(jnp.bfloat16),
        value_part,
        preferred_element_type=jnp.float32,
    )
    return (numerator, jnp.sum(weights, axis=(3, 4)))


def block_apply(state, block_index, tap_weights, block_gain, up_weight, down_weight, last):
    lat_rows = state.shape[1]
    out_cols = state.shape[2] - 2
    secants = secant_rows(lat_rows)[None, :, None]
    padded = jnp.pad(state.astype(jnp.float32), ((0, 0), (1, 1), (0, 0)))
    stencil_sum = jnp.zeros((state.shape[0], lat_rows, out_cols), jnp.float32)
    for row_step in (-1, 0, 1):
        for col_step in (-1, 0, 1):
            shifted = padded[
                :, 1 + row_step : 1 + row_step + lat_rows, 1 + col_step : 1 + col_step + out_cols
            ]
            tap_row = tap_weights[3 * (row_step + 1) + col_step + 1][:, None, None]
            if col_step != 0:
                stencil_sum = stencil_sum + tap_row * secants * shifted
            else:
                stencil_sum = stencil_sum + tap_row * shifted
    smoothed = stencil_sum.astype(jnp.bfloat16)
    full_channels = gather_half(smoothed)
    gain = mine_first(block_gain[block_index], 0)
    block_normed = norm_channels(full_channels.astype(jnp.float32), gain).astype(jnp.bfloat16)
    block_normed = block_normed.reshape(full_channels.shape[0], -1)
    hidden = jax.nn.gelu(
        jnp.dot(mine_first(up_weight[block_index], 1), block_normed, preferred_element_type=jnp.float32)
    ).astype(jnp.bfloat16)
    partial = group_partial(down_weight[block_index], hidden)
    center = state[:, :, 1:-1]
    if last:
        chips = lax.axis_size("lev") // 2
        chip = lax.axis_index("lev") // 2
        center = jnp.take(center.reshape(chips, -1, *center.shape[1:]), chip, axis=0)
        update = scatter_sum(partial, "lev")
    else:
        update = reduce_half(partial)
    return (center.astype(jnp.float32) + update.reshape(center.shape)).astype(jnp.bfloat16)


def edges(values, width):
    return jnp.concatenate([values[..., :width], values[..., -width:]], axis=-1)


def per_device(
    latent, att_gain, qkv_weight, out_weight, stencil_weight, block_gain, up_weight, down_weight
):
    ch_local, lat_rows, columns = latent.shape
    head_size = C // H
    heads_local = qkv_weight.shape[1] // head_size
    reach = BLOCKS
    gathered = gather_channels(latent)
    taps = half_weights(stencil_weight)
    own_latent = core_half(gathered)
    normed = norm_channels(gathered.astype(jnp.float32), att_gain).astype(jnp.bfloat16)
    projected = jnp.einsum("koc,crw->korw", qkv_weight, normed, preferred_element_type=jnp.float32)
    projected = projected.reshape(3, heads_local, head_size, lat_rows, columns)
    queries = unit_heads(projected[0]).astype(jnp.bfloat16)
    key_rows = unit_heads(projected[1]).astype(jnp.bfloat16)
    value_rows = projected[2].astype(jnp.bfloat16)

    key_value = jnp.stack([key_rows, value_rows]).reshape(-1, lat_rows, columns)
    rim = jnp.concatenate([edges(queries.reshape(ch_local, lat_rows, columns), reach), edges(latent, reach)])
    rim_rows = rim.size // (lat_rows * columns)
    payload = jnp.concatenate([key_value, rim.reshape(rim_rows, lat_rows, columns)], axis=0)
    strips = lax.axis_size("lon")
    pieces = [key_value]
    from_left = from_right = None
    for shift in range(1, strips):
        pairs = [(i, (i + shift) % strips) for i in range(strips)]
        sent = payload if shift in (1, strips - 1) else key_value
        got = lax.ppermute(sent, "lon", pairs)
        pieces.append(got[: key_value.shape[0]])
        if shift == 1:
            from_left = got[key_value.shape[0] :].reshape(rim.shape)[..., reach:]
        if shift == strips - 1:
            from_right = got[key_value.shape[0] :].reshape(rim.shape)[..., :reach]
    all_keys = jnp.stack(pieces).reshape(strips, 2, heads_local, head_size, lat_rows, columns)
    wide_queries = jnp.concatenate(
        [from_left[:ch_local], queries.reshape(ch_local, lat_rows, columns), from_right[:ch_local]], axis=-1
    ).reshape(heads_local, head_size, lat_rows, -1)

    numerator, denominator = make_fold(wide_queries, (all_keys[:, 0], all_keys[:, 1]))
    attended = (numerator / denominator[:, None]).astype(jnp.bfloat16)
    halo = jnp.stack([from_left[ch_local:], from_right[ch_local:]])
    update, halos = reduce_half(group_partial(out_weight, attended.reshape(ch_local, -1)), halo)
    halos = jnp.moveaxis(halos, 0, 1).reshape(2, -1, lat_rows, reach)
    wide_latent = jnp.concatenate([halos[0], own_latent, halos[1]], axis=-1)
    current = (wide_latent.astype(jnp.float32) + update.reshape(wide_latent.shape)).astype(
        jnp.bfloat16
    )
    for block_index in range(BLOCKS):
        current = block_apply(
            current, block_index, taps[block_index], block_gain, up_weight, down_weight,
            block_index == BLOCKS - 1,
        )
    return current


def solution(mesh):
    placed = (
        P("lev", "member", "lon"),
        P(),
        P(None, "lev", None),
        P("lev", None),
        P(None, None, "lev"),
        P(),
        P(None, "lev", None),
        P(None, "lev", None),
    )
    return jax.shard_map(
        per_device, mesh=mesh, in_specs=placed, out_specs=P("lev", "member", "lon"), check_vma=False
    )
```

```python
import math

import jax
import jax.numpy as jnp
from jax import lax
from jax.sharding import PartitionSpec as P

C = 512
H = 8
BLOCKS = 2


attention_scale = 24.0
band_start = 30.0
grid_step = 0.25
epsilon = 1e-06


def secant_rows(count):
    rows = jnp.arange(count).astype(jnp.float32)
    return 1.0 / jnp.cos((band_start + grid_step * rows) * (math.pi / 180.0))


def norm_channels(values, gain):
    scale = lax.rsqrt(jnp.mean(values * values, axis=0, keepdims=True) + epsilon)
    return values * scale * gain[:, None, None]


def unit_heads(values):
    return values * lax.rsqrt(jnp.sum(values * values, axis=1, keepdims=True) + epsilon)


def gather_channels(values):
    return lax.all_gather(values, "lev", axis=0, tiled=True)


def scatter_sum(partial, axis):
    devices = lax.axis_size(axis)
    me = lax.axis_index(axis)
    chips, core = devices // 2, me % 2
    chip = me // 2
    blocks = partial.reshape(chips, 2, -1, *partial.shape[1:])
    mine = jnp.take(blocks, core, axis=1).astype(jnp.float32)
    theirs = jnp.take(blocks, 1 - core, axis=1)
    pair = mine + lax.ppermute(theirs, axis, [(i, i ^ 1) for i in range(devices)]).astype(jnp.float32)
    total = jnp.take(pair, chip, axis=0)
    for shift in range(1, chips):
        pairs = [(i, ((i // 2 + shift) % chips) * 2 + i % 2) for i in range(devices)]
        sent = jnp.take(pair, (chip + shift) % chips, axis=0).astype(jnp.bfloat16)
        total = total + lax.ppermute(sent, axis, pairs).astype(jnp.float32)
    return total


def spread_sum(weight, activation):
    partial = lax.dot_general(
        weight, activation, (((0,), (0,)), ((), ())), preferred_element_type=jnp.float32
    ).astype(jnp.bfloat16)
    return scatter_sum(partial, "lev")


def gather_strips(values, axis):
    devices = lax.axis_size(axis)
    pieces = [values]
    for shift in range(1, devices):
        pairs = [(i, (i + shift) % devices) for i in range(devices)]
        pieces.append(lax.ppermute(values, axis, pairs))
    return jnp.concatenate(pieces, axis=-1)


def make_fold(queries, pieces):
    key_part, value_part = pieces
    scores = (
        jnp.einsum("hdri,phdrj->hripj", queries, key_part, preferred_element_type=jnp.float32)
        * attention_scale
    )
    weights = jnp.exp(scores)
    numerator = jnp.einsum(
        "hripj,phdrj->hdri",
        weights.astype(jnp.bfloat16),
        value_part,
        preferred_element_type=jnp.float32,
    )
    return (numerator, jnp.sum(weights, axis=(3, 4)))


def block_apply(state, block_index, stencil_weight, block_gain, up_weight, down_weight):
    lat_rows = state.shape[1]
    out_cols = state.shape[2] - 2
    secants = secant_rows(lat_rows)[None, :, None]
    padded = jnp.pad(state.astype(jnp.float32), ((0, 0), (1, 1), (0, 0)))
    tap_weights = stencil_weight[block_index]
    stencil_sum = jnp.zeros((state.shape[0], lat_rows, out_cols), jnp.float32)
    for row_step in (-1, 0, 1):
        for col_step in (-1, 0, 1):
            shifted = padded[
                :, 1 + row_step : 1 + row_step + lat_rows, 1 + col_step : 1 + col_step + out_cols
            ]
            tap_row = tap_weights[3 * (row_step + 1) + col_step + 1][:, None, None]
            if col_step != 0:
                stencil_sum = stencil_sum + tap_row * secants * shifted
            else:
                stencil_sum = stencil_sum + tap_row * shifted
    smoothed = stencil_sum.astype(jnp.bfloat16)
    full_channels = gather_channels(smoothed)
    block_normed = norm_channels(full_channels.astype(jnp.float32), block_gain[block_index]).astype(
        jnp.bfloat16
    )
    block_normed = block_normed.reshape(full_channels.shape[0], -1)
    hidden = jax.nn.gelu(
        jnp.dot(up_weight[block_index], block_normed, preferred_element_type=jnp.float32)
    ).astype(jnp.bfloat16)
    update = spread_sum(down_weight[block_index], hidden)
    center = state[:, :, 1:-1]
    return (center.astype(jnp.float32) + update.reshape(center.shape)).astype(jnp.bfloat16)


def edges(values, width):
    return jnp.concatenate([values[..., :width], values[..., -width:]], axis=-1)


def per_device(
    latent, att_gain, qkv_weight, out_weight, stencil_weight, block_gain, up_weight, down_weight
):
    ch_local, lat_rows, columns = latent.shape
    head_size = C // H
    heads_local = qkv_weight.shape[1] // head_size
    reach = BLOCKS
    latent_rim, latent = lax.optimization_barrier((edges(latent, reach), latent))
    gathered = gather_channels(latent)
    normed = norm_channels(gathered.astype(jnp.float32), att_gain).astype(jnp.bfloat16)
    projected = jnp.einsum("koc,crw->korw", qkv_weight, normed, preferred_element_type=jnp.float32)
    projected = projected.reshape(3, heads_local, head_size, lat_rows, columns)
    queries = unit_heads(projected[0]).astype(jnp.bfloat16)
    key_rows = unit_heads(projected[1]).astype(jnp.bfloat16)
    value_rows = projected[2].astype(jnp.bfloat16)

    key_value = jnp.stack([key_rows, value_rows]).reshape(-1, lat_rows, columns)
    rim = jnp.stack([edges(queries.reshape(ch_local, lat_rows, columns), reach), latent_rim])
    rim_rows = rim.size // (lat_rows * columns)
    payload = jnp.concatenate([key_value, rim.reshape(rim_rows, lat_rows, columns)], axis=0)
    strips = lax.axis_size("lon")
    pieces = [key_value]
    from_left = from_right = None
    for shift in range(1, strips):
        pairs = [(i, (i + shift) % strips) for i in range(strips)]
        sent = payload if shift in (1, strips - 1) else key_value
        got = lax.ppermute(sent, "lon", pairs)
        pieces.append(got[: key_value.shape[0]])
        if shift == 1:
            from_left = got[key_value.shape[0] :].reshape(rim.shape)[..., reach:]
        if shift == strips - 1:
            from_right = got[key_value.shape[0] :].reshape(rim.shape)[..., :reach]
    all_keys = jnp.stack(pieces).reshape(strips, 2, heads_local, head_size, lat_rows, columns)
    wide_queries = jnp.concatenate(
        [from_left[0], queries.reshape(ch_local, lat_rows, columns), from_right[0]], axis=-1
    ).reshape(heads_local, head_size, lat_rows, -1)
    wide_latent = jnp.concatenate([from_left[1], latent, from_right[1]], axis=-1)

    numerator, denominator = make_fold(wide_queries, (all_keys[:, 0], all_keys[:, 1]))
    attended = (numerator / denominator[:, None]).astype(jnp.bfloat16)
    update = spread_sum(out_weight, attended.reshape(ch_local, -1))
    current = (wide_latent.astype(jnp.float32) + update.reshape(wide_latent.shape)).astype(
        jnp.bfloat16
    )
    for block_index in range(BLOCKS):
        current = block_apply(
            current, block_index, stencil_weight, block_gain, up_weight, down_weight
        )
    return current


def solution(mesh):
    placed = (
        P("lev", "member", "lon"),
        P(),
        P(None, "lev", None),
        P("lev", None),
        P(None, None, "lev"),
        P(),
        P(None, "lev", None),
        P(None, "lev", None),
    )
    return jax.shard_map(
        per_device, mesh=mesh, in_specs=placed, out_specs=P("lev", "member", "lon"), check_vma=False
    )
```

```python
import math

import jax
import jax.numpy as jnp
from jax import lax
from jax.sharding import PartitionSpec as P

C = 512
H = 8
BLOCKS = 2


attention_scale = 24.0
band_start = 30.0
grid_step = 0.25
epsilon = 1e-06


def secant_rows(count):
    rows = jnp.arange(count).astype(jnp.float32)
    return 1.0 / jnp.cos((band_start + grid_step * rows) * (math.pi / 180.0))


def norm_channels(values, gain):
    scale = lax.rsqrt(jnp.mean(values * values, axis=0, keepdims=True) + epsilon)
    return values * scale * gain[:, None, None]


def unit_heads(values):
    return values * lax.rsqrt(jnp.sum(values * values, axis=1, keepdims=True) + epsilon)


def gather_channels(values):
    return lax.all_gather(values, "lev", axis=0, tiled=True)


def scatter_sum(partial, axis):
    devices = lax.axis_size(axis)
    me = lax.axis_index(axis)
    chips, core = devices // 2, me % 2
    chip = me // 2
    blocks = partial.reshape(chips, 2, -1, *partial.shape[1:])
    mine = jnp.take(blocks, core, axis=1).astype(jnp.float32)
    theirs = jnp.take(blocks, 1 - core, axis=1)
    pair = mine + lax.ppermute(theirs, axis, [(i, i ^ 1) for i in range(devices)]).astype(jnp.float32)
    total = jnp.take(pair, chip, axis=0)
    for shift in range(1, chips):
        pairs = [(i, ((i // 2 + shift) % chips) * 2 + i % 2) for i in range(devices)]
        sent = jnp.take(pair, (chip + shift) % chips, axis=0).astype(jnp.bfloat16)
        total = total + lax.ppermute(sent, axis, pairs).astype(jnp.float32)
    return total


def reduce_half(partial, extra=None):
    devices = lax.axis_size("lev")
    me = lax.axis_index("lev")
    chips, core = devices // 2, me % 2
    chip = me // 2
    blocks = partial.reshape(chips, 2, -1, *partial.shape[1:])
    mine = jnp.take(blocks, core, axis=1).astype(jnp.float32)
    theirs = jnp.take(blocks, 1 - core, axis=1)
    pair = mine + lax.ppermute(theirs, "lev", [(i, i ^ 1) for i in range(devices)]).astype(jnp.float32)
    pair = pair.astype(jnp.bfloat16).reshape(-1, *partial.shape[1:])
    total = pair.astype(jnp.float32)
    rows = pair.shape[0]
    sent = pair
    if extra is not None:
        width = partial.shape[1]
        flat = extra.reshape(-1)
        spare = (-flat.shape[0]) % width
        sent = jnp.concatenate([pair, jnp.pad(flat, (0, spare)).reshape(-1, width)], axis=0)
    extras = [extra]
    for shift in range(1, chips):
        pairs = [(i, ((i // 2 - shift) % chips) * 2 + i % 2) for i in range(devices)]
        got = lax.ppermute(sent, "lev", pairs)
        total = total + got[:rows].astype(jnp.float32)
        if extra is not None:
            extras.append(got[rows:].reshape(-1)[: extra.size].reshape(extra.shape))
    if extra is None:
        return total
    return total, jnp.roll(jnp.stack(extras), chip, axis=0)


def gather_half(values):
    devices = lax.axis_size("lev")
    theirs = lax.ppermute(values, "lev", [(i, i ^ 1) for i in range(devices)])
    return jnp.concatenate([values, theirs], axis=0)


def mine_first(values, axis):
    devices = lax.axis_size("lev")
    grouped = values.reshape(*values.shape[:axis], devices // 2, 2, -1, *values.shape[axis + 1 :])
    swapped = jnp.flip(grouped, axis=axis + 1)
    chosen = jnp.where(lax.axis_index("lev") % 2 == 0, grouped, swapped)
    return jnp.moveaxis(chosen, axis + 1, axis).reshape(values.shape)


def spread_sum(weight, activation):
    partial = lax.dot_general(
        weight, activation, (((0,), (0,)), ((), ())), preferred_element_type=jnp.float32
    ).astype(jnp.bfloat16)
    return scatter_sum(partial, "lev")


def gather_strips(values, axis):
    devices = lax.axis_size(axis)
    pieces = [values]
    for shift in range(1, devices):
        pairs = [(i, (i + shift) % devices) for i in range(devices)]
        pieces.append(lax.ppermute(values, axis, pairs))
    return jnp.concatenate(pieces, axis=-1)


def make_fold(queries, pieces):
    key_part, value_part = pieces
    scores = (
        jnp.einsum("hdri,phdrj->hripj", queries, key_part, preferred_element_type=jnp.float32)
        * attention_scale
    )
    weights = jnp.exp(scores)
    numerator = jnp.einsum(
        "hripj,phdrj->hdri",
        weights.astype(jnp.bfloat16),
        value_part,
        preferred_element_type=jnp.float32,
    )
    return (numerator, jnp.sum(weights, axis=(3, 4)))


def smooth(state, tap_weights):
    lat_rows = state.shape[1]
    out_cols = state.shape[2] - 2
    secants = secant_rows(lat_rows)[None, :, None]
    padded = jnp.pad(state.astype(jnp.float32), ((0, 0), (1, 1), (0, 0)))
    stencil_sum = jnp.zeros((state.shape[0], lat_rows, out_cols), jnp.float32)
    for row_step in (-1, 0, 1):
        for col_step in (-1, 0, 1):
            shifted = padded[
                :, 1 + row_step : 1 + row_step + lat_rows, 1 + col_step : 1 + col_step + out_cols
            ]
            tap_row = tap_weights[3 * (row_step + 1) + col_step + 1][:, None, None]
            if col_step != 0:
                stencil_sum = stencil_sum + tap_row * secants * shifted
            else:
                stencil_sum = stencil_sum + tap_row * shifted
    return stencil_sum.astype(jnp.bfloat16)


def mlp_partial(full_channels, gain, up, down):
    block_normed = norm_channels(full_channels.astype(jnp.float32), gain).astype(jnp.bfloat16)
    block_normed = block_normed.reshape(full_channels.shape[0], -1)
    hidden = jax.nn.gelu(jnp.dot(up, block_normed, preferred_element_type=jnp.float32)).astype(
        jnp.bfloat16
    )
    return lax.dot_general(
        down, hidden, (((0,), (0,)), ((), ())), preferred_element_type=jnp.float32
    ).astype(jnp.bfloat16)


def run_blocks(state, stencil_weight, block_gain, up_weight, down_weight):
    devices = lax.axis_size("lev")
    chips, chip = devices // 2, lax.axis_index("lev") // 2
    full = gather_channels(smooth(state, stencil_weight[0]))
    partial = mlp_partial(full, block_gain[0], up_weight[0], down_weight[0])
    center = state[:, :, 1:-1]
    taps = stencil_weight[1]
    high = taps.astype(jnp.bfloat16)
    middle = (taps - high.astype(jnp.float32)).astype(jnp.bfloat16)
    low = (taps - high.astype(jnp.float32) - middle.astype(jnp.float32)).astype(jnp.bfloat16)
    extra = jnp.concatenate([center.reshape(-1), high.reshape(-1), middle.reshape(-1), low.reshape(-1)])
    update, extras = reduce_half(partial, extra)
    size = center.size
    centers = extras[:, :size].reshape(chips * center.shape[0], *center.shape[1:])
    pieces = extras[:, size:].astype(jnp.float32).reshape(chips, 3, *taps.shape)
    half_taps = jnp.moveaxis(pieces[:, 0] + pieces[:, 1] + pieces[:, 2], 0, -2).reshape(taps.shape[0], -1)
    state = (centers.astype(jnp.float32) + update.reshape(centers.shape)).astype(jnp.bfloat16)
    full = gather_half(smooth(state, half_taps))
    partial = mlp_partial(
        full, mine_first(block_gain[1], 0), mine_first(up_weight[1], 1), down_weight[1]
    )
    center = jnp.take(state[:, :, 1:-1].reshape(chips, -1, *state.shape[1:2], state.shape[2] - 2), chip, axis=0)
    update = scatter_sum(partial, "lev")
    return (center.astype(jnp.float32) + update.reshape(center.shape)).astype(jnp.bfloat16)


def edges(values, width):
    return jnp.concatenate([values[..., :width], values[..., -width:]], axis=-1)


def per_device(
    latent, att_gain, qkv_weight, out_weight, stencil_weight, block_gain, up_weight, down_weight
):
    ch_local, lat_rows, columns = latent.shape
    head_size = C // H
    heads_local = qkv_weight.shape[1] // head_size
    reach = BLOCKS
    gathered = gather_channels(latent)
    normed = norm_channels(gathered.astype(jnp.float32), att_gain).astype(jnp.bfloat16)
    projected = jnp.einsum("koc,crw->korw", qkv_weight, normed, preferred_element_type=jnp.float32)
    projected = projected.reshape(3, heads_local, head_size, lat_rows, columns)
    queries = unit_heads(projected[0]).astype(jnp.bfloat16)
    key_rows = unit_heads(projected[1]).astype(jnp.bfloat16)
    value_rows = projected[2].astype(jnp.bfloat16)

    key_value = jnp.stack([key_rows, value_rows]).reshape(-1, lat_rows, columns)
    rim = jnp.stack([edges(queries.reshape(ch_local, lat_rows, columns), reach), edges(latent, reach)])
    rim_rows = rim.size // (lat_rows * columns)
    payload = jnp.concatenate([key_value, rim.reshape(rim_rows, lat_rows, columns)], axis=0)
    strips = lax.axis_size("lon")
    pieces = [key_value]
    from_left = from_right = None
    for shift in range(1, strips):
        pairs = [(i, (i + shift) % strips) for i in range(strips)]
        sent = payload if shift in (1, strips - 1) else key_value
        got = lax.ppermute(sent, "lon", pairs)
        pieces.append(got[: key_value.shape[0]])
        if shift == 1:
            from_left = got[key_value.shape[0] :].reshape(rim.shape)[..., reach:]
        if shift == strips - 1:
            from_right = got[key_value.shape[0] :].reshape(rim.shape)[..., :reach]
    all_keys = jnp.stack(pieces).reshape(strips, 2, heads_local, head_size, lat_rows, columns)
    wide_queries = jnp.concatenate(
        [from_left[0], queries.reshape(ch_local, lat_rows, columns), from_right[0]], axis=-1
    ).reshape(heads_local, head_size, lat_rows, -1)
    wide_latent = jnp.concatenate([from_left[1], latent, from_right[1]], axis=-1)

    numerator, denominator = make_fold(wide_queries, (all_keys[:, 0], all_keys[:, 1]))
    attended = (numerator / denominator[:, None]).astype(jnp.bfloat16)
    update = spread_sum(out_weight, attended.reshape(ch_local, -1))
    current = (wide_latent.astype(jnp.float32) + update.reshape(wide_latent.shape)).astype(
        jnp.bfloat16
    )
    current = run_blocks(current, stencil_weight, block_gain, up_weight, down_weight)
    return current


def solution(mesh):
    placed = (
        P("lev", "member", "lon"),
        P(),
        P(None, "lev", None),
        P("lev", None),
        P(None, None, "lev"),
        P(),
        P(None, "lev", None),
        P(None, "lev", None),
    )
    return jax.shard_map(
        per_device, mesh=mesh, in_specs=placed, out_specs=P("lev", "member", "lon"), check_vma=False
    )
```

```python
import math

import jax
import jax.numpy as jnp
from jax import lax
from jax.sharding import PartitionSpec as P

C = 512
H = 8
BLOCKS = 2


attention_scale = 24.0
band_start = 30.0
grid_step = 0.25
epsilon = 1e-06


def secant_rows(count):
    rows = jnp.arange(count).astype(jnp.float32)
    return 1.0 / jnp.cos((band_start + grid_step * rows) * (math.pi / 180.0))


def norm_channels(values, gain):
    scale = lax.rsqrt(jnp.mean(values * values, axis=0, keepdims=True) + epsilon)
    return values * scale * gain[:, None, None]


def unit_heads(values):
    return values * lax.rsqrt(jnp.sum(values * values, axis=1, keepdims=True) + epsilon)


def gather_channels(values):
    return lax.all_gather(values, "lev", axis=0, tiled=True)


def scatter_sum(partial, axis):
    devices = lax.axis_size(axis)
    me = lax.axis_index(axis)
    chips, core = devices // 2, me % 2
    chip = me // 2
    blocks = partial.reshape(chips, 2, -1, *partial.shape[1:])
    mine = jnp.take(blocks, core, axis=1).astype(jnp.float32)
    theirs = jnp.take(blocks, 1 - core, axis=1)
    pair = mine + lax.ppermute(theirs, axis, [(i, i ^ 1) for i in range(devices)]).astype(jnp.float32)
    total = jnp.take(pair, chip, axis=0)
    for shift in range(1, chips):
        pairs = [(i, ((i // 2 + shift) % chips) * 2 + i % 2) for i in range(devices)]
        sent = jnp.take(pair, (chip + shift) % chips, axis=0).astype(jnp.bfloat16)
        total = total + lax.ppermute(sent, axis, pairs).astype(jnp.float32)
    return total


def spread_sum(weight, activation):
    partial = lax.dot_general(
        weight, activation, (((0,), (0,)), ((), ())), preferred_element_type=jnp.float32
    ).astype(jnp.bfloat16)
    return scatter_sum(partial, "lev")


def gather_strips(values, axis):
    devices = lax.axis_size(axis)
    pieces = [values]
    for shift in range(1, devices):
        pairs = [(i, (i + shift) % devices) for i in range(devices)]
        pieces.append(lax.ppermute(values, axis, pairs))
    return jnp.concatenate(pieces, axis=-1)


def make_fold(queries, pieces):
    key_part, value_part = pieces
    scores = (
        jnp.einsum("hdri,phdrj->hripj", queries, key_part, preferred_element_type=jnp.float32)
        * attention_scale
    )
    weights = jnp.exp(scores)
    numerator = jnp.einsum(
        "hripj,phdrj->hdri",
        weights.astype(jnp.bfloat16),
        value_part,
        preferred_element_type=jnp.float32,
    )
    return (numerator, jnp.sum(weights, axis=(3, 4)))


def block_apply(state, block_index, stencil_weight, block_gain, up_weight, down_weight):
    lat_rows = state.shape[1]
    out_cols = state.shape[2] - 2
    secants = secant_rows(lat_rows)[None, :, None]
    padded = jnp.pad(state.astype(jnp.float32), ((0, 0), (1, 1), (0, 0)))
    tap_weights = stencil_weight[block_index]
    stencil_sum = jnp.zeros((state.shape[0], lat_rows, out_cols), jnp.float32)
    for row_step in (-1, 0, 1):
        for col_step in (-1, 0, 1):
            shifted = padded[
                :, 1 + row_step : 1 + row_step + lat_rows, 1 + col_step : 1 + col_step + out_cols
            ]
            tap_row = tap_weights[3 * (row_step + 1) + col_step + 1][:, None, None]
            if col_step != 0:
                stencil_sum = stencil_sum + tap_row * secants * shifted
            else:
                stencil_sum = stencil_sum + tap_row * shifted
    smoothed = stencil_sum.astype(jnp.bfloat16)
    full_channels = gather_channels(smoothed)
    block_normed = norm_channels(full_channels.astype(jnp.float32), block_gain[block_index]).astype(
        jnp.bfloat16
    )
    block_normed = block_normed.reshape(full_channels.shape[0], -1)
    hidden = jax.nn.gelu(
        jnp.dot(up_weight[block_index], block_normed, preferred_element_type=jnp.float32)
    ).astype(jnp.bfloat16)
    update = spread_sum(down_weight[block_index], hidden)
    center = state[:, :, 1:-1]
    return (center.astype(jnp.float32) + update.reshape(center.shape)).astype(jnp.bfloat16)


def edges(values, width):
    return jnp.concatenate([values[..., :width], values[..., -width:]], axis=-1)


def per_device(
    latent, att_gain, qkv_weight, out_weight, stencil_weight, block_gain, up_weight, down_weight
):
    ch_local, lat_rows, columns = latent.shape
    head_size = C // H
    heads_local = qkv_weight.shape[1] // head_size
    reach = BLOCKS
    gathered = gather_channels(latent)
    normed = norm_channels(gathered.astype(jnp.float32), att_gain).astype(jnp.bfloat16)
    projected = jnp.einsum("koc,crw->korw", qkv_weight, normed, preferred_element_type=jnp.float32)
    projected = projected.reshape(3, heads_local, head_size, lat_rows, columns)
    queries = unit_heads(projected[0]).astype(jnp.bfloat16)
    key_rows = unit_heads(projected[1]).astype(jnp.bfloat16)
    value_rows = projected[2].astype(jnp.bfloat16)

    key_value = jnp.stack([key_rows, value_rows]).reshape(-1, lat_rows, columns)
    rim = jnp.stack([edges(queries.reshape(ch_local, lat_rows, columns), reach), edges(latent, reach)])
    rim_rows = rim.size // (lat_rows * columns)
    payload = jnp.concatenate([key_value, rim.reshape(rim_rows, lat_rows, columns)], axis=0)
    strips = lax.axis_size("lon")
    pieces = [key_value]
    from_left = from_right = None
    for shift in range(1, strips):
        pairs = [(i, (i + shift) % strips) for i in range(strips)]
        got = lax.ppermute(payload, "lon", pairs)
        pieces.append(got[: key_value.shape[0]])
        if shift == 1:
            from_left = got[key_value.shape[0] :].reshape(rim.shape)[..., reach:]
        if shift == strips - 1:
            from_right = got[key_value.shape[0] :].reshape(rim.shape)[..., :reach]
    all_keys = jnp.stack(pieces).reshape(strips, 2, heads_local, head_size, lat_rows, columns)
    wide_queries = jnp.concatenate(
        [from_left[0], queries.reshape(ch_local, lat_rows, columns), from_right[0]], axis=-1
    ).reshape(heads_local, head_size, lat_rows, -1)
    wide_latent = jnp.concatenate([from_left[1], latent, from_right[1]], axis=-1)

    numerator, denominator = make_fold(wide_queries, (all_keys[:, 0], all_keys[:, 1]))
    attended = (numerator / denominator[:, None]).astype(jnp.bfloat16)
    update = spread_sum(out_weight, attended.reshape(ch_local, -1))
    current = (wide_latent.astype(jnp.float32) + update.reshape(wide_latent.shape)).astype(
        jnp.bfloat16
    )
    for block_index in range(BLOCKS):
        current = block_apply(
            current, block_index, stencil_weight, block_gain, up_weight, down_weight
        )
    return current


def solution(mesh):
    placed = (
        P("lev", "member", "lon"),
        P(),
        P(None, "lev", None),
        P("lev", None),
        P(None, None, "lev"),
        P(),
        P(None, "lev", None),
        P(None, "lev", None),
    )
    return jax.shard_map(
        per_device, mesh=mesh, in_specs=placed, out_specs=P("lev", "member", "lon"), check_vma=False
    )
```

```python
import math

import jax
import jax.numpy as jnp
from jax import lax
from jax.sharding import PartitionSpec as P

C = 512
H = 8
BLOCKS = 2


attention_scale = 24.0
band_start = 30.0
grid_step = 0.25
epsilon = 1e-06


def secant_rows(count):
    rows = jnp.arange(count).astype(jnp.float32)
    return 1.0 / jnp.cos((band_start + grid_step * rows) * (math.pi / 180.0))


def norm_channels(values, gain):
    scale = lax.rsqrt(jnp.mean(values * values, axis=0, keepdims=True) + epsilon)
    return values * scale * gain[:, None, None]


def unit_heads(values):
    return values * lax.rsqrt(jnp.sum(values * values, axis=1, keepdims=True) + epsilon)


def gather_channels(values):
    return lax.all_gather(values, "lev", axis=0, tiled=True)


def scatter_sum(partial, axis):
    devices = lax.axis_size(axis)
    me = lax.axis_index(axis)
    chips, core = devices // 2, me % 2
    chip = me // 2
    blocks = partial.reshape(chips, 2, -1, *partial.shape[1:])
    mine = jnp.take(blocks, core, axis=1).astype(jnp.float32)
    theirs = jnp.take(blocks, 1 - core, axis=1)
    pair = mine + lax.ppermute(theirs, axis, [(i, i ^ 1) for i in range(devices)]).astype(jnp.float32)
    total = jnp.take(pair, chip, axis=0)
    for shift in range(1, chips):
        pairs = [(i, ((i // 2 + shift) % chips) * 2 + i % 2) for i in range(devices)]
        sent = jnp.take(pair, (chip + shift) % chips, axis=0).astype(jnp.bfloat16)
        total = total + lax.ppermute(sent, axis, pairs).astype(jnp.float32)
    return total


def spread_sum(weight, activation):
    partial = lax.dot_general(
        weight, activation, (((0,), (0,)), ((), ())), preferred_element_type=jnp.float32
    ).astype(jnp.bfloat16)
    return scatter_sum(partial, "lev")


def gather_strips(values, axis):
    devices = lax.axis_size(axis)
    pieces = [values]
    for shift in range(1, devices):
        pairs = [(i, (i + shift) % devices) for i in range(devices)]
        pieces.append(lax.ppermute(values, axis, pairs))
    return jnp.concatenate(pieces, axis=-1)


def make_fold(queries, pieces):
    key_part, value_part = pieces
    scores = (
        jnp.einsum("hdri,phdrj->hripj", queries, key_part, preferred_element_type=jnp.float32)
        * attention_scale
    )
    weights = jnp.exp(scores)
    numerator = jnp.einsum(
        "hripj,phdrj->hdri",
        weights.astype(jnp.bfloat16),
        value_part,
        preferred_element_type=jnp.float32,
    )
    return (numerator, jnp.sum(weights, axis=(3, 4)))


def block_apply(state, block_index, stencil_weight, block_gain, up_weight, down_weight):
    lat_rows = state.shape[1]
    out_cols = state.shape[2] - 2
    secants = secant_rows(lat_rows)[None, :, None]
    padded = jnp.pad(state.astype(jnp.float32), ((0, 0), (1, 1), (0, 0)))
    tap_weights = stencil_weight[block_index]
    stencil_sum = jnp.zeros((state.shape[0], lat_rows, out_cols), jnp.float32)
    for row_step in (-1, 0, 1):
        for col_step in (-1, 0, 1):
            shifted = padded[
                :, 1 + row_step : 1 + row_step + lat_rows, 1 + col_step : 1 + col_step + out_cols
            ]
            tap_row = tap_weights[3 * (row_step + 1) + col_step + 1][:, None, None]
            if col_step != 0:
                stencil_sum = stencil_sum + tap_row * secants * shifted
            else:
                stencil_sum = stencil_sum + tap_row * shifted
    smoothed = stencil_sum.astype(jnp.bfloat16)
    full_channels = gather_channels(smoothed)
    block_normed = norm_channels(full_channels.astype(jnp.float32), block_gain[block_index]).astype(
        jnp.bfloat16
    )
    block_normed = block_normed.reshape(full_channels.shape[0], -1)
    hidden = jax.nn.gelu(
        jnp.dot(up_weight[block_index], block_normed, preferred_element_type=jnp.float32)
    ).astype(jnp.bfloat16)
    update = spread_sum(down_weight[block_index], hidden)
    center = state[:, :, 1:-1]
    return (center.astype(jnp.float32) + update.reshape(center.shape)).astype(jnp.bfloat16)


def edges(values, width):
    return jnp.concatenate([values[..., :width], values[..., -width:]], axis=-1)


def per_device(
    latent, att_gain, qkv_weight, out_weight, stencil_weight, block_gain, up_weight, down_weight
):
    ch_local, lat_rows, columns = latent.shape
    head_size = C // H
    heads_local = qkv_weight.shape[1] // head_size
    reach = BLOCKS
    gathered = gather_channels(latent)
    normed = norm_channels(gathered.astype(jnp.float32), att_gain).astype(jnp.bfloat16)
    projected = jnp.einsum("koc,crw->korw", qkv_weight, normed, preferred_element_type=jnp.float32)
    projected = projected.reshape(3, heads_local, head_size, lat_rows, columns)
    queries = unit_heads(projected[0]).astype(jnp.bfloat16)
    key_rows = unit_heads(projected[1]).astype(jnp.bfloat16)
    value_rows = projected[2].astype(jnp.bfloat16)

    key_value = jnp.stack([key_rows, value_rows]).reshape(-1, lat_rows, columns)
    rim = jnp.stack([edges(queries.reshape(ch_local, lat_rows, columns), reach), edges(latent, reach)])
    rim_rows = rim.size // (lat_rows * columns)
    payload = jnp.concatenate([key_value, rim.reshape(rim_rows, lat_rows, columns)], axis=0)
    strips = lax.axis_size("lon")
    pieces = [key_value]
    from_left = from_right = None
    for shift in range(1, strips):
        pairs = [(i, (i + shift) % strips) for i in range(strips)]
        sent = payload if shift in (1, strips - 1) else key_value
        got = lax.ppermute(sent, "lon", pairs)
        pieces.append(got[: key_value.shape[0]])
        if shift == 1:
            from_left = got[key_value.shape[0] :].reshape(rim.shape)[..., reach:]
        if shift == strips - 1:
            from_right = got[key_value.shape[0] :].reshape(rim.shape)[..., :reach]
    all_keys = jnp.stack(pieces).reshape(strips, 2, heads_local, head_size, lat_rows, columns)
    wide_queries = jnp.concatenate(
        [from_left[0], queries.reshape(ch_local, lat_rows, columns), from_right[0]], axis=-1
    ).reshape(heads_local, head_size, lat_rows, -1)
    wide_latent = jnp.concatenate([from_left[1], latent, from_right[1]], axis=-1)

    numerator, denominator = make_fold(wide_queries, (all_keys[:, 0], all_keys[:, 1]))
    attended = (numerator / denominator[:, None]).astype(jnp.bfloat16)
    partial = jnp.einsum(
        "kc,krw->crw", out_weight, attended.reshape(ch_local, lat_rows, -1),
        preferred_element_type=jnp.float32,
    ).astype(jnp.bfloat16)
    update = scatter_sum(partial, "lev")
    current = (wide_latent.astype(jnp.float32) + update.reshape(wide_latent.shape)).astype(
        jnp.bfloat16
    )
    for block_index in range(BLOCKS):
        current = block_apply(
            current, block_index, stencil_weight, block_gain, up_weight, down_weight
        )
    return current


def solution(mesh):
    placed = (
        P("lev", "member", "lon"),
        P(),
        P(None, "lev", None),
        P("lev", None),
        P(None, None, "lev"),
        P(),
        P(None, "lev", None),
        P(None, "lev", None),
    )
    return jax.shard_map(
        per_device, mesh=mesh, in_specs=placed, out_specs=P("lev", "member", "lon"), check_vma=False
    )
```

```python
import math

import jax
import jax.numpy as jnp
from jax import lax
from jax.sharding import PartitionSpec as P

C = 512
H = 8
BLOCKS = 2


attention_scale = 24.0
band_start = 30.0
grid_step = 0.25
epsilon = 1e-06


def secant_rows(count):
    rows = jnp.arange(count).astype(jnp.float32)
    return 1.0 / jnp.cos((band_start + grid_step * rows) * (math.pi / 180.0))


def norm_channels(values, gain):
    scale = lax.rsqrt(jnp.mean(values * values, axis=0, keepdims=True) + epsilon)
    return values * scale * gain[:, None, None]


def unit_heads(values):
    return values * lax.rsqrt(jnp.sum(values * values, axis=1, keepdims=True) + epsilon)


def gather_channels(values):
    return lax.all_gather(values, "lev", axis=0, tiled=True)


def scatter_sum(partial, axis):
    devices = lax.axis_size(axis)
    me = lax.axis_index(axis)
    chips, core = devices // 2, me % 2
    chip = me // 2
    blocks = partial.reshape(chips, 2, -1, *partial.shape[1:])
    mine = jnp.take(blocks, core, axis=1).astype(jnp.float32)
    theirs = jnp.take(blocks, 1 - core, axis=1)
    pair = mine + lax.ppermute(theirs, axis, [(i, i ^ 1) for i in range(devices)]).astype(jnp.float32)
    total = jnp.take(pair, chip, axis=0)
    for shift in range(1, chips):
        pairs = [(i, ((i // 2 + shift) % chips) * 2 + i % 2) for i in range(devices)]
        sent = jnp.take(pair, (chip + shift) % chips, axis=0).astype(jnp.bfloat16)
        total = total + lax.ppermute(sent, axis, pairs).astype(jnp.float32)
    return total


def spread_sum(weight, activation):
    partial = lax.dot_general(
        weight, activation, (((0,), (0,)), ((), ())), preferred_element_type=jnp.float32
    ).astype(jnp.bfloat16)
    return scatter_sum(partial, "lev")


def gather_strips(values, axis):
    devices = lax.axis_size(axis)
    pieces = [values]
    for shift in range(1, devices):
        pairs = [(i, (i + shift) % devices) for i in range(devices)]
        pieces.append(lax.ppermute(values, axis, pairs))
    return jnp.concatenate(pieces, axis=-1)


def make_fold(queries, pieces):
    key_part, value_part = pieces
    scores = (
        jnp.einsum("hdri,phdrj->hripj", queries, key_part, preferred_element_type=jnp.float32)
        * attention_scale
    )
    weights = jnp.exp(scores)
    numerator = jnp.einsum(
        "hripj,phdrj->hdri",
        weights.astype(jnp.bfloat16),
        value_part,
        preferred_element_type=jnp.float32,
    )
    return (numerator, jnp.sum(weights, axis=(3, 4)))


def block_apply(state, block_index, stencil_weight, block_gain, up_weight, down_weight):
    lat_rows = state.shape[1]
    out_cols = state.shape[2] - 2
    secants = secant_rows(lat_rows)[None, :, None]
    padded = jnp.pad(state.astype(jnp.float32), ((0, 0), (1, 1), (0, 0)))
    tap_weights = stencil_weight[block_index]
    stencil_sum = jnp.zeros((state.shape[0], lat_rows, out_cols), jnp.float32)
    for row_step in (-1, 0, 1):
        for col_step in (-1, 0, 1):
            shifted = padded[
                :, 1 + row_step : 1 + row_step + lat_rows, 1 + col_step : 1 + col_step + out_cols
            ]
            tap_row = tap_weights[3 * (row_step + 1) + col_step + 1][:, None, None]
            if col_step != 0:
                stencil_sum = stencil_sum + tap_row * secants * shifted
            else:
                stencil_sum = stencil_sum + tap_row * shifted
    smoothed = stencil_sum.astype(jnp.bfloat16)
    full_channels = gather_channels(smoothed)
    block_normed = norm_channels(full_channels.astype(jnp.float32), block_gain[block_index]).astype(
        jnp.bfloat16
    )
    block_normed = block_normed.reshape(full_channels.shape[0], -1)
    hidden = jax.nn.gelu(
        jnp.dot(up_weight[block_index], block_normed, preferred_element_type=jnp.float32)
    ).astype(jnp.bfloat16)
    if block_index == BLOCKS - 1:
        partial = jnp.einsum(
            "hc,hrw->crw", down_weight[block_index], hidden.reshape(hidden.shape[0], lat_rows, out_cols),
            preferred_element_type=jnp.float32,
        ).astype(jnp.bfloat16)
        update = scatter_sum(partial, "lev")
    else:
        update = spread_sum(down_weight[block_index], hidden)
    center = state[:, :, 1:-1]
    return (center.astype(jnp.float32) + update.reshape(center.shape)).astype(jnp.bfloat16)


def edges(values, width):
    return jnp.concatenate([values[..., :width], values[..., -width:]], axis=-1)


def per_device(
    latent, att_gain, qkv_weight, out_weight, stencil_weight, block_gain, up_weight, down_weight
):
    ch_local, lat_rows, columns = latent.shape
    head_size = C // H
    heads_local = qkv_weight.shape[1] // head_size
    reach = BLOCKS
    gathered = gather_channels(latent)
    normed = norm_channels(gathered.astype(jnp.float32), att_gain).astype(jnp.bfloat16)
    projected = jnp.einsum("koc,crw->korw", qkv_weight, normed, preferred_element_type=jnp.float32)
    projected = projected.reshape(3, heads_local, head_size, lat_rows, columns)
    queries = unit_heads(projected[0]).astype(jnp.bfloat16)
    key_rows = unit_heads(projected[1]).astype(jnp.bfloat16)
    value_rows = projected[2].astype(jnp.bfloat16)

    key_value = jnp.stack([key_rows, value_rows]).reshape(-1, lat_rows, columns)
    rim = jnp.stack([edges(queries.reshape(ch_local, lat_rows, columns), reach), edges(latent, reach)])
    rim_rows = rim.size // (lat_rows * columns)
    payload = jnp.concatenate([key_value, rim.reshape(rim_rows, lat_rows, columns)], axis=0)
    strips = lax.axis_size("lon")
    pieces = [key_value]
    from_left = from_right = None
    for shift in range(1, strips):
        pairs = [(i, (i + shift) % strips) for i in range(strips)]
        sent = payload if shift in (1, strips - 1) else key_value
        got = lax.ppermute(sent, "lon", pairs)
        pieces.append(got[: key_value.shape[0]])
        if shift == 1:
            from_left = got[key_value.shape[0] :].reshape(rim.shape)[..., reach:]
        if shift == strips - 1:
            from_right = got[key_value.shape[0] :].reshape(rim.shape)[..., :reach]
    all_keys = jnp.stack(pieces).reshape(strips, 2, heads_local, head_size, lat_rows, columns)
    wide_queries = jnp.concatenate(
        [from_left[0], queries.reshape(ch_local, lat_rows, columns), from_right[0]], axis=-1
    ).reshape(heads_local, head_size, lat_rows, -1)
    wide_latent = jnp.concatenate([from_left[1], latent, from_right[1]], axis=-1)

    numerator, denominator = make_fold(wide_queries, (all_keys[:, 0], all_keys[:, 1]))
    attended = (numerator / denominator[:, None]).astype(jnp.bfloat16)
    update = spread_sum(out_weight, attended.reshape(ch_local, -1))
    current = (wide_latent.astype(jnp.float32) + update.reshape(wide_latent.shape)).astype(
        jnp.bfloat16
    )
    for block_index in range(BLOCKS):
        current = block_apply(
            current, block_index, stencil_weight, block_gain, up_weight, down_weight
        )
    return current


def solution(mesh):
    placed = (
        P("lev", "member", "lon"),
        P(),
        P(None, "lev", None),
        P("lev", None),
        P(None, None, "lev"),
        P(),
        P(None, "lev", None),
        P(None, "lev", None),
    )
    return jax.shard_map(
        per_device, mesh=mesh, in_specs=placed, out_specs=P("lev", "member", "lon"), check_vma=False
    )
```

```python
import math

import jax
import jax.numpy as jnp
from jax import lax
from jax.sharding import PartitionSpec as P

C = 512
H = 8
BLOCKS = 2


attention_scale = 24.0
band_start = 30.0
grid_step = 0.25
epsilon = 1e-06


def secant_rows(count):
    rows = jnp.arange(count).astype(jnp.float32)
    return 1.0 / jnp.cos((band_start + grid_step * rows) * (math.pi / 180.0))


def norm_channels(values, gain):
    scale = lax.rsqrt(jnp.mean(values * values, axis=0, keepdims=True) + epsilon)
    return values * scale * gain[:, None, None]


def unit_heads(values):
    return values * lax.rsqrt(jnp.sum(values * values, axis=1, keepdims=True) + epsilon)


def gather_channels(values):
    return lax.all_gather(values, "lev", axis=0, tiled=True)


def scatter_sum(partial, axis):
    devices = lax.axis_size(axis)
    me = lax.axis_index(axis)
    chips, core = devices // 2, me % 2
    chip = me // 2
    blocks = partial.reshape(chips, 2, -1, *partial.shape[1:])
    mine = jnp.take(blocks, core, axis=1).astype(jnp.float32)
    theirs = jnp.take(blocks, 1 - core, axis=1)
    pair = mine + lax.ppermute(theirs, axis, [(i, i ^ 1) for i in range(devices)]).astype(jnp.float32)
    total = jnp.take(pair, chip, axis=0)
    for shift in range(1, chips):
        pairs = [(i, ((i // 2 + shift) % chips) * 2 + i % 2) for i in range(devices)]
        sent = jnp.take(pair, (chip + shift) % chips, axis=0).astype(jnp.bfloat16)
        total = total + lax.ppermute(sent, axis, pairs).astype(jnp.float32)
    return total


def spread_sum(weight, activation):
    partial = lax.dot_general(
        weight, activation, (((0,), (0,)), ((), ())), preferred_element_type=jnp.float32
    ).astype(jnp.bfloat16)
    return scatter_sum(partial, "lev")


def gather_strips(values, axis):
    devices = lax.axis_size(axis)
    pieces = [values]
    for shift in range(1, devices):
        pairs = [(i, (i + shift) % devices) for i in range(devices)]
        pieces.append(lax.ppermute(values, axis, pairs))
    return jnp.concatenate(pieces, axis=-1)


def make_fold(queries, pieces):
    key_part, value_part = pieces
    scores = (
        jnp.einsum("hdri,phdrj->hripj", queries, key_part, preferred_element_type=jnp.float32)
        * attention_scale
    )
    weights = jnp.exp(scores)
    numerator = jnp.einsum(
        "hripj,phdrj->hdri",
        weights.astype(jnp.bfloat16),
        value_part,
        preferred_element_type=jnp.float32,
    )
    return (numerator, jnp.sum(weights, axis=(3, 4)))


def block_apply(state, block_index, stencil_weight, block_gain, up_weight, down_weight):
    lat_rows = state.shape[1]
    out_cols = state.shape[2] - 2
    secants = secant_rows(lat_rows)[None, :, None]
    padded = jnp.pad(state.astype(jnp.float32), ((0, 0), (1, 1), (0, 0)))
    tap_weights = stencil_weight[block_index]
    stencil_sum = jnp.zeros((state.shape[0], lat_rows, out_cols), jnp.float32)
    for row_step in (-1, 0, 1):
        for col_step in (-1, 0, 1):
            shifted = padded[
                :, 1 + row_step : 1 + row_step + lat_rows, 1 + col_step : 1 + col_step + out_cols
            ]
            tap_row = tap_weights[3 * (row_step + 1) + col_step + 1][:, None, None]
            if col_step != 0:
                stencil_sum = stencil_sum + tap_row * secants * shifted
            else:
                stencil_sum = stencil_sum + tap_row * shifted
    smoothed = stencil_sum.astype(jnp.bfloat16)
    full_channels = gather_channels(smoothed)
    block_normed = norm_channels(full_channels.astype(jnp.float32), block_gain[block_index]).astype(
        jnp.bfloat16
    )
    block_normed = block_normed.reshape(full_channels.shape[0], -1)
    hidden = jax.nn.gelu(
        jnp.dot(up_weight[block_index], block_normed, preferred_element_type=jnp.float32)
    ).astype(jnp.bfloat16)
    if block_index == BLOCKS - 1:
        partial = jnp.einsum(
            "hc,hrw->crw", down_weight[block_index], hidden.reshape(hidden.shape[0], lat_rows, out_cols),
            preferred_element_type=jnp.float32,
        ).astype(jnp.bfloat16)
        update = scatter_sum(partial, "lev")
    else:
        update = spread_sum(down_weight[block_index], hidden)
    center = state[:, :, 1:-1]
    return (center.astype(jnp.float32) + update.reshape(center.shape)).astype(jnp.bfloat16)


def edges(values, width):
    return jnp.concatenate([values[..., :width], values[..., -width:]], axis=-1)


def per_device(
    latent, att_gain, qkv_weight, out_weight, stencil_weight, block_gain, up_weight, down_weight
):
    ch_local, lat_rows, columns = latent.shape
    head_size = C // H
    heads_local = qkv_weight.shape[1] // head_size
    reach = BLOCKS
    gathered = gather_channels(latent)
    normed = norm_channels(gathered.astype(jnp.float32), att_gain).astype(jnp.bfloat16)
    projected = jnp.einsum("koc,crw->korw", qkv_weight, normed, preferred_element_type=jnp.float32)
    projected = projected.reshape(3, heads_local, head_size, lat_rows, columns)
    queries = unit_heads(projected[0]).astype(jnp.bfloat16)
    key_rows = unit_heads(projected[1]).astype(jnp.bfloat16)
    value_rows = projected[2].astype(jnp.bfloat16)

    key_value = jnp.stack([key_rows, value_rows]).reshape(-1, lat_rows, columns)
    rim = jnp.stack([edges(queries.reshape(ch_local, lat_rows, columns), reach), edges(latent, reach)])
    rim_rows = rim.size // (lat_rows * columns)
    payload = jnp.concatenate([key_value, rim.reshape(rim_rows, lat_rows, columns)], axis=0)
    strips = lax.axis_size("lon")
    pieces = [key_value]
    from_left = from_right = None
    for shift in range(1, strips):
        pairs = [(i, (i + shift) % strips) for i in range(strips)]
        sent = payload if shift in (1, strips - 1) else key_value
        got = lax.ppermute(sent, "lon", pairs)
        pieces.append(got[: key_value.shape[0]])
        if shift == 1:
            from_left = got[key_value.shape[0] :].reshape(rim.shape)[..., reach:]
        if shift == strips - 1:
            from_right = got[key_value.shape[0] :].reshape(rim.shape)[..., :reach]
    all_keys = jnp.stack(pieces).reshape(strips, 2, heads_local, head_size, lat_rows, columns)
    wide_queries = jnp.concatenate(
        [from_left[0], queries.reshape(ch_local, lat_rows, columns), from_right[0]], axis=-1
    ).reshape(heads_local, head_size, lat_rows, -1)
    wide_latent = jnp.concatenate([from_left[1], latent, from_right[1]], axis=-1)

    numerator, denominator = make_fold(wide_queries, (all_keys[:, 0], all_keys[:, 1]))
    attended = (numerator / denominator[:, None]).astype(jnp.bfloat16)
    partial = jnp.einsum(
        "kc,krw->crw", out_weight, attended.reshape(ch_local, lat_rows, -1),
        preferred_element_type=jnp.float32,
    ).astype(jnp.bfloat16)
    update = scatter_sum(partial, "lev")
    current = (wide_latent.astype(jnp.float32) + update.reshape(wide_latent.shape)).astype(
        jnp.bfloat16
    )
    for block_index in range(BLOCKS):
        current = block_apply(
            current, block_index, stencil_weight, block_gain, up_weight, down_weight
        )
    return current


def solution(mesh):
    placed = (
        P("lev", "member", "lon"),
        P(),
        P(None, "lev", None),
        P("lev", None),
        P(None, None, "lev"),
        P(),
        P(None, "lev", None),
        P(None, "lev", None),
    )
    return jax.shard_map(
        per_device, mesh=mesh, in_specs=placed, out_specs=P("lev", "member", "lon"), check_vma=False
    )
```

```python
import math

import jax
import jax.numpy as jnp
from jax import lax
from jax.sharding import PartitionSpec as P

C = 512
H = 8
BLOCKS = 2


attention_scale = 24.0
band_start = 30.0
grid_step = 0.25
epsilon = 1e-06


def secant_rows(count):
    rows = jnp.arange(count).astype(jnp.float32)
    return 1.0 / jnp.cos((band_start + grid_step * rows) * (math.pi / 180.0))


def norm_channels(values, gain):
    scale = lax.rsqrt(jnp.mean(values * values, axis=0, keepdims=True) + epsilon)
    return values * scale * gain[:, None, None]


def unit_heads(values):
    return values * lax.rsqrt(jnp.sum(values * values, axis=1, keepdims=True) + epsilon)


def gather_channels(values):
    return lax.all_gather(values, "lev", axis=0, tiled=True)


def scatter_sum(partial, axis):
    devices = lax.axis_size(axis)
    me = lax.axis_index(axis)
    chips, core = devices // 2, me % 2
    chip = me // 2
    blocks = partial.reshape(chips, 2, -1, *partial.shape[1:])
    mine = jnp.take(blocks, core, axis=1).astype(jnp.float32)
    theirs = jnp.take(blocks, 1 - core, axis=1)
    pair = mine + lax.ppermute(theirs, axis, [(i, i ^ 1) for i in range(devices)]).astype(jnp.float32)
    total = jnp.take(pair, chip, axis=0)
    for shift in range(1, chips):
        pairs = [(i, ((i // 2 + shift) % chips) * 2 + i % 2) for i in range(devices)]
        sent = jnp.take(pair, (chip + shift) % chips, axis=0).astype(jnp.bfloat16)
        total = total + lax.ppermute(sent, axis, pairs).astype(jnp.float32)
    return total


def spread_sum(weight, activation):
    partial = lax.dot_general(
        weight, activation, (((0,), (0,)), ((), ())), preferred_element_type=jnp.float32
    ).astype(jnp.bfloat16)
    return scatter_sum(partial, "lev")


def gather_strips(values, axis):
    devices = lax.axis_size(axis)
    pieces = [values]
    for shift in range(1, devices):
        pairs = [(i, (i + shift) % devices) for i in range(devices)]
        pieces.append(lax.ppermute(values, axis, pairs))
    return jnp.concatenate(pieces, axis=-1)


def make_fold(queries, pieces):
    key_part, value_part = pieces
    scores = (
        jnp.einsum("hdri,phdrj->hripj", queries, key_part, preferred_element_type=jnp.float32)
        * attention_scale
    )
    weights = jnp.exp(scores)
    numerator = jnp.einsum(
        "hripj,phdrj->hdri",
        weights.astype(jnp.bfloat16),
        value_part,
        preferred_element_type=jnp.float32,
    )
    return (numerator, jnp.sum(weights, axis=(3, 4)))


def block_apply(state, block_index, stencil_weight, block_gain, up_weight, down_weight):
    lat_rows = state.shape[1]
    out_cols = state.shape[2] - 2
    secants = secant_rows(lat_rows)[None, :, None]
    padded = jnp.pad(state.astype(jnp.float32), ((0, 0), (1, 1), (0, 0)))
    tap_weights = stencil_weight[block_index]
    stencil_sum = jnp.zeros((state.shape[0], lat_rows, out_cols), jnp.float32)
    for row_step in (-1, 0, 1):
        for col_step in (-1, 0, 1):
            shifted = padded[
                :, 1 + row_step : 1 + row_step + lat_rows, 1 + col_step : 1 + col_step + out_cols
            ]
            tap_row = tap_weights[3 * (row_step + 1) + col_step + 1][:, None, None]
            if col_step != 0:
                stencil_sum = stencil_sum + tap_row * secants * shifted
            else:
                stencil_sum = stencil_sum + tap_row * shifted
    smoothed = stencil_sum.astype(jnp.bfloat16)
    full_channels = gather_channels(smoothed)
    block_normed = norm_channels(full_channels.astype(jnp.float32), block_gain[block_index]).astype(
        jnp.bfloat16
    )
    block_normed = block_normed.reshape(full_channels.shape[0], -1)
    hidden = jax.nn.gelu(
        jnp.dot(up_weight[block_index], block_normed, preferred_element_type=jnp.float32)
    ).astype(jnp.bfloat16)
    update = spread_sum(down_weight[block_index], hidden)
    center = state[:, :, 1:-1]
    return (center.astype(jnp.float32) + update.reshape(center.shape)).astype(jnp.bfloat16)


def edges(values, width):
    return jnp.concatenate([values[..., :width], values[..., -width:]], axis=-1)


def per_device(
    latent, att_gain, qkv_weight, out_weight, stencil_weight, block_gain, up_weight, down_weight
):
    ch_local, lat_rows, columns = latent.shape
    head_size = C // H
    heads_local = qkv_weight.shape[1] // head_size
    reach = BLOCKS
    gathered = gather_channels(latent.reshape(ch_local, -1)).reshape(-1, lat_rows, columns)
    normed = norm_channels(gathered.astype(jnp.float32), att_gain).astype(jnp.bfloat16)
    projected = jnp.einsum("koc,crw->korw", qkv_weight, normed, preferred_element_type=jnp.float32)
    projected = projected.reshape(3, heads_local, head_size, lat_rows, columns)
    queries = unit_heads(projected[0]).astype(jnp.bfloat16)
    key_rows = unit_heads(projected[1]).astype(jnp.bfloat16)
    value_rows = projected[2].astype(jnp.bfloat16)

    key_value = jnp.stack([key_rows, value_rows]).reshape(-1, lat_rows, columns)
    rim = jnp.stack([edges(queries.reshape(ch_local, lat_rows, columns), reach), edges(latent, reach)])
    rim_rows = rim.size // (lat_rows * columns)
    payload = jnp.concatenate([key_value, rim.reshape(rim_rows, lat_rows, columns)], axis=0)
    strips = lax.axis_size("lon")
    pieces = [key_value]
    from_left = from_right = None
    for shift in range(1, strips):
        pairs = [(i, (i + shift) % strips) for i in range(strips)]
        sent = payload if shift in (1, strips - 1) else key_value
        got = lax.ppermute(sent, "lon", pairs)
        pieces.append(got[: key_value.shape[0]])
        if shift == 1:
            from_left = got[key_value.shape[0] :].reshape(rim.shape)[..., reach:]
        if shift == strips - 1:
            from_right = got[key_value.shape[0] :].reshape(rim.shape)[..., :reach]
    all_keys = jnp.stack(pieces).reshape(strips, 2, heads_local, head_size, lat_rows, columns)
    wide_queries = jnp.concatenate(
        [from_left[0], queries.reshape(ch_local, lat_rows, columns), from_right[0]], axis=-1
    ).reshape(heads_local, head_size, lat_rows, -1)
    wide_latent = jnp.concatenate([from_left[1], latent, from_right[1]], axis=-1)

    numerator, denominator = make_fold(wide_queries, (all_keys[:, 0], all_keys[:, 1]))
    attended = (numerator / denominator[:, None]).astype(jnp.bfloat16)
    update = spread_sum(out_weight, attended.reshape(ch_local, -1))
    current = (wide_latent.astype(jnp.float32) + update.reshape(wide_latent.shape)).astype(
        jnp.bfloat16
    )
    for block_index in range(BLOCKS):
        current = block_apply(
            current, block_index, stencil_weight, block_gain, up_weight, down_weight
        )
    return current


def solution(mesh):
    placed = (
        P("lev", "member", "lon"),
        P(),
        P(None, "lev", None),
        P("lev", None),
        P(None, None, "lev"),
        P(),
        P(None, "lev", None),
        P(None, "lev", None),
    )
    return jax.shard_map(
        per_device, mesh=mesh, in_specs=placed, out_specs=P("lev", "member", "lon"), check_vma=False
    )
```

```python
import math

import jax
import jax.numpy as jnp
from jax import lax
from jax.sharding import PartitionSpec as P

C = 512
H = 8
BLOCKS = 2


attention_scale = 24.0
band_start = 30.0
grid_step = 0.25
epsilon = 1e-06


def secant_rows(count):
    rows = jnp.arange(count).astype(jnp.float32)
    return 1.0 / jnp.cos((band_start + grid_step * rows) * (math.pi / 180.0))


def norm_channels(values, gain):
    scale = lax.rsqrt(jnp.mean(values * values, axis=0, keepdims=True) + epsilon)
    return values * scale * gain[:, None, None]


def unit_heads(values):
    return values * lax.rsqrt(jnp.sum(values * values, axis=1, keepdims=True) + epsilon)


def gather_channels(values):
    return lax.all_gather(values, "lev", axis=0, tiled=True)


def scatter_sum(partial, axis):
    devices = lax.axis_size(axis)
    me = lax.axis_index(axis)
    chips, core = devices // 2, me % 2
    chip = me // 2
    blocks = partial.reshape(chips, 2, -1, *partial.shape[1:])
    mine = jnp.take(blocks, core, axis=1).astype(jnp.float32)
    theirs = jnp.take(blocks, 1 - core, axis=1)
    pair = mine + lax.ppermute(theirs, axis, [(i, i ^ 1) for i in range(devices)]).astype(jnp.float32)
    total = jnp.take(pair, chip, axis=0)
    for shift in range(1, chips):
        pairs = [(i, ((i // 2 + shift) % chips) * 2 + i % 2) for i in range(devices)]
        sent = jnp.take(pair, (chip + shift) % chips, axis=0).astype(jnp.bfloat16)
        total = total + lax.ppermute(sent, axis, pairs).astype(jnp.float32)
    return total


def spread_sum(weight, activation):
    partial = lax.dot_general(
        weight, activation, (((0,), (0,)), ((), ())), preferred_element_type=jnp.float32
    ).astype(jnp.bfloat16)
    return scatter_sum(partial, "lev")


def gather_strips(values, axis):
    devices = lax.axis_size(axis)
    pieces = [values]
    for shift in range(1, devices):
        pairs = [(i, (i + shift) % devices) for i in range(devices)]
        pieces.append(lax.ppermute(values, axis, pairs))
    return jnp.concatenate(pieces, axis=-1)


def make_fold(queries, pieces):
    key_part, value_part = pieces
    scores = (
        jnp.einsum("hdri,phdrj->hripj", queries, key_part, preferred_element_type=jnp.float32)
        * attention_scale
    )
    weights = jnp.exp(scores)
    numerator = jnp.einsum(
        "hripj,phdrj->hdri",
        weights.astype(jnp.bfloat16),
        value_part,
        preferred_element_type=jnp.float32,
    )
    return (numerator, jnp.sum(weights, axis=(3, 4)))


def block_apply(state, block_index, stencil_weight, block_gain, up_weight, down_weight):
    lat_rows = state.shape[1]
    out_cols = state.shape[2] - 2
    secants = secant_rows(lat_rows)[None, :, None]
    padded = jnp.pad(state.astype(jnp.float32), ((0, 0), (1, 1), (0, 0)))
    tap_weights = stencil_weight[block_index]
    stencil_sum = jnp.zeros((state.shape[0], lat_rows, out_cols), jnp.float32)
    for row_step in (-1, 0, 1):
        for col_step in (-1, 0, 1):
            shifted = padded[
                :, 1 + row_step : 1 + row_step + lat_rows, 1 + col_step : 1 + col_step + out_cols
            ]
            tap_row = tap_weights[3 * (row_step + 1) + col_step + 1][:, None, None]
            if col_step != 0:
                stencil_sum = stencil_sum + tap_row * secants * shifted
            else:
                stencil_sum = stencil_sum + tap_row * shifted
    smoothed = stencil_sum.astype(jnp.bfloat16)
    full_channels = gather_channels(smoothed.reshape(smoothed.shape[0], -1)).reshape(-1, *smoothed.shape[1:])
    block_normed = norm_channels(full_channels.astype(jnp.float32), block_gain[block_index]).astype(
        jnp.bfloat16
    )
    block_normed = block_normed.reshape(full_channels.shape[0], -1)
    hidden = jax.nn.gelu(
        jnp.dot(up_weight[block_index], block_normed, preferred_element_type=jnp.float32)
    ).astype(jnp.bfloat16)
    update = spread_sum(down_weight[block_index], hidden)
    center = state[:, :, 1:-1]
    return (center.astype(jnp.float32) + update.reshape(center.shape)).astype(jnp.bfloat16)


def edges(values, width):
    return jnp.concatenate([values[..., :width], values[..., -width:]], axis=-1)


def per_device(
    latent, att_gain, qkv_weight, out_weight, stencil_weight, block_gain, up_weight, down_weight
):
    ch_local, lat_rows, columns = latent.shape
    head_size = C // H
    heads_local = qkv_weight.shape[1] // head_size
    reach = BLOCKS
    gathered = gather_channels(latent.reshape(ch_local, -1)).reshape(-1, lat_rows, columns)
    normed = norm_channels(gathered.astype(jnp.float32), att_gain).astype(jnp.bfloat16)
    projected = jnp.einsum("koc,crw->korw", qkv_weight, normed, preferred_element_type=jnp.float32)
    projected = projected.reshape(3, heads_local, head_size, lat_rows, columns)
    queries = unit_heads(projected[0]).astype(jnp.bfloat16)
    key_rows = unit_heads(projected[1]).astype(jnp.bfloat16)
    value_rows = projected[2].astype(jnp.bfloat16)

    key_value = jnp.stack([key_rows, value_rows]).reshape(-1, lat_rows, columns)
    rim = jnp.stack([edges(queries.reshape(ch_local, lat_rows, columns), reach), edges(latent, reach)])
    rim_rows = rim.size // (lat_rows * columns)
    payload = jnp.concatenate([key_value, rim.reshape(rim_rows, lat_rows, columns)], axis=0)
    strips = lax.axis_size("lon")
    pieces = [key_value]
    from_left = from_right = None
    for shift in range(1, strips):
        pairs = [(i, (i + shift) % strips) for i in range(strips)]
        sent = payload if shift in (1, strips - 1) else key_value
        got = lax.ppermute(sent, "lon", pairs)
        pieces.append(got[: key_value.shape[0]])
        if shift == 1:
            from_left = got[key_value.shape[0] :].reshape(rim.shape)[..., reach:]
        if shift == strips - 1:
            from_right = got[key_value.shape[0] :].reshape(rim.shape)[..., :reach]
    all_keys = jnp.stack(pieces).reshape(strips, 2, heads_local, head_size, lat_rows, columns)
    wide_queries = jnp.concatenate(
        [from_left[0], queries.reshape(ch_local, lat_rows, columns), from_right[0]], axis=-1
    ).reshape(heads_local, head_size, lat_rows, -1)
    wide_latent = jnp.concatenate([from_left[1], latent, from_right[1]], axis=-1)

    numerator, denominator = make_fold(wide_queries, (all_keys[:, 0], all_keys[:, 1]))
    attended = (numerator / denominator[:, None]).astype(jnp.bfloat16)
    update = spread_sum(out_weight, attended.reshape(ch_local, -1))
    current = (wide_latent.astype(jnp.float32) + update.reshape(wide_latent.shape)).astype(
        jnp.bfloat16
    )
    for block_index in range(BLOCKS):
        current = block_apply(
            current, block_index, stencil_weight, block_gain, up_weight, down_weight
        )
    return current


def solution(mesh):
    placed = (
        P("lev", "member", "lon"),
        P(),
        P(None, "lev", None),
        P("lev", None),
        P(None, None, "lev"),
        P(),
        P(None, "lev", None),
        P(None, "lev", None),
    )
    return jax.shard_map(
        per_device, mesh=mesh, in_specs=placed, out_specs=P("lev", "member", "lon"), check_vma=False
    )
```
